32 devices in a mesh: req: 4 (over y, x), exp: 8 (over z, core).
Axes of the slice: x: 2, y: 2, z: 4, core: 2. Of those that a mesh axis runs over, the one named last changes fastest.
Arguments:
- tokens: bfloat16 [4, 512, 2048], P('req', 'exp'), may hold values from -6 to 6
- cache: bfloat16 [4, 1024, 4096], P('req', None, 'exp'), may hold values from -64 to 64
- cache_len: int32 [4], P('req'), may hold values from 1 to 1024, 2560 in all
- attn_routes: int32 [4, 512, 2], P('req', 'exp'), may hold values from 0 to 7, all different within a row; in each aligned block of 64 rows (0 to 63, 64 to 127, ..., all dimensions but the last counted through in order) at most 24 rows name the same one
- mlp_routes: int32 [4, 512, 2], P('req', 'exp'), may hold values from 0 to 7, all different within a row; in each aligned block of 64 rows (0 to 63, 64 to 127, ..., all dimensions but the last counted through in order) at most 24 rows name the same one
- norm_attn: float32 [2048], replicated, may hold values from 0.5 to 1.5
- attn_router: bfloat16 [2048, 8], replicated, may hold values from -0.125 to 0.125
- w_query: bfloat16 [128, 2048, 128], P('exp'), may hold values from -0.125 to 0.125
- w_keyval: bfloat16 [2048, 4096], P(None, 'exp'), may hold values from -0.125 to 0.125
- w_out: bfloat16 [128, 128, 2048], P('exp'), may hold values from -0.125 to 0.125
- norm_mlp: float32 [2048], replicated, may hold values from 0.5 to 1.5
- mlp_router: bfloat16 [2048, 8], replicated, may hold values from -0.125 to 0.125
- w_gate: bfloat16 [8, 2048, 5632], P('exp'), may hold values from -0.125 to 0.125
- w_up: bfloat16 [8, 2048, 5632], P('exp'), may hold values from -0.125 to 0.125
- w_down: bfloat16 [8, 5632, 2048], P('exp'), may hold values from -0.078125 to 0.078125
Outputs:
- hidden_out: bfloat16 [4, 512, 2048], P('req', 'exp')
- cache_out: bfloat16 [4, 1536, 4096], P('req', None, 'exp')
The draws below stay inside these ranges and needn't reach their ends.
Inputs may be any that keep to these rules, and one draw needn't show every extreme that they name: `attn_routes`: in each aligned block of 64 rows, no expert is named by more than 24 rows. `mlp_routes`: in each aligned block of 64 rows, no expert is named by more than 24 rows.
All inputs are finite; a program needn't handle non-finite values. No bound on the sum of `cache_len` on one device may be relied on, other than what follows from the above.
Results may differ from the reference program's by a relative error of at most 0.015.
The reference program's roundings to bfloat16 on the way count: a program that leaves them out, or rounds other values in their place, can miss the bound.
Values may be sent and summed in bfloat16 or wider, within the bound.
No kernel may reach another device: no remote copies, remote signals or barrier semaphores. Data moves between devices by JAX's collectives and lax.ppermute only.
A program may use at most 256 MiB of HBM per device.

```python
import math
import jax
import jax.numpy as jnp
import numpy as np
from jax import lax

D = 2048
KVH = 16
HD = 128
EA = 8
EM = 8
FF = 5632
TOPK = 2
TOK_DEV = 64
CACHE_MAX = 1024
MOST = 24
STRETCH = 512
CAPACITY = 192
SPLIT = 1
FFS = 5632
HPD = 16
N_REQ = 4


def draw_cache(key, part):
    base_vals = jax.random.normal(jax.random.fold_in(key, 11), (N_REQ, CACHE_MAX, 2 * KVH * HD), jnp.float32)
    base_vals = jnp.clip(base_vals, -6.0, 6.0)
    return base_vals.astype(jnp.bfloat16)


def block_scale(stream_key, shape, shards, smallest, top_value):
    loudness = 1.0
    for axis_at, blocks in shards:
        steps = jax.random.uniform(jax.random.fold_in(jax.random.fold_in(stream_key, 6), axis_at), (blocks,), jnp.float32, smallest / len(shards), top_value / len(shards))
        loudness = loudness * jnp.repeat(jnp.exp(steps), shape[axis_at] // blocks).reshape((-1,) + (1,) * (len(shape) - 1 - axis_at))
    return loudness


def length_profile(count, total, bound, slope):
    portions = [(1 << 20) // math.isqrt(standing ** slope) + 1 for standing in range(2, count + 1)]
    rest, counts = total - bound - (count - 1), [1] * (count - 1)
    while rest > 0:
        candidates = [i for i in range(count - 1) if counts[i] < bound]
        whole, budget = sum([portions[i] for i in candidates]), rest
        for i in candidates:
            more = min(bound - counts[i], max(1, budget * portions[i] // whole), rest)
            counts[i] = counts[i] + more
            rest = rest - more
    return np.array([bound] + counts)


def ragged_sizes(key, amount, total, reach, skew):
    if amount == 2:
        one = jax.random.randint(key, (), max(1, total - reach), min(reach, total - 1) + 1)
        return jnp.stack([one, total - one])
    sizes = jnp.asarray(length_profile(amount, total, reach, skew), jnp.int32)
    pairs = (amount - 1) // 2
    source_of, sink = sizes[1:1 + 2 * pairs:2], sizes[2:2 + 2 * pairs:2]
    room = jnp.minimum(source_of - 1, reach - sink)
    shifted = jax.random.randint(jax.random.fold_in(key, 1), (pairs,), 0, 1 << 20) % (room + 1)
    sizes = sizes.at[1:1 + 2 * pairs:2].set(source_of - shifted).at[2:2 + 2 * pairs:2].set(sink + shifted)
    return sizes[jax.random.permutation(jax.random.fold_in(key, 2), amount)]


def deal_out(rng, own, number, rows, count, top, reach, slope):
    ranking = jax.random.permutation(rng, count)
    heavy_load, ordinary = portions_of(count, rows * top, reach, slope, True), portions_of(count, rows * top, reach, slope, False)
    places = jnp.arange(count)

    def named(lengths, offset_by):
        used = int((lengths > 0).sum())
        fixed = max(1, used // 4)
        shifted = fixed + (places - fixed + offset_by * (used - fixed)) % max(1, count - fixed)
        return jnp.zeros((count,), jnp.int32).at[ranking[jnp.where(places < fixed, places, shifted)]].set(jnp.asarray(lengths, jnp.int32))

    lengths = jnp.where(number % 4 == 0, named(heavy_load, number // 4), named(ordinary, number - number // 4 - 1))
    mixed = jax.random.permutation(jax.random.fold_in(own, 3), count)
    source_of, receiver = mixed[0:count // 2 * 2:2], mixed[1:count // 2 * 2:2]
    room = jnp.minimum(lengths[source_of] - 1, reach - lengths[receiver]) // 2
    room = jnp.where((source_of == ranking[0]) | (receiver == ranking[0]) | (lengths[receiver] == 0), 0, jnp.maximum(room, 0))
    shifted = jax.random.randint(jax.random.fold_in(own, 4), (count // 2,), 0, 1 << 20) % (room + 1)
    lengths = lengths.at[source_of].add(-shifted).at[receiver].add(shifted)
    items = jnp.searchsorted(jnp.cumsum(lengths), jnp.arange(rows * top), side="right").astype(jnp.int32)
    grid = items.reshape(top, rows).T
    grid = grid[jax.random.permutation(jax.random.fold_in(own, 1), rows)]
    offset_by = jax.random.randint(jax.random.fold_in(own, 2), (rows, 1), 0, top)
    return jnp.take_along_axis(grid, (jnp.arange(top)[None, :] + offset_by) % top, axis=1)


def portions_of(amount, total, bound, skew, full):
    portions = [(1 << 20) // math.isqrt(rank ** skew) + 1 for rank in range(1, amount + 1)]
    largest = bound if full else min(bound, max(-(-total // amount), total * portions[0] // sum(portions)))
    least = 1 if total - largest >= amount - 1 else 0
    counts, rest = [largest] + [least] * (amount - 1), total - largest - least * (amount - 1)
    while rest > 0:
        free = [i for i in range(1, amount) if counts[i] < largest] or [i for i in range(1, amount) if counts[i] < bound]
        pool, budget = sum([portions[i] for i in free]), rest
        for i in free:
            more = min(bound - counts[i], max(1, budget * portions[i] // pool), rest)
            counts[i] = counts[i] + more
            rest = rest - more
    return np.array(counts)


def centred(stream_key, shape, width, limit, shards=(), held_as=jnp.bfloat16):
    gain = block_scale(stream_key, shape, shards, -0.22, 0.18) if shards else 1.0
    entries = jax.random.normal(stream_key, shape, jnp.float32) * width * gain
    return jnp.minimum(jnp.maximum(entries, -limit), limit).astype(held_as)


def setup_inputs(seed: int = 0) -> dict:
    key_list = jax.random.split(jax.random.key(seed), 16)
    tokens = centred(key_list[0], (N_REQ, STRETCH, D), 1.0, 6.0, ((0, 4), (1, 8)))
    cache = draw_cache(jax.random.fold_in(key_list[15], 71), 0)
    cache_len = ragged_sizes(key_list[2], N_REQ, 5 * CACHE_MAX // 2, CACHE_MAX, 2).astype(jnp.int32)
    attn_routes_keys = jax.random.split(jax.random.fold_in(key_list[3], 1), N_REQ * STRETCH // TOK_DEV)
    attn_routes_turns = jax.random.permutation(jax.random.fold_in(key_list[3], 3), N_REQ * STRETCH // TOK_DEV)
    attn_routes = jax.vmap(lambda own, number: deal_out(jax.random.fold_in(key_list[3], 2), own, number, TOK_DEV, EA, TOPK, MOST, 2))(attn_routes_keys, attn_routes_turns).reshape((N_REQ, STRETCH, TOPK))
    mlp_routes_keys = jax.random.split(jax.random.fold_in(key_list[4], 1), N_REQ * STRETCH // TOK_DEV)
    mlp_routes_turns = jax.random.permutation(jax.random.fold_in(key_list[4], 3), N_REQ * STRETCH // TOK_DEV)
    mlp_routes = jax.vmap(lambda own, number: deal_out(jax.random.fold_in(key_list[4], 2), own, number, TOK_DEV, EM, TOPK, MOST, 2))(mlp_routes_keys, mlp_routes_turns).reshape((N_REQ, STRETCH, TOPK))
    norm_attn = jnp.clip(1.0 + 0.1 * jax.random.normal(key_list[5], (D,), jnp.float32), 0.5, 1.5)
    attn_router = centred(key_list[6], (D, EA), D ** -0.5, 0.125)
    w_query = centred(key_list[7], (KVH * EA, D, HD), D ** -0.5, 0.125, ((0, 8),))
    w_keyval = centred(key_list[8], (D, 2 * KVH * HD), D ** -0.5, 0.125, ((1, 8),))
    w_out = centred(key_list[9], (KVH * EA, HD, D), (KVH * HD) ** -0.5, 0.125, ((0, 8),))
    norm_mlp = jnp.clip(1.0 + 0.1 * jax.random.normal(key_list[10], (D,), jnp.float32), 0.5, 1.5)
    mlp_router = centred(key_list[11], (D, EM), D ** -0.5, 0.125)
    w_gate = centred(key_list[12], (EM * SPLIT, D, FFS), D ** -0.5, 0.125, ((0, 8),))
    w_up = centred(key_list[13], (EM * SPLIT, D, FFS), D ** -0.5, 0.125, ((0, 8),))
    w_down = centred(key_list[14], (EM * SPLIT, FFS, D), FF ** -0.5, 0.078125, ((0, 8),))
    return dict(tokens=tokens, cache=cache, cache_len=cache_len, attn_routes=attn_routes, mlp_routes=mlp_routes, norm_attn=norm_attn, attn_router=attn_router, w_query=w_query, w_keyval=w_keyval, w_out=w_out, norm_mlp=norm_mlp, mlp_router=mlp_router, w_gate=w_gate, w_up=w_up, w_down=w_down)


epsilon = 1e-05
rope_base = 10000.0
masked_score = -1e+30

def rms_norm(values, gain_vec):
    widened = values.astype(jnp.float32)
    inv_rms = lax.rsqrt(lax.optimization_barrier(jnp.mean(widened * widened, axis=-1, keepdims=True)) + epsilon)
    return (widened * inv_rms * gain_vec.astype(jnp.float32)).astype(jnp.bfloat16)

def rotate(values, position):
    half_dim = values.shape[-1] // 2
    inv_freq = rope_base ** (-jnp.arange(half_dim).astype(jnp.float32) / half_dim)
    angles = position.astype(jnp.float32)[..., None] * inv_freq
    cosine = jnp.cos(angles)
    sines = jnp.sin(angles)
    first_half = values[..., :half_dim]
    second_half = values[..., half_dim:]
    return jnp.concatenate([first_half * cosine - second_half * sines, second_half * cosine + first_half * sines], axis=-1)

def pick_gates(normed, router, routes):
    logits = jnp.dot(normed, router, preferred_element_type=jnp.float32)
    labels = jnp.arange(router.shape[1], dtype=jnp.int32)
    onehot = (routes[:, :, None] == labels[None, None, :]).astype(jnp.float32)
    chosen = lax.optimization_barrier(jnp.sum(onehot * logits[:, None, :], axis=-1))
    return jax.nn.softmax(chosen, axis=-1)

def one_group(tokens, cache, length, attn_routes, mlp_routes, norm_attn, attn_router, w_query, w_keyval, w_out, norm_mlp, mlp_router, w_gate, w_up, w_down):
    row_count = tokens.shape[0]
    normed = rms_norm(tokens, norm_attn)
    new_pos = length + jnp.arange(row_count, dtype=jnp.int32)
    fresh_kv = jnp.dot(normed, w_keyval, preferred_element_type=jnp.float32).reshape(row_count, KVH, 2, HD)
    fresh_kv = jnp.stack([rotate(fresh_kv[:, :, 0], new_pos[:, None]), fresh_kv[:, :, 1]], axis=2).astype(jnp.bfloat16)
    fresh_flat = fresh_kv.reshape(row_count, 2 * KVH * HD)
    padded = jnp.concatenate([cache, jnp.zeros((row_count, 2 * KVH * HD), jnp.bfloat16)], axis=0)
    placed = lax.dynamic_update_slice(jnp.zeros_like(padded), fresh_flat, (length.astype(jnp.int32), jnp.int32(0)))
    slot_ids = jnp.arange(CACHE_MAX + row_count, dtype=jnp.int32)
    cache_next = jnp.where((slot_ids < length)[:, None], padded, placed)
    old_kv = cache.reshape(CACHE_MAX, KVH, 2, HD)
    key_all = jnp.concatenate([old_kv[:, :, 0], fresh_kv[:, :, 0]], axis=0)
    value_all = jnp.concatenate([old_kv[:, :, 1], fresh_kv[:, :, 1]], axis=0)
    attn_gates = pick_gates(normed, attn_router, attn_routes)
    normed_pad = jnp.concatenate([normed, jnp.zeros((1, D), jnp.bfloat16)], axis=0)
    quarters = KVH // HPD
    query_w = jnp.swapaxes(w_query.reshape(quarters, EA, HPD, D, HD), 1, 2).reshape(KVH, EA, D, HD)
    out_w = jnp.swapaxes(w_out.reshape(quarters, EA, HPD, HD, D), 1, 2).reshape(KVH, EA, HD, D)
    attn_sum = jnp.zeros((row_count, D), jnp.float32)
    for expert in range(EA):
        matches = attn_routes == expert
        weight = lax.optimization_barrier(jnp.sum(jnp.where(matches, attn_gates, 0.0), axis=1))
        weight_pad = jnp.concatenate([weight, jnp.zeros((1,), jnp.float32)], axis=0)
        picked = jnp.nonzero(jnp.any(matches, axis=1), size=CAPACITY, fill_value=row_count)[0].astype(jnp.int32)
        chosen = normed_pad[picked].astype(jnp.float32)
        queries = jnp.einsum('sd,jdk->sjk', chosen, query_w[:, expert].astype(jnp.float32))
        queries = rotate(queries, (length + picked)[:, None]).astype(jnp.bfloat16)
        visible = jnp.where(slot_ids[None, :] < CACHE_MAX, slot_ids[None, :] < length, slot_ids[None, :] - CACHE_MAX <= picked[:, None])

        def per_head(inputs):
            query_head, key_head, value_head = inputs
            scores = jnp.dot(query_head, key_head.T, preferred_element_type=jnp.float32) * HD ** (-0.5)
            scores = jnp.where(visible, scores, masked_score)
            top_score = lax.optimization_barrier(jnp.max(scores, axis=-1, keepdims=True))
            weights = jnp.exp(scores - top_score)
            total = lax.optimization_barrier(jnp.sum(weights, axis=-1, keepdims=True))
            summed = jnp.dot(weights.astype(jnp.bfloat16), value_head, preferred_element_type=jnp.float32)
            return (summed / total).astype(jnp.bfloat16)
        head_outs = lax.map(per_head, (jnp.swapaxes(queries, 0, 1), jnp.swapaxes(key_all, 0, 1), jnp.swapaxes(value_all, 0, 1)))
        head_outs = lax.optimization_barrier(head_outs)
        projected = jnp.einsum('jsk,jkd->sd', head_outs.astype(jnp.float32), out_w[:, expert].astype(jnp.float32))
        attn_sum = attn_sum.at[picked].add(projected * weight_pad[picked][:, None], mode='drop')
    middle = lax.optimization_barrier((tokens.astype(jnp.float32) + attn_sum).astype(jnp.bfloat16))
    normed_mlp = rms_norm(middle, norm_mlp)
    mlp_gates = pick_gates(normed_mlp, mlp_router, mlp_routes)
    normed_mlp_pad = jnp.concatenate([normed_mlp, jnp.zeros((1, D), jnp.bfloat16)], axis=0)
    mlp_sum = jnp.zeros((row_count, D), jnp.float32)
    for expert in range(EM):
        matches = mlp_routes == expert
        weight = lax.optimization_barrier(jnp.sum(jnp.where(matches, mlp_gates, 0.0), axis=1))
        weight_pad = jnp.concatenate([weight, jnp.zeros((1,), jnp.float32)], axis=0)
        picked = jnp.nonzero(jnp.any(matches, axis=1), size=CAPACITY, fill_value=row_count)[0].astype(jnp.int32)
        chosen = normed_mlp_pad[picked]
        total_out = jnp.zeros((CAPACITY, D), jnp.float32)
        for slice_idx in range(SPLIT):
            weight_idx = expert * SPLIT + slice_idx
            gate_part = jnp.dot(chosen, w_gate[weight_idx], preferred_element_type=jnp.float32)
            up_part = jnp.dot(chosen, w_up[weight_idx], preferred_element_type=jnp.float32)
            hidden = (jax.nn.silu(gate_part) * up_part).astype(jnp.bfloat16)
            slice_out = lax.optimization_barrier(jnp.dot(hidden, w_down[weight_idx], preferred_element_type=jnp.float32).astype(jnp.bfloat16))
            total_out = total_out + slice_out.astype(jnp.float32)
        mlp_sum = mlp_sum.at[picked].add(total_out * weight_pad[picked][:, None], mode='drop')
    hidden_out = (middle.astype(jnp.float32) + mlp_sum).astype(jnp.bfloat16)
    return (hidden_out, cache_next)

def reference(tokens, cache, cache_len, attn_routes, mlp_routes, norm_attn, attn_router, w_query, w_keyval, w_out, norm_mlp, mlp_router, w_gate, w_up, w_down):
    outputs = []
    cache_list = []
    for group_idx in range(N_REQ):
        layer_out, cache_next = one_group(tokens[group_idx], cache[group_idx], cache_len[group_idx], attn_routes[group_idx], mlp_routes[group_idx], norm_attn, attn_router, w_query, w_keyval, w_out, norm_mlp, mlp_router, w_gate, w_up, w_down)
        outputs.append(layer_out)
        cache_list.append(cache_next)
    return (jnp.stack(outputs, axis=0), jnp.stack(cache_list, axis=0))
```

```python
import math

import jax
import jax.numpy as jnp
from jax import lax
from jax.sharding import PartitionSpec as P

MOST = 24


epsilon = 1e-05
rope_base = 10000.0
masked_score = -1e30


def from_partner(value, axis, stride):
    mask = 2**stride
    pairs = [(source, source ^ mask) for source in range(lax.axis_size(axis))]
    return lax.ppermute(value, axis, pairs)


def rms_norm(values, gain_vec):
    widened = values.astype(jnp.float32)
    inv_rms = lax.rsqrt(jnp.mean(widened * widened, axis=-1, keepdims=True) + epsilon)
    return (widened * inv_rms * gain_vec).astype(jnp.bfloat16)


def rotate(values, position):
    half_dim = values.shape[-1] // 2
    inv_freq = rope_base ** (-jnp.arange(half_dim).astype(jnp.float32) / half_dim)
    angles = position.astype(jnp.float32)[..., None] * inv_freq
    cosine = jnp.cos(angles)
    sines = jnp.sin(angles)
    first_half = values[..., :half_dim]
    second_half = values[..., half_dim:]
    return jnp.concatenate(
        [first_half * cosine - second_half * sines, second_half * cosine + first_half * sines],
        axis=-1,
    )


def pick_gates(normed, router, routes):
    logits = jnp.dot(normed, router, preferred_element_type=jnp.float32)
    labels = jnp.arange(router.shape[1], dtype=jnp.int32)
    onehot = (routes[:, :, None] == labels[None, None, :]).astype(jnp.float32)
    chosen = jnp.sum(onehot * logits[:, None, :], axis=-1)
    return jax.nn.softmax(chosen, axis=-1)


def slot_tables(routes, gates, labels, rows_block, slot_count):
    row_total = routes.shape[0]
    block_count = row_total // rows_block
    matches = routes[:, :, None] == labels[None, None, :]
    member = jnp.any(matches, axis=1).astype(jnp.int32).reshape(block_count, rows_block, -1)
    weight = jnp.sum(jnp.where(matches, gates[:, :, None], 0.0), axis=1).reshape(
        block_count, rows_block, -1
    )
    ranking = jnp.cumsum(member, axis=1) - 1
    slot_ids = jnp.arange(slot_count, dtype=jnp.int32)
    onehot = ((member[..., None] > 0) & (ranking[..., None] == slot_ids)).astype(jnp.int32)
    local_row = jnp.arange(rows_block, dtype=jnp.int32)[None, :, None, None]
    token_ids = (
        jnp.sum(onehot * local_row, axis=1)
        + (jnp.arange(block_count, dtype=jnp.int32) * rows_block)[:, None, None]
    )
    shares = jnp.sum(onehot.astype(jnp.float32) * weight[..., None], axis=1)
    return (token_ids, shares)


def spread_rows(terms, token_ids, extent):
    term_part = terms.reshape(-1, terms.shape[-1])
    id_part = token_ids.reshape(-1)
    return jnp.zeros((extent, terms.shape[-1]), jnp.float32).at[id_part].add(term_part, mode="drop")


def attend(queries, query_pos, key_cache, value_cache, key_fresh, value_fresh, length):
    query_count = queries.shape[0]
    head_dim = queries.shape[1]
    factor = head_dim ** (-0.5)

    def absorb(state, key_block, value_block, visible):
        running_top, running_total, running_acc = state
        scores = jnp.dot(queries, key_block.T, preferred_element_type=jnp.float32) * factor
        scores = jnp.where(visible, scores, masked_score)
        new_top = jnp.maximum(running_top, jnp.max(scores, axis=1))
        fading = jnp.exp(running_top - new_top)
        weights = jnp.exp(scores - new_top[:, None])
        running_total = running_total * fading + jnp.sum(weights, axis=1)
        running_acc = running_acc * fading[:, None] + jnp.dot(
            weights.astype(jnp.bfloat16), value_block, preferred_element_type=jnp.float32
        )
        return (new_top, running_total, running_acc)

    state = (
        jnp.full((query_count,), masked_score, jnp.float32),
        jnp.zeros((query_count,), jnp.float32),
        jnp.zeros((query_count, head_dim), jnp.float32),
    )
    cache_span = math.gcd(512, key_cache.shape[0])

    def cache_step(step_idx, state):
        offset = step_idx * cache_span
        key_block = lax.dynamic_slice_in_dim(key_cache, offset, cache_span, 0)
        value_block = lax.dynamic_slice_in_dim(value_cache, offset, cache_span, 0)
        visible = (offset + jnp.arange(cache_span, dtype=jnp.int32))[None, :] < length
        return absorb(state, key_block, value_block, visible)

    state = lax.fori_loop(0, (length + cache_span - 1) // cache_span, cache_step, state)
    fresh_span = math.gcd(512, key_fresh.shape[0])
    for offset in range(0, key_fresh.shape[0], fresh_span):
        visible = (offset + jnp.arange(fresh_span, dtype=jnp.int32))[None, :] <= query_pos[:, None]
        state = absorb(
            state,
            key_fresh[offset : offset + fresh_span],
            value_fresh[offset : offset + fresh_span],
            visible,
        )
    running_top, running_total, running_acc = state
    return (running_acc / running_total[:, None]).astype(jnp.bfloat16)


def local_slots(routes, labels, slot_count):
    matches = routes[:, :, None] == labels[None, None, :]
    member = jnp.any(matches, axis=1).astype(jnp.int32)
    ranking = jnp.cumsum(member, axis=0) - 1
    slot_ids = jnp.arange(slot_count, dtype=jnp.int32)
    onehot = ((member[..., None] > 0) & (ranking[..., None] == slot_ids)).astype(jnp.int32)
    rows = jnp.arange(routes.shape[0], dtype=jnp.int32)[:, None, None]
    return jnp.sum(onehot * rows, axis=0)


def route_slots(routes, label_count):
    labels = jnp.arange(label_count, dtype=jnp.int32)
    member = jnp.any(routes[:, :, None] == labels[None, None, :], axis=1).astype(jnp.int32)
    ranking = jnp.cumsum(member, axis=0) - 1
    return jnp.take_along_axis(ranking, routes, axis=1)


def combine(received, routes, gates, slots, split_count):
    slot_count = received.shape[1]
    flat = received.reshape(-1, received.shape[-1])
    total = jnp.zeros((routes.shape[0], received.shape[-1]), jnp.float32)
    for route in range(routes.shape[1]):
        expert = routes[:, route]
        part = jnp.zeros_like(total)
        for piece in range(split_count):
            index = (expert * split_count + piece) * slot_count + slots[:, route]
            part = part + flat[index].astype(jnp.float32)
        total = total + part * gates[:, route][:, None]
    return total


def head_attention(queries, query_pos, keys, values, length, cache_limit):
    factor = queries.shape[-1] ** (-0.5)
    scores = jnp.einsum("hqk,hsk->hqs", queries, keys, preferred_element_type=jnp.float32) * factor
    slot_ids = jnp.arange(keys.shape[1], dtype=jnp.int32)[None, :]
    visible = jnp.where(
        slot_ids < cache_limit, slot_ids < length, slot_ids - cache_limit <= query_pos[:, None]
    )
    scores = jnp.where(visible[None], scores, masked_score)
    top = jnp.max(scores, axis=-1, keepdims=True)
    weights = jnp.exp(scores - top)
    total = jnp.sum(weights, axis=-1, keepdims=True)
    summed = jnp.einsum(
        "hqs,hsk->hqk", weights.astype(jnp.bfloat16), values, preferred_element_type=jnp.float32
    )
    return (summed / total).astype(jnp.bfloat16)


def body(
    tokens,
    cache,
    cache_len,
    attn_routes,
    mlp_routes,
    norm_attn,
    attn_router,
    w_query,
    w_keyval,
    w_out,
    norm_mlp,
    mlp_router,
    w_gate,
    w_up,
    w_down,
):
    device_count = lax.axis_size("exp")
    position = lax.axis_index("exp")
    own_rows = tokens[0]
    rows_block = own_rows.shape[0]
    model_width = own_rows.shape[1]
    length = cache_len[0]
    slot_count = MOST
    heads_here = w_query.shape[0]
    head_dim = w_query.shape[2]
    columns = w_keyval.shape[1]
    experts_attn = attn_router.shape[1]
    kv_heads = columns * device_count // (2 * head_dim)
    fast_attn = (
        device_count == experts_attn and heads_here == kv_heads and columns % (2 * head_dim) == 0
    )
    if not fast_attn:
        return base_body(
            tokens, cache, cache_len, attn_routes, mlp_routes, norm_attn, attn_router, w_query,
            w_keyval, w_out, norm_mlp, mlp_router, w_gate, w_up, w_down,
        )
    normed = rms_norm(own_rows, norm_attn)
    route_rows = jnp.zeros((16, model_width), jnp.bfloat16)
    route_rows = route_rows.at[0, : 2 * rows_block].set(
        attn_routes[0].reshape(-1).astype(jnp.bfloat16)
    )
    gathered = lax.all_gather(
        jnp.concatenate([normed, route_rows], axis=0), "exp", axis=0, tiled=False
    )
    group_normed = gathered[:, :rows_block].reshape(-1, model_width)
    group_routes = (
        gathered[:, rows_block, : 2 * rows_block].astype(jnp.int32).reshape(-1, 2)
    )
    row_total = group_normed.shape[0]
    block_count = row_total // rows_block
    new_pos = length + jnp.arange(row_total, dtype=jnp.int32)
    fresh_kv = jnp.dot(group_normed, w_keyval, preferred_element_type=jnp.float32)
    split_new = fresh_kv.reshape(row_total, columns // (2 * head_dim), 2, head_dim)
    rotated = rotate(split_new[:, :, 0], new_pos[:, None])
    fresh_kv = (
        jnp.stack([rotated, split_new[:, :, 1]], axis=2)
        .astype(jnp.bfloat16)
        .reshape(row_total, columns)
    )
    cache_limit = cache.shape[1]
    padded = jnp.concatenate([cache[0], jnp.zeros((row_total, columns), jnp.bfloat16)], axis=0)
    placed = lax.dynamic_update_slice(jnp.zeros_like(padded), fresh_kv, (length, jnp.int32(0)))
    slot_ids = jnp.arange(cache_limit + row_total, dtype=jnp.int32)
    cache_next = jnp.where((slot_ids < length)[:, None], padded, placed)

    all_labels = jnp.arange(experts_attn, dtype=jnp.int32)
    blocks_routes = group_routes.reshape(block_count, rows_block, -1)
    slot_tokens = jax.vmap(lambda r: local_slots(r, all_labels, slot_count))(blocks_routes)
    slot_tokens = slot_tokens + (jnp.arange(block_count, dtype=jnp.int32) * rows_block)[:, None, None]
    expert_tokens = jnp.swapaxes(slot_tokens, 0, 1).reshape(experts_attn, -1)
    my_tokens = expert_tokens[position]
    picked_rows = group_normed[my_tokens]
    queries = jnp.einsum("sd,hdk->hsk", picked_rows, w_query, preferred_element_type=jnp.float32)
    queries = rotate(queries, (length + my_tokens)[None, :]).astype(jnp.bfloat16)
    heads_local = columns // (2 * head_dim)
    query_slots = queries.shape[1]
    send_q = queries.reshape(device_count, heads_local, query_slots, head_dim)
    recv_q = lax.all_to_all(send_q, "exp", 0, 0, tiled=True)
    recv_q = jnp.swapaxes(recv_q, 0, 1).reshape(heads_local, device_count * query_slots, head_dim)
    query_pos = expert_tokens.reshape(-1)
    split_old = cache[0].reshape(cache_limit, heads_local, 2, head_dim)
    split_fresh = fresh_kv.reshape(row_total, heads_local, 2, head_dim)
    keys = jnp.swapaxes(jnp.concatenate([split_old[:, :, 0], split_fresh[:, :, 0]], axis=0), 0, 1)
    values = jnp.swapaxes(jnp.concatenate([split_old[:, :, 1], split_fresh[:, :, 1]], axis=0), 0, 1)
    head_outs = head_attention(recv_q, query_pos, keys, values, length, cache_limit)
    send_o = jnp.swapaxes(
        head_outs.reshape(heads_local, device_count, query_slots, head_dim), 0, 1
    )
    recv_o = lax.all_to_all(send_o, "exp", 0, 0, tiled=True)
    recv_o = recv_o.reshape(heads_here, query_slots, head_dim)
    projected = jnp.einsum("hsk,hkd->sd", recv_o, w_out, preferred_element_type=jnp.float32)
    send_p = projected.astype(jnp.bfloat16).reshape(block_count, slot_count, model_width)
    recv_p = lax.all_to_all(send_p, "exp", 0, 0, tiled=True)
    own_attn_routes = attn_routes[0]
    attn_gates = pick_gates(normed, attn_router, own_attn_routes)
    attn_own = combine(
        recv_p, own_attn_routes, attn_gates, route_slots(own_attn_routes, experts_attn), 1
    )
    middle = (own_rows.astype(jnp.float32) + attn_own).astype(jnp.bfloat16)
    normed_mlp = rms_norm(middle, norm_mlp)
    experts_mlp = mlp_router.shape[1]
    split_count = device_count // experts_mlp
    own_mlp_routes = mlp_routes[0]
    mlp_gates = pick_gates(normed_mlp, mlp_router, own_mlp_routes)
    mlp_tokens = local_slots(own_mlp_routes, jnp.arange(experts_mlp, dtype=jnp.int32), slot_count)
    dest_tokens = jnp.repeat(mlp_tokens, split_count, axis=0)
    send_m = normed_mlp[dest_tokens.reshape(-1)].reshape(device_count, slot_count, model_width)
    inputs = lax.all_to_all(send_m, "exp", 0, 0, tiled=True).reshape(-1, model_width)
    gate_part = jnp.dot(inputs, w_gate[0], preferred_element_type=jnp.float32)
    up_part = jnp.dot(inputs, w_up[0], preferred_element_type=jnp.float32)
    hidden = (jax.nn.silu(gate_part) * up_part).astype(jnp.bfloat16)
    slice_out = jnp.dot(hidden, w_down[0], preferred_element_type=jnp.float32).astype(jnp.bfloat16)
    recv_m = lax.all_to_all(
        slice_out.reshape(device_count, slot_count, model_width), "exp", 0, 0, tiled=True
    )
    mlp_own = combine(
        recv_m, own_mlp_routes, mlp_gates, route_slots(own_mlp_routes, experts_mlp), split_count
    )
    layer_out = (middle.astype(jnp.float32) + mlp_own).astype(jnp.bfloat16)
    return (layer_out[None], cache_next[None])


def base_body(
    tokens,
    cache,
    cache_len,
    attn_routes,
    mlp_routes,
    norm_attn,
    attn_router,
    w_query,
    w_keyval,
    w_out,
    norm_mlp,
    mlp_router,
    w_gate,
    w_up,
    w_down,
):
    device_count = lax.axis_size("exp")
    position = lax.axis_index("exp")
    own_rows = tokens[0]
    rows_block = own_rows.shape[0]
    model_width = own_rows.shape[1]
    length = cache_len[0]
    slot_count = MOST
    normed = rms_norm(own_rows, norm_attn)
    group_normed, group_routes = (
        lax.all_gather(normed, "exp", axis=0, tiled=True),
        lax.all_gather(attn_routes[0], "exp", axis=0, tiled=True),
    )
    row_total = group_normed.shape[0]
    block_count = row_total // rows_block
    heads_here = w_query.shape[0]
    head_dim = w_query.shape[2]
    columns = w_keyval.shape[1]
    experts_attn = attn_router.shape[1]
    my_attn = jnp.reshape(position % experts_attn, (1,))
    new_pos = length + jnp.arange(row_total, dtype=jnp.int32)
    fresh_kv = jnp.dot(group_normed, w_keyval, preferred_element_type=jnp.float32)
    if columns < 2 * head_dim:
        is_key = position % 2 == 0
        fresh_kv = jnp.where(is_key, rotate(fresh_kv, new_pos), fresh_kv).astype(jnp.bfloat16)
    else:
        split_new = fresh_kv.reshape(row_total, columns // (2 * head_dim), 2, head_dim)
        rotated = rotate(split_new[:, :, 0], new_pos[:, None])
        fresh_kv = (
            jnp.stack([rotated, split_new[:, :, 1]], axis=2)
            .astype(jnp.bfloat16)
            .reshape(row_total, columns)
        )
    cache_limit = cache.shape[1]
    padded = jnp.concatenate([cache[0], jnp.zeros((row_total, columns), jnp.bfloat16)], axis=0)
    placed = lax.dynamic_update_slice(jnp.zeros_like(padded), fresh_kv, (length, jnp.int32(0)))
    slot_ids = jnp.arange(cache_limit + row_total, dtype=jnp.int32)
    cache_next = jnp.where((slot_ids < length)[:, None], padded, placed)
    group_cache = cache[0]
    group_fresh = fresh_kv
    for bit in range(experts_attn.bit_length() - 1):
        other_cache, other_fresh = from_partner((group_cache, group_fresh), "exp", bit)
        lower = position // (1 << bit) % 2 == 0
        group_cache = jnp.where(
            lower,
            jnp.concatenate([group_cache, other_cache], axis=1),
            jnp.concatenate([other_cache, group_cache], axis=1),
        )
        group_fresh = jnp.where(
            lower,
            jnp.concatenate([group_fresh, other_fresh], axis=1),
            jnp.concatenate([other_fresh, group_fresh], axis=1),
        )
    split_old = group_cache.reshape(cache_limit, heads_here, 2, head_dim)
    split_fresh = group_fresh.reshape(row_total, heads_here, 2, head_dim)
    attn_gates = pick_gates(group_normed, attn_router, group_routes)
    attn_tokens, attn_shares = slot_tables(
        group_routes, attn_gates, my_attn, rows_block, slot_count
    )
    token_flat = attn_tokens[:, 0, :].reshape(-1)
    share_flat = attn_shares[:, 0, :].reshape(-1)
    picked_rows = group_normed[token_flat]
    queries = jnp.einsum("sd,hdk->hsk", picked_rows, w_query, preferred_element_type=jnp.float32)
    queries = rotate(queries, (length + token_flat)[None, :]).astype(jnp.bfloat16)
    attend_heads = jax.vmap(attend, in_axes=(0, None, 1, 1, 1, 1, None))
    head_outs = attend_heads(
        queries,
        token_flat,
        split_old[:, :, 0],
        split_old[:, :, 1],
        split_fresh[:, :, 0],
        split_fresh[:, :, 1],
        length,
    )
    projected = jnp.einsum("hsk,hkd->sd", head_outs, w_out, preferred_element_type=jnp.float32)
    projected = (projected * share_flat[:, None]).reshape(block_count, slot_count, model_width)
    attn_ids = attn_tokens[:, 0, :]
    attn_own = lax.psum_scatter(
        spread_rows(projected, attn_ids, rows_block * lax.axis_size("exp")).astype(jnp.bfloat16),
        "exp",
        scatter_dimension=0,
        tiled=True,
    ).astype(jnp.float32)
    middle = lax.optimization_barrier(
        (own_rows.astype(jnp.float32) + attn_own).astype(jnp.bfloat16)
    )
    normed_mlp = rms_norm(middle, norm_mlp)
    experts_mlp = mlp_router.shape[1]
    split_count = device_count // experts_mlp
    my_expert = jnp.reshape(position // split_count, (1,))
    all_normed, all_routes = (
        lax.all_gather(normed_mlp, "exp", axis=0, tiled=True),
        lax.all_gather(mlp_routes[0], "exp", axis=0, tiled=True),
    )
    all_gates = pick_gates(all_normed, mlp_router, all_routes)
    mlp_tokens, mlp_shares = slot_tables(all_routes, all_gates, my_expert, rows_block, slot_count)
    inputs = all_normed[mlp_tokens.reshape(-1)]
    gate_part = jnp.dot(inputs, w_gate[0], preferred_element_type=jnp.float32)
    up_part = jnp.dot(inputs, w_up[0], preferred_element_type=jnp.float32)
    hidden = (jax.nn.silu(gate_part) * up_part).astype(jnp.bfloat16)
    slice_out = lax.optimization_barrier(
        jnp.dot(hidden, w_down[0], preferred_element_type=jnp.float32).astype(jnp.bfloat16)
    )
    weighted = (slice_out.astype(jnp.float32) * mlp_shares.reshape(-1)[:, None]).reshape(
        block_count, slot_count, model_width
    )
    mlp_ids = mlp_tokens[:, 0, :]
    mlp_own = lax.psum_scatter(
        spread_rows(weighted, mlp_ids, rows_block * lax.axis_size("exp")).astype(jnp.bfloat16),
        "exp",
        scatter_dimension=0,
        tiled=True,
    ).astype(jnp.float32)
    layer_out = (middle.astype(jnp.float32) + mlp_own).astype(jnp.bfloat16)
    return (layer_out[None], cache_next[None])


def solution(mesh):
    placed = (
        P("req", "exp", None),
        P("req", None, "exp"),
        P("req"),
        P("req", "exp", None),
        P("req", "exp", None),
        P(),
        P(),
        P("exp", None, None),
        P(None, "exp"),
        P("exp", None, None),
        P(),
        P(),
        P("exp", None, None),
        P("exp", None, None),
        P("exp", None, None),
    )
    return jax.shard_map(
        body,
        mesh=mesh,
        in_specs=placed,
        out_specs=(P("req", "exp", None), P("req", None, "exp")),
        check_vma=False,
    )
```

```python
import math

import jax
import jax.numpy as jnp
from jax import lax
from jax.experimental import pallas as pl
from jax.experimental.pallas import tpu as pltpu
from jax.sharding import PartitionSpec as P

MOST = 24


epsilon = 1e-05
rope_base = 10000.0
masked_score = -1e30


def from_partner(value, axis, stride):
    mask = 2**stride
    pairs = [(source, source ^ mask) for source in range(lax.axis_size(axis))]
    return lax.ppermute(value, axis, pairs)


def rms_norm(values, gain_vec):
    widened = values.astype(jnp.float32)
    inv_rms = lax.rsqrt(jnp.mean(widened * widened, axis=-1, keepdims=True) + epsilon)
    return (widened * inv_rms * gain_vec).astype(jnp.bfloat16)


def rotate(values, position):
    half_dim = values.shape[-1] // 2
    inv_freq = rope_base ** (-jnp.arange(half_dim).astype(jnp.float32) / half_dim)
    angles = position.astype(jnp.float32)[..., None] * inv_freq
    cosine = jnp.cos(angles)
    sines = jnp.sin(angles)
    first_half = values[..., :half_dim]
    second_half = values[..., half_dim:]
    return jnp.concatenate(
        [first_half * cosine - second_half * sines, second_half * cosine + first_half * sines],
        axis=-1,
    )


def pick_gates(normed, router, routes):
    logits = jnp.dot(normed, router, preferred_element_type=jnp.float32)
    labels = jnp.arange(router.shape[1], dtype=jnp.int32)
    onehot = (routes[:, :, None] == labels[None, None, :]).astype(jnp.float32)
    chosen = jnp.sum(onehot * logits[:, None, :], axis=-1)
    return jax.nn.softmax(chosen, axis=-1)


def slot_tables(routes, gates, labels, rows_block, slot_count):
    row_total = routes.shape[0]
    block_count = row_total // rows_block
    matches = routes[:, :, None] == labels[None, None, :]
    member = jnp.any(matches, axis=1).astype(jnp.int32).reshape(block_count, rows_block, -1)
    weight = jnp.sum(jnp.where(matches, gates[:, :, None], 0.0), axis=1).reshape(
        block_count, rows_block, -1
    )
    ranking = jnp.cumsum(member, axis=1) - 1
    slot_ids = jnp.arange(slot_count, dtype=jnp.int32)
    onehot = ((member[..., None] > 0) & (ranking[..., None] == slot_ids)).astype(jnp.int32)
    local_row = jnp.arange(rows_block, dtype=jnp.int32)[None, :, None, None]
    token_ids = (
        jnp.sum(onehot * local_row, axis=1)
        + (jnp.arange(block_count, dtype=jnp.int32) * rows_block)[:, None, None]
    )
    shares = jnp.sum(onehot.astype(jnp.float32) * weight[..., None], axis=1)
    return (token_ids, shares)


def spread_rows(terms, token_ids, extent):
    term_part = terms.reshape(-1, terms.shape[-1])
    id_part = token_ids.reshape(-1)
    return jnp.zeros((extent, terms.shape[-1]), jnp.float32).at[id_part].add(term_part, mode="drop")


def attend(queries, query_pos, key_cache, value_cache, key_fresh, value_fresh, length):
    query_count = queries.shape[0]
    head_dim = queries.shape[1]
    factor = head_dim ** (-0.5)

    def absorb(state, key_block, value_block, visible):
        running_top, running_total, running_acc = state
        scores = jnp.dot(queries, key_block.T, preferred_element_type=jnp.float32) * factor
        scores = jnp.where(visible, scores, masked_score)
        new_top = jnp.maximum(running_top, jnp.max(scores, axis=1))
        fading = jnp.exp(running_top - new_top)
        weights = jnp.exp(scores - new_top[:, None])
        running_total = running_total * fading + jnp.sum(weights, axis=1)
        running_acc = running_acc * fading[:, None] + jnp.dot(
            weights.astype(jnp.bfloat16), value_block, preferred_element_type=jnp.float32
        )
        return (new_top, running_total, running_acc)

    state = (
        jnp.full((query_count,), masked_score, jnp.float32),
        jnp.zeros((query_count,), jnp.float32),
        jnp.zeros((query_count, head_dim), jnp.float32),
    )
    cache_span = math.gcd(512, key_cache.shape[0])

    def cache_step(step_idx, state):
        offset = step_idx * cache_span
        key_block = lax.dynamic_slice_in_dim(key_cache, offset, cache_span, 0)
        value_block = lax.dynamic_slice_in_dim(value_cache, offset, cache_span, 0)
        visible = (offset + jnp.arange(cache_span, dtype=jnp.int32))[None, :] < length
        return absorb(state, key_block, value_block, visible)

    state = lax.fori_loop(0, (length + cache_span - 1) // cache_span, cache_step, state)
    fresh_span = math.gcd(512, key_fresh.shape[0])
    for offset in range(0, key_fresh.shape[0], fresh_span):
        visible = (offset + jnp.arange(fresh_span, dtype=jnp.int32))[None, :] <= query_pos[:, None]
        state = absorb(
            state,
            key_fresh[offset : offset + fresh_span],
            value_fresh[offset : offset + fresh_span],
            visible,
        )
    running_top, running_total, running_acc = state
    return (running_acc / running_total[:, None]).astype(jnp.bfloat16)


def running_count(member):
    rows = member.shape[0]
    lower = (
        jnp.arange(rows, dtype=jnp.int32)[None, :] <= jnp.arange(rows, dtype=jnp.int32)[:, None]
    ).astype(jnp.bfloat16)
    counts = jnp.dot(lower, member.astype(jnp.bfloat16), preferred_element_type=jnp.float32)
    return counts.astype(jnp.int32)


def local_slots(routes, labels, slot_count):
    matches = routes[:, :, None] == labels[None, None, :]
    member = jnp.any(matches, axis=1).astype(jnp.int32)
    ranking = running_count(member) - 1
    slot_ids = jnp.arange(slot_count, dtype=jnp.int32)
    onehot = ((member[..., None] > 0) & (ranking[..., None] == slot_ids)).astype(jnp.int32)
    rows = jnp.arange(routes.shape[0], dtype=jnp.int32)[:, None, None]
    return jnp.sum(onehot * rows, axis=0)


def route_slots(routes, label_count):
    labels = jnp.arange(label_count, dtype=jnp.int32)
    member = jnp.any(routes[:, :, None] == labels[None, None, :], axis=1).astype(jnp.int32)
    ranking = running_count(member) - 1
    return jnp.take_along_axis(ranking, routes, axis=1)


def combine(received, routes, gates, slots, split_count):
    slot_count = received.shape[1]
    flat = received.reshape(-1, received.shape[-1])
    total = jnp.zeros((routes.shape[0], received.shape[-1]), jnp.float32)
    for route in range(routes.shape[1]):
        expert = routes[:, route]
        part = jnp.zeros_like(total)
        for piece in range(split_count):
            index = (expert * split_count + piece) * slot_count + slots[:, route]
            part = part + flat[index].astype(jnp.float32)
        total = total + part * gates[:, route][:, None]
    return total


def mlp_kernel(x_ref, gate_ref, up_ref, down_ref, out_ref, acc_ref):
    step = pl.program_id(0)

    @pl.when(step == 0)
    def _():
        acc_ref[...] = jnp.zeros_like(acc_ref)

    rows = x_ref[...]
    gate_part = jnp.dot(rows, gate_ref[...], preferred_element_type=jnp.float32)
    up_part = jnp.dot(rows, up_ref[...], preferred_element_type=jnp.float32)
    hidden = (gate_part / (1.0 + jnp.exp(-gate_part)) * up_part).astype(jnp.bfloat16)
    acc_ref[...] += jnp.dot(hidden, down_ref[...], preferred_element_type=jnp.float32)

    @pl.when(step == pl.num_programs(0) - 1)
    def _():
        out_ref[...] = acc_ref[...].astype(out_ref.dtype)


def expert_mlp(rows, w_gate, w_up, w_down):
    row_count, width = rows.shape
    hidden_units = w_gate.shape[-1]
    tile = next(t for t in (512, 256, 128) if hidden_units % t == 0)
    return pl.pallas_call(
        mlp_kernel,
        grid=(hidden_units // tile,),
        in_specs=[
            pl.BlockSpec((row_count, width), lambda k: (0, 0)),
            pl.BlockSpec((None, width, tile), lambda k: (0, 0, k)),
            pl.BlockSpec((None, width, tile), lambda k: (0, 0, k)),
            pl.BlockSpec((None, tile, width), lambda k: (0, k, 0)),
        ],
        out_specs=pl.BlockSpec((row_count, width), lambda k: (0, 0)),
        out_shape=jax.ShapeDtypeStruct((row_count, width), jnp.bfloat16),
        scratch_shapes=[pltpu.VMEM((row_count, width), jnp.float32)],
        compiler_params=pltpu.CompilerParams(dimension_semantics=("arbitrary",)),
    )(rows, w_gate, w_up, w_down)


def head_attention(queries, query_pos, keys, values, length, cache_limit):
    factor = queries.shape[-1] ** (-0.5)
    scores = jnp.einsum("hqk,hsk->hqs", queries, keys, preferred_element_type=jnp.float32) * factor
    slot_ids = jnp.arange(keys.shape[1], dtype=jnp.int32)[None, :]
    visible = jnp.where(
        slot_ids < cache_limit, slot_ids < length, slot_ids - cache_limit <= query_pos[:, None]
    )
    scores = jnp.where(visible[None], scores, masked_score)
    top = jnp.max(scores, axis=-1, keepdims=True)
    weights = jnp.exp(scores - top)
    total = jnp.sum(weights, axis=-1, keepdims=True)
    summed = jnp.einsum(
        "hqs,hsk->hqk", weights.astype(jnp.bfloat16), values, preferred_element_type=jnp.float32
    )
    return (summed / total).astype(jnp.bfloat16)


def body(
    tokens,
    cache,
    cache_len,
    attn_routes,
    mlp_routes,
    norm_attn,
    attn_router,
    w_query,
    w_keyval,
    w_out,
    norm_mlp,
    mlp_router,
    w_gate,
    w_up,
    w_down,
):
    device_count = lax.axis_size("exp")
    position = lax.axis_index("exp")
    own_rows = tokens[0]
    rows_block = own_rows.shape[0]
    model_width = own_rows.shape[1]
    length = cache_len[0]
    slot_count = MOST
    heads_here = w_query.shape[0]
    head_dim = w_query.shape[2]
    columns = w_keyval.shape[1]
    experts_attn = attn_router.shape[1]
    kv_heads = columns * device_count // (2 * head_dim)
    fast_attn = (
        device_count == experts_attn and heads_here == kv_heads and columns % (2 * head_dim) == 0
    )
    if not fast_attn:
        return base_body(
            tokens, cache, cache_len, attn_routes, mlp_routes, norm_attn, attn_router, w_query,
            w_keyval, w_out, norm_mlp, mlp_router, w_gate, w_up, w_down,
        )
    normed = rms_norm(own_rows, norm_attn)
    route_rows = jnp.zeros((16, model_width), jnp.bfloat16)
    route_rows = route_rows.at[0, : 2 * rows_block].set(
        attn_routes[0].reshape(-1).astype(jnp.bfloat16)
    )
    gathered = lax.all_gather(
        jnp.concatenate([normed, route_rows], axis=0), "exp", axis=0, tiled=False
    )
    group_normed = gathered[:, :rows_block].reshape(-1, model_width)
    group_routes = (
        gathered[:, rows_block, : 2 * rows_block].astype(jnp.int32).reshape(-1, 2)
    )
    row_total = group_normed.shape[0]
    block_count = row_total // rows_block
    new_pos = length + jnp.arange(row_total, dtype=jnp.int32)
    fresh_kv = jnp.dot(group_normed, w_keyval, preferred_element_type=jnp.float32)
    split_new = fresh_kv.reshape(row_total, columns // (2 * head_dim), 2, head_dim)
    rotated = rotate(split_new[:, :, 0], new_pos[:, None])
    fresh_kv = (
        jnp.stack([rotated, split_new[:, :, 1]], axis=2)
        .astype(jnp.bfloat16)
        .reshape(row_total, columns)
    )
    cache_limit = cache.shape[1]
    padded = jnp.concatenate([cache[0], jnp.zeros((row_total, columns), jnp.bfloat16)], axis=0)
    placed = lax.dynamic_update_slice(jnp.zeros_like(padded), fresh_kv, (length, jnp.int32(0)))
    slot_ids = jnp.arange(cache_limit + row_total, dtype=jnp.int32)
    cache_next = jnp.where((slot_ids < length)[:, None], padded, placed)

    all_labels = jnp.arange(experts_attn, dtype=jnp.int32)
    blocks_routes = group_routes.reshape(block_count, rows_block, -1)
    slot_tokens = jax.vmap(lambda r: local_slots(r, all_labels, slot_count))(blocks_routes)
    slot_tokens = slot_tokens + (jnp.arange(block_count, dtype=jnp.int32) * rows_block)[:, None, None]
    expert_tokens = jnp.swapaxes(slot_tokens, 0, 1).reshape(experts_attn, -1)
    my_tokens = expert_tokens[position]
    picked_rows = group_normed[my_tokens]
    queries = jnp.einsum("sd,hdk->hsk", picked_rows, w_query, preferred_element_type=jnp.float32)
    queries = rotate(queries, (length + my_tokens)[None, :]).astype(jnp.bfloat16)
    heads_local = columns // (2 * head_dim)
    query_slots = queries.shape[1]
    send_q = queries.reshape(device_count, heads_local, query_slots, head_dim)
    recv_q = lax.all_to_all(send_q, "exp", 0, 0, tiled=True)
    recv_q = jnp.swapaxes(recv_q, 0, 1).reshape(heads_local, device_count * query_slots, head_dim)
    query_pos = expert_tokens.reshape(-1)
    split_old = cache[0].reshape(cache_limit, heads_local, 2, head_dim)
    split_fresh = fresh_kv.reshape(row_total, heads_local, 2, head_dim)
    keys = jnp.swapaxes(jnp.concatenate([split_old[:, :, 0], split_fresh[:, :, 0]], axis=0), 0, 1)
    values = jnp.swapaxes(jnp.concatenate([split_old[:, :, 1], split_fresh[:, :, 1]], axis=0), 0, 1)
    head_outs = head_attention(recv_q, query_pos, keys, values, length, cache_limit)
    send_o = jnp.swapaxes(
        head_outs.reshape(heads_local, device_count, query_slots, head_dim), 0, 1
    )
    recv_o = lax.all_to_all(send_o, "exp", 0, 0, tiled=True)
    recv_o = recv_o.reshape(heads_here, query_slots, head_dim)
    projected = jnp.einsum("hsk,hkd->sd", recv_o, w_out, preferred_element_type=jnp.float32)
    send_p = projected.astype(jnp.bfloat16).reshape(block_count, slot_count, model_width)
    recv_p = lax.all_to_all(send_p, "exp", 0, 0, tiled=True)
    own_attn_routes = attn_routes[0]
    attn_gates = pick_gates(normed, attn_router, own_attn_routes)
    attn_own = combine(
        recv_p, own_attn_routes, attn_gates, route_slots(own_attn_routes, experts_attn), 1
    )
    middle = (own_rows.astype(jnp.float32) + attn_own).astype(jnp.bfloat16)
    normed_mlp = rms_norm(middle, norm_mlp)
    experts_mlp = mlp_router.shape[1]
    split_count = device_count // experts_mlp
    own_mlp_routes = mlp_routes[0]
    mlp_gates = pick_gates(normed_mlp, mlp_router, own_mlp_routes)
    mlp_tokens = local_slots(own_mlp_routes, jnp.arange(experts_mlp, dtype=jnp.int32), slot_count)
    dest_tokens = jnp.repeat(mlp_tokens, split_count, axis=0)
    send_m = normed_mlp[dest_tokens.reshape(-1)].reshape(device_count, slot_count, model_width)
    inputs = lax.all_to_all(send_m, "exp", 0, 0, tiled=True).reshape(-1, model_width)
    slice_out = expert_mlp(inputs, w_gate, w_up, w_down)
    recv_m = lax.all_to_all(
        slice_out.reshape(device_count, slot_count, model_width), "exp", 0, 0, tiled=True
    )
    mlp_own = combine(
        recv_m, own_mlp_routes, mlp_gates, route_slots(own_mlp_routes, experts_mlp), split_count
    )
    layer_out = (middle.astype(jnp.float32) + mlp_own).astype(jnp.bfloat16)
    return (layer_out[None], cache_next[None])


def base_body(
    tokens,
    cache,
    cache_len,
    attn_routes,
    mlp_routes,
    norm_attn,
    attn_router,
    w_query,
    w_keyval,
    w_out,
    norm_mlp,
    mlp_router,
    w_gate,
    w_up,
    w_down,
):
    device_count = lax.axis_size("exp")
    position = lax.axis_index("exp")
    own_rows = tokens[0]
    rows_block = own_rows.shape[0]
    model_width = own_rows.shape[1]
    length = cache_len[0]
    slot_count = MOST
    normed = rms_norm(own_rows, norm_attn)
    group_normed, group_routes = (
        lax.all_gather(normed, "exp", axis=0, tiled=True),
        lax.all_gather(attn_routes[0], "exp", axis=0, tiled=True),
    )
    row_total = group_normed.shape[0]
    block_count = row_total // rows_block
    heads_here = w_query.shape[0]
    head_dim = w_query.shape[2]
    columns = w_keyval.shape[1]
    experts_attn = attn_router.shape[1]
    my_attn = jnp.reshape(position % experts_attn, (1,))
    new_pos = length + jnp.arange(row_total, dtype=jnp.int32)
    fresh_kv = jnp.dot(group_normed, w_keyval, preferred_element_type=jnp.float32)
    if columns < 2 * head_dim:
        is_key = position % 2 == 0
        fresh_kv = jnp.where(is_key, rotate(fresh_kv, new_pos), fresh_kv).astype(jnp.bfloat16)
    else:
        split_new = fresh_kv.reshape(row_total, columns // (2 * head_dim), 2, head_dim)
        rotated = rotate(split_new[:, :, 0], new_pos[:, None])
        fresh_kv = (
            jnp.stack([rotated, split_new[:, :, 1]], axis=2)
            .astype(jnp.bfloat16)
            .reshape(row_total, columns)
        )
    cache_limit = cache.shape[1]
    padded = jnp.concatenate([cache[0], jnp.zeros((row_total, columns), jnp.bfloat16)], axis=0)
    placed = lax.dynamic_update_slice(jnp.zeros_like(padded), fresh_kv, (length, jnp.int32(0)))
    slot_ids = jnp.arange(cache_limit + row_total, dtype=jnp.int32)
    cache_next = jnp.where((slot_ids < length)[:, None], padded, placed)
    group_cache = cache[0]
    group_fresh = fresh_kv
    for bit in range(experts_attn.bit_length() - 1):
        other_cache, other_fresh = from_partner((group_cache, group_fresh), "exp", bit)
        lower = position // (1 << bit) % 2 == 0
        group_cache = jnp.where(
            lower,
            jnp.concatenate([group_cache, other_cache], axis=1),
            jnp.concatenate([other_cache, group_cache], axis=1),
        )
        group_fresh = jnp.where(
            lower,
            jnp.concatenate([group_fresh, other_fresh], axis=1),
            jnp.concatenate([other_fresh, group_fresh], axis=1),
        )
    split_old = group_cache.reshape(cache_limit, heads_here, 2, head_dim)
    split_fresh = group_fresh.reshape(row_total, heads_here, 2, head_dim)
    attn_gates = pick_gates(group_normed, attn_router, group_routes)
    attn_tokens, attn_shares = slot_tables(
        group_routes, attn_gates, my_attn, rows_block, slot_count
    )
    token_flat = attn_tokens[:, 0, :].reshape(-1)
    share_flat = attn_shares[:, 0, :].reshape(-1)
    picked_rows = group_normed[token_flat]
    queries = jnp.einsum("sd,hdk->hsk", picked_rows, w_query, preferred_element_type=jnp.float32)
    queries = rotate(queries, (length + token_flat)[None, :]).astype(jnp.bfloat16)
    attend_heads = jax.vmap(attend, in_axes=(0, None, 1, 1, 1, 1, None))
    head_outs = attend_heads(
        queries,
        token_flat,
        split_old[:, :, 0],
        split_old[:, :, 1],
        split_fresh[:, :, 0],
        split_fresh[:, :, 1],
        length,
    )
    projected = jnp.einsum("hsk,hkd->sd", head_outs, w_out, preferred_element_type=jnp.float32)
    projected = (projected * share_flat[:, None]).reshape(block_count, slot_count, model_width)
    attn_ids = attn_tokens[:, 0, :]
    attn_own = lax.psum_scatter(
        spread_rows(projected, attn_ids, rows_block * lax.axis_size("exp")).astype(jnp.bfloat16),
        "exp",
        scatter_dimension=0,
        tiled=True,
    ).astype(jnp.float32)
    middle = lax.optimization_barrier(
        (own_rows.astype(jnp.float32) + attn_own).astype(jnp.bfloat16)
    )
    normed_mlp = rms_norm(middle, norm_mlp)
    experts_mlp = mlp_router.shape[1]
    split_count = device_count // experts_mlp
    my_expert = jnp.reshape(position // split_count, (1,))
    all_normed, all_routes = (
        lax.all_gather(normed_mlp, "exp", axis=0, tiled=True),
        lax.all_gather(mlp_routes[0], "exp", axis=0, tiled=True),
    )
    all_gates = pick_gates(all_normed, mlp_router, all_routes)
    mlp_tokens, mlp_shares = slot_tables(all_routes, all_gates, my_expert, rows_block, slot_count)
    inputs = all_normed[mlp_tokens.reshape(-1)]
    gate_part = jnp.dot(inputs, w_gate[0], preferred_element_type=jnp.float32)
    up_part = jnp.dot(inputs, w_up[0], preferred_element_type=jnp.float32)
    hidden = (jax.nn.silu(gate_part) * up_part).astype(jnp.bfloat16)
    slice_out = lax.optimization_barrier(
        jnp.dot(hidden, w_down[0], preferred_element_type=jnp.float32).astype(jnp.bfloat16)
    )
    weighted = (slice_out.astype(jnp.float32) * mlp_shares.reshape(-1)[:, None]).reshape(
        block_count, slot_count, model_width
    )
    mlp_ids = mlp_tokens[:, 0, :]
    mlp_own = lax.psum_scatter(
        spread_rows(weighted, mlp_ids, rows_block * lax.axis_size("exp")).astype(jnp.bfloat16),
        "exp",
        scatter_dimension=0,
        tiled=True,
    ).astype(jnp.float32)
    layer_out = (middle.astype(jnp.float32) + mlp_own).astype(jnp.bfloat16)
    return (layer_out[None], cache_next[None])


def solution(mesh):
    placed = (
        P("req", "exp", None),
        P("req", None, "exp"),
        P("req"),
        P("req", "exp", None),
        P("req", "exp", None),
        P(),
        P(),
        P("exp", None, None),
        P(None, "exp"),
        P("exp", None, None),
        P(),
        P(),
        P("exp", None, None),
        P("exp", None, None),
        P("exp", None, None),
    )
    return jax.shard_map(
        body,
        mesh=mesh,
        in_specs=placed,
        out_specs=(P("req", "exp", None), P("req", None, "exp")),
        check_vma=False,
    )
```

```python
import functools
import math

import jax
import jax.numpy as jnp
from jax import lax
from jax.experimental import pallas as pl
from jax.experimental.pallas import tpu as pltpu
from jax.sharding import PartitionSpec as P

MOST = 24


epsilon = 1e-05
rope_base = 10000.0
masked_score = -1e30


def from_partner(value, axis, stride):
    mask = 2**stride
    pairs = [(source, source ^ mask) for source in range(lax.axis_size(axis))]
    return lax.ppermute(value, axis, pairs)


def rms_norm(values, gain_vec):
    widened = values.astype(jnp.float32)
    inv_rms = lax.rsqrt(jnp.mean(widened * widened, axis=-1, keepdims=True) + epsilon)
    return (widened * inv_rms * gain_vec).astype(jnp.bfloat16)


def rotate(values, position):
    half_dim = values.shape[-1] // 2
    inv_freq = rope_base ** (-jnp.arange(half_dim).astype(jnp.float32) / half_dim)
    angles = position.astype(jnp.float32)[..., None] * inv_freq
    cosine = jnp.cos(angles)
    sines = jnp.sin(angles)
    first_half = values[..., :half_dim]
    second_half = values[..., half_dim:]
    return jnp.concatenate(
        [first_half * cosine - second_half * sines, second_half * cosine + first_half * sines],
        axis=-1,
    )


def pick_gates(normed, router, routes):
    logits = jnp.dot(normed, router, preferred_element_type=jnp.float32)
    labels = jnp.arange(router.shape[1], dtype=jnp.int32)
    onehot = (routes[:, :, None] == labels[None, None, :]).astype(jnp.float32)
    chosen = jnp.sum(onehot * logits[:, None, :], axis=-1)
    return jax.nn.softmax(chosen, axis=-1)


def slot_tables(routes, gates, labels, rows_block, slot_count):
    row_total = routes.shape[0]
    block_count = row_total // rows_block
    matches = routes[:, :, None] == labels[None, None, :]
    member = jnp.any(matches, axis=1).astype(jnp.int32).reshape(block_count, rows_block, -1)
    weight = jnp.sum(jnp.where(matches, gates[:, :, None], 0.0), axis=1).reshape(
        block_count, rows_block, -1
    )
    ranking = jnp.cumsum(member, axis=1) - 1
    slot_ids = jnp.arange(slot_count, dtype=jnp.int32)
    onehot = ((member[..., None] > 0) & (ranking[..., None] == slot_ids)).astype(jnp.int32)
    local_row = jnp.arange(rows_block, dtype=jnp.int32)[None, :, None, None]
    token_ids = (
        jnp.sum(onehot * local_row, axis=1)
        + (jnp.arange(block_count, dtype=jnp.int32) * rows_block)[:, None, None]
    )
    shares = jnp.sum(onehot.astype(jnp.float32) * weight[..., None], axis=1)
    return (token_ids, shares)


def spread_rows(terms, token_ids, extent):
    term_part = terms.reshape(-1, terms.shape[-1])
    id_part = token_ids.reshape(-1)
    return jnp.zeros((extent, terms.shape[-1]), jnp.float32).at[id_part].add(term_part, mode="drop")


def attend(queries, query_pos, key_cache, value_cache, key_fresh, value_fresh, length):
    query_count = queries.shape[0]
    head_dim = queries.shape[1]
    factor = head_dim ** (-0.5)

    def absorb(state, key_block, value_block, visible):
        running_top, running_total, running_acc = state
        scores = jnp.dot(queries, key_block.T, preferred_element_type=jnp.float32) * factor
        scores = jnp.where(visible, scores, masked_score)
        new_top = jnp.maximum(running_top, jnp.max(scores, axis=1))
        fading = jnp.exp(running_top - new_top)
        weights = jnp.exp(scores - new_top[:, None])
        running_total = running_total * fading + jnp.sum(weights, axis=1)
        running_acc = running_acc * fading[:, None] + jnp.dot(
            weights.astype(jnp.bfloat16), value_block, preferred_element_type=jnp.float32
        )
        return (new_top, running_total, running_acc)

    state = (
        jnp.full((query_count,), masked_score, jnp.float32),
        jnp.zeros((query_count,), jnp.float32),
        jnp.zeros((query_count, head_dim), jnp.float32),
    )
    cache_span = math.gcd(512, key_cache.shape[0])

    def cache_step(step_idx, state):
        offset = step_idx * cache_span
        key_block = lax.dynamic_slice_in_dim(key_cache, offset, cache_span, 0)
        value_block = lax.dynamic_slice_in_dim(value_cache, offset, cache_span, 0)
        visible = (offset + jnp.arange(cache_span, dtype=jnp.int32))[None, :] < length
        return absorb(state, key_block, value_block, visible)

    state = lax.fori_loop(0, (length + cache_span - 1) // cache_span, cache_step, state)
    fresh_span = math.gcd(512, key_fresh.shape[0])
    for offset in range(0, key_fresh.shape[0], fresh_span):
        visible = (offset + jnp.arange(fresh_span, dtype=jnp.int32))[None, :] <= query_pos[:, None]
        state = absorb(
            state,
            key_fresh[offset : offset + fresh_span],
            value_fresh[offset : offset + fresh_span],
            visible,
        )
    running_top, running_total, running_acc = state
    return (running_acc / running_total[:, None]).astype(jnp.bfloat16)


def running_count(member):
    rows = member.shape[0]
    lower = (
        jnp.arange(rows, dtype=jnp.int32)[None, :] <= jnp.arange(rows, dtype=jnp.int32)[:, None]
    ).astype(jnp.bfloat16)
    counts = jnp.dot(lower, member.astype(jnp.bfloat16), preferred_element_type=jnp.float32)
    return counts.astype(jnp.int32)


def local_slots(routes, labels, slot_count):
    matches = routes[:, :, None] == labels[None, None, :]
    member = jnp.any(matches, axis=1).astype(jnp.int32)
    ranking = running_count(member) - 1
    slot_ids = jnp.arange(slot_count, dtype=jnp.int32)
    onehot = ((member[..., None] > 0) & (ranking[..., None] == slot_ids)).astype(jnp.int32)
    rows = jnp.arange(routes.shape[0], dtype=jnp.int32)[:, None, None]
    return jnp.sum(onehot * rows, axis=0)


def route_slots(routes, label_count):
    labels = jnp.arange(label_count, dtype=jnp.int32)
    member = jnp.any(routes[:, :, None] == labels[None, None, :], axis=1).astype(jnp.int32)
    ranking = running_count(member) - 1
    return jnp.take_along_axis(ranking, routes, axis=1)


def combine(received, routes, gates, slots, split_count):
    slot_count = received.shape[1]
    flat = received.reshape(-1, received.shape[-1])
    total = jnp.zeros((routes.shape[0], received.shape[-1]), jnp.float32)
    for route in range(routes.shape[1]):
        expert = routes[:, route]
        part = jnp.zeros_like(total)
        for piece in range(split_count):
            index = (expert * split_count + piece) * slot_count + slots[:, route]
            part = part + flat[index].astype(jnp.float32)
        total = total + part * gates[:, route][:, None]
    return total


def mlp_kernel(x_ref, gate_ref, up_ref, down_ref, out_ref, acc_ref):
    step = pl.program_id(0)

    @pl.when(step == 0)
    def _():
        acc_ref[...] = jnp.zeros_like(acc_ref)

    rows = x_ref[...]
    gate_part = jnp.dot(rows, gate_ref[...], preferred_element_type=jnp.float32)
    up_part = jnp.dot(rows, up_ref[...], preferred_element_type=jnp.float32)
    hidden = (gate_part / (1.0 + jnp.exp(-gate_part)) * up_part).astype(jnp.bfloat16)
    acc_ref[...] += jnp.dot(hidden, down_ref[...], preferred_element_type=jnp.float32)

    @pl.when(step == pl.num_programs(0) - 1)
    def _():
        out_ref[...] = acc_ref[...].astype(out_ref.dtype)


def expert_mlp(rows, w_gate, w_up, w_down):
    row_count, width = rows.shape
    hidden_units = w_gate.shape[-1]
    tile = next(t for t in (512, 256, 128) if hidden_units % t == 0)
    return pl.pallas_call(
        mlp_kernel,
        grid=(hidden_units // tile,),
        in_specs=[
            pl.BlockSpec((row_count, width), lambda k: (0, 0)),
            pl.BlockSpec((None, width, tile), lambda k: (0, 0, k)),
            pl.BlockSpec((None, width, tile), lambda k: (0, 0, k)),
            pl.BlockSpec((None, tile, width), lambda k: (0, k, 0)),
        ],
        out_specs=pl.BlockSpec((row_count, width), lambda k: (0, 0)),
        out_shape=jax.ShapeDtypeStruct((row_count, width), jnp.bfloat16),
        scratch_shapes=[pltpu.VMEM((row_count, width), jnp.float32)],
        compiler_params=pltpu.CompilerParams(dimension_semantics=("arbitrary",)),
    )(rows, w_gate, w_up, w_down)


def attention_kernel(length_ref, query_ref, pos_ref, key_ref, value_ref, out_ref, *, cache_limit):
    length = length_ref[0]
    queries = query_ref[...]
    factor = queries.shape[-1] ** (-0.5)
    scores = (
        lax.dot_general(
            queries, key_ref[...], (((1,), (1,)), ((), ())), preferred_element_type=jnp.float32
        )
        * factor
    )
    column = lax.broadcasted_iota(jnp.int32, scores.shape, 1)
    in_cache = column < cache_limit
    visible = (in_cache & (column < length)) | (
        jnp.logical_not(in_cache) & (column - cache_limit <= pos_ref[...])
    )
    scores = jnp.where(visible, scores, masked_score)
    top = jnp.max(scores, axis=1, keepdims=True)
    weights = jnp.exp(scores - top)
    total = jnp.sum(weights, axis=1, keepdims=True)
    summed = jnp.dot(weights.astype(jnp.bfloat16), value_ref[...], preferred_element_type=jnp.float32)
    out_ref[...] = (summed / total).astype(out_ref.dtype)


def kernel_attention(queries, query_pos, keys, values, length, cache_limit):
    head_count, query_count, head_dim = queries.shape
    key_count = keys.shape[1]
    tile = next(t for t in (256, 128, 64, 32, 16, 8) if query_count % t == 0)
    grid_spec = pltpu.PrefetchScalarGridSpec(
        num_scalar_prefetch=1,
        grid=(head_count, query_count // tile),
        in_specs=[
            pl.BlockSpec((None, tile, head_dim), lambda h, i, n: (h, i, 0)),
            pl.BlockSpec((tile, 1), lambda h, i, n: (i, 0)),
            pl.BlockSpec((None, key_count, head_dim), lambda h, i, n: (h, 0, 0)),
            pl.BlockSpec((None, key_count, head_dim), lambda h, i, n: (h, 0, 0)),
        ],
        out_specs=pl.BlockSpec((None, tile, head_dim), lambda h, i, n: (h, i, 0)),
    )
    return pl.pallas_call(
        functools.partial(attention_kernel, cache_limit=cache_limit),
        grid_spec=grid_spec,
        out_shape=jax.ShapeDtypeStruct(queries.shape, jnp.bfloat16),
        compiler_params=pltpu.CompilerParams(dimension_semantics=("arbitrary", "arbitrary")),
    )(jnp.reshape(length, (1,)).astype(jnp.int32), queries, query_pos.reshape(-1, 1), keys, values)


def head_attention(queries, query_pos, keys, values, length, cache_limit):
    factor = queries.shape[-1] ** (-0.5)
    scores = jnp.einsum("hqk,hsk->hqs", queries, keys, preferred_element_type=jnp.float32) * factor
    slot_ids = jnp.arange(keys.shape[1], dtype=jnp.int32)[None, :]
    visible = jnp.where(
        slot_ids < cache_limit, slot_ids < length, slot_ids - cache_limit <= query_pos[:, None]
    )
    scores = jnp.where(visible[None], scores, masked_score)
    top = jnp.max(scores, axis=-1, keepdims=True)
    weights = jnp.exp(scores - top)
    total = jnp.sum(weights, axis=-1, keepdims=True)
    summed = jnp.einsum(
        "hqs,hsk->hqk", weights.astype(jnp.bfloat16), values, preferred_element_type=jnp.float32
    )
    return (summed / total).astype(jnp.bfloat16)


def body(
    tokens,
    cache,
    cache_len,
    attn_routes,
    mlp_routes,
    norm_attn,
    attn_router,
    w_query,
    w_keyval,
    w_out,
    norm_mlp,
    mlp_router,
    w_gate,
    w_up,
    w_down,
):
    device_count = lax.axis_size("exp")
    position = lax.axis_index("exp")
    own_rows = tokens[0]
    rows_block = own_rows.shape[0]
    model_width = own_rows.shape[1]
    length = cache_len[0]
    slot_count = MOST
    heads_here = w_query.shape[0]
    head_dim = w_query.shape[2]
    columns = w_keyval.shape[1]
    experts_attn = attn_router.shape[1]
    kv_heads = columns * device_count // (2 * head_dim)
    fast_attn = (
        device_count == experts_attn and heads_here == kv_heads and columns % (2 * head_dim) == 0
    )
    if not fast_attn:
        return base_body(
            tokens, cache, cache_len, attn_routes, mlp_routes, norm_attn, attn_router, w_query,
            w_keyval, w_out, norm_mlp, mlp_router, w_gate, w_up, w_down,
        )
    normed = rms_norm(own_rows, norm_attn)
    route_rows = jnp.zeros((16, model_width), jnp.bfloat16)
    route_rows = route_rows.at[0, : 2 * rows_block].set(
        attn_routes[0].reshape(-1).astype(jnp.bfloat16)
    )
    gathered = lax.all_gather(
        jnp.concatenate([normed, route_rows], axis=0), "exp", axis=0, tiled=False
    )
    group_normed = gathered[:, :rows_block].reshape(-1, model_width)
    group_routes = (
        gathered[:, rows_block, : 2 * rows_block].astype(jnp.int32).reshape(-1, 2)
    )
    row_total = group_normed.shape[0]
    block_count = row_total // rows_block
    new_pos = length + jnp.arange(row_total, dtype=jnp.int32)
    fresh_kv = jnp.dot(group_normed, w_keyval, preferred_element_type=jnp.float32)
    split_new = fresh_kv.reshape(row_total, columns // (2 * head_dim), 2, head_dim)
    rotated = rotate(split_new[:, :, 0], new_pos[:, None])
    fresh_kv = (
        jnp.stack([rotated, split_new[:, :, 1]], axis=2)
        .astype(jnp.bfloat16)
        .reshape(row_total, columns)
    )
    cache_limit = cache.shape[1]
    padded = jnp.concatenate([cache[0], jnp.zeros((row_total, columns), jnp.bfloat16)], axis=0)
    placed = lax.dynamic_update_slice(jnp.zeros_like(padded), fresh_kv, (length, jnp.int32(0)))
    slot_ids = jnp.arange(cache_limit + row_total, dtype=jnp.int32)
    cache_next = jnp.where((slot_ids < length)[:, None], padded, placed)

    all_labels = jnp.arange(experts_attn, dtype=jnp.int32)
    blocks_routes = group_routes.reshape(block_count, rows_block, -1)
    slot_tokens = jax.vmap(lambda r: local_slots(r, all_labels, slot_count))(blocks_routes)
    slot_tokens = slot_tokens + (jnp.arange(block_count, dtype=jnp.int32) * rows_block)[:, None, None]
    expert_tokens = jnp.swapaxes(slot_tokens, 0, 1).reshape(experts_attn, -1)
    my_tokens = expert_tokens[position]
    picked_rows = group_normed[my_tokens]
    queries = jnp.einsum("sd,hdk->hsk", picked_rows, w_query, preferred_element_type=jnp.float32)
    queries = rotate(queries, (length + my_tokens)[None, :]).astype(jnp.bfloat16)
    heads_local = columns // (2 * head_dim)
    query_slots = queries.shape[1]
    send_q = queries.reshape(device_count, heads_local, query_slots, head_dim)
    recv_q = lax.all_to_all(send_q, "exp", 0, 0, tiled=True)
    recv_q = jnp.swapaxes(recv_q, 0, 1).reshape(heads_local, device_count * query_slots, head_dim)
    query_pos = expert_tokens.reshape(-1)
    split_old = cache[0].reshape(cache_limit, heads_local, 2, head_dim)
    split_fresh = fresh_kv.reshape(row_total, heads_local, 2, head_dim)
    keys = jnp.swapaxes(jnp.concatenate([split_old[:, :, 0], split_fresh[:, :, 0]], axis=0), 0, 1)
    values = jnp.swapaxes(jnp.concatenate([split_old[:, :, 1], split_fresh[:, :, 1]], axis=0), 0, 1)
    head_outs = kernel_attention(recv_q, query_pos, keys, values, length, cache_limit)
    send_o = jnp.swapaxes(
        head_outs.reshape(heads_local, device_count, query_slots, head_dim), 0, 1
    )
    recv_o = lax.all_to_all(send_o, "exp", 0, 0, tiled=True)
    recv_o = recv_o.reshape(heads_here, query_slots, head_dim)
    projected = jnp.einsum("hsk,hkd->sd", recv_o, w_out, preferred_element_type=jnp.float32)
    send_p = projected.astype(jnp.bfloat16).reshape(block_count, slot_count, model_width)
    recv_p = lax.all_to_all(send_p, "exp", 0, 0, tiled=True)
    own_attn_routes = attn_routes[0]
    attn_gates = pick_gates(normed, attn_router, own_attn_routes)
    attn_own = combine(
        recv_p, own_attn_routes, attn_gates, route_slots(own_attn_routes, experts_attn), 1
    )
    middle = (own_rows.astype(jnp.float32) + attn_own).astype(jnp.bfloat16)
    normed_mlp = rms_norm(middle, norm_mlp)
    experts_mlp = mlp_router.shape[1]
    split_count = device_count // experts_mlp
    own_mlp_routes = mlp_routes[0]
    mlp_gates = pick_gates(normed_mlp, mlp_router, own_mlp_routes)
    mlp_tokens = local_slots(own_mlp_routes, jnp.arange(experts_mlp, dtype=jnp.int32), slot_count)
    dest_tokens = jnp.repeat(mlp_tokens, split_count, axis=0)
    send_m = normed_mlp[dest_tokens.reshape(-1)].reshape(device_count, slot_count, model_width)
    inputs = lax.all_to_all(send_m, "exp", 0, 0, tiled=True).reshape(-1, model_width)
    slice_out = expert_mlp(inputs, w_gate, w_up, w_down)
    recv_m = lax.all_to_all(
        slice_out.reshape(device_count, slot_count, model_width), "exp", 0, 0, tiled=True
    )
    mlp_own = combine(
        recv_m, own_mlp_routes, mlp_gates, route_slots(own_mlp_routes, experts_mlp), split_count
    )
    layer_out = (middle.astype(jnp.float32) + mlp_own).astype(jnp.bfloat16)
    return (layer_out[None], cache_next[None])


def base_body(
    tokens,
    cache,
    cache_len,
    attn_routes,
    mlp_routes,
    norm_attn,
    attn_router,
    w_query,
    w_keyval,
    w_out,
    norm_mlp,
    mlp_router,
    w_gate,
    w_up,
    w_down,
):
    device_count = lax.axis_size("exp")
    position = lax.axis_index("exp")
    own_rows = tokens[0]
    rows_block = own_rows.shape[0]
    model_width = own_rows.shape[1]
    length = cache_len[0]
    slot_count = MOST
    normed = rms_norm(own_rows, norm_attn)
    group_normed, group_routes = (
        lax.all_gather(normed, "exp", axis=0, tiled=True),
        lax.all_gather(attn_routes[0], "exp", axis=0, tiled=True),
    )
    row_total = group_normed.shape[0]
    block_count = row_total // rows_block
    heads_here = w_query.shape[0]
    head_dim = w_query.shape[2]
    columns = w_keyval.shape[1]
    experts_attn = attn_router.shape[1]
    my_attn = jnp.reshape(position % experts_attn, (1,))
    new_pos = length + jnp.arange(row_total, dtype=jnp.int32)
    fresh_kv = jnp.dot(group_normed, w_keyval, preferred_element_type=jnp.float32)
    if columns < 2 * head_dim:
        is_key = position % 2 == 0
        fresh_kv = jnp.where(is_key, rotate(fresh_kv, new_pos), fresh_kv).astype(jnp.bfloat16)
    else:
        split_new = fresh_kv.reshape(row_total, columns // (2 * head_dim), 2, head_dim)
        rotated = rotate(split_new[:, :, 0], new_pos[:, None])
        fresh_kv = (
            jnp.stack([rotated, split_new[:, :, 1]], axis=2)
            .astype(jnp.bfloat16)
            .reshape(row_total, columns)
        )
    cache_limit = cache.shape[1]
    padded = jnp.concatenate([cache[0], jnp.zeros((row_total, columns), jnp.bfloat16)], axis=0)
    placed = lax.dynamic_update_slice(jnp.zeros_like(padded), fresh_kv, (length, jnp.int32(0)))
    slot_ids = jnp.arange(cache_limit + row_total, dtype=jnp.int32)
    cache_next = jnp.where((slot_ids < length)[:, None], padded, placed)
    group_cache = cache[0]
    group_fresh = fresh_kv
    for bit in range(experts_attn.bit_length() - 1):
        other_cache, other_fresh = from_partner((group_cache, group_fresh), "exp", bit)
        lower = position // (1 << bit) % 2 == 0
        group_cache = jnp.where(
            lower,
            jnp.concatenate([group_cache, other_cache], axis=1),
            jnp.concatenate([other_cache, group_cache], axis=1),
        )
        group_fresh = jnp.where(
            lower,
            jnp.concatenate([group_fresh, other_fresh], axis=1),
            jnp.concatenate([other_fresh, group_fresh], axis=1),
        )
    split_old = group_cache.reshape(cache_limit, heads_here, 2, head_dim)
    split_fresh = group_fresh.reshape(row_total, heads_here, 2, head_dim)
    attn_gates = pick_gates(group_normed, attn_router, group_routes)
    attn_tokens, attn_shares = slot_tables(
        group_routes, attn_gates, my_attn, rows_block, slot_count
    )
    token_flat = attn_tokens[:, 0, :].reshape(-1)
    share_flat = attn_shares[:, 0, :].reshape(-1)
    picked_rows = group_normed[token_flat]
    queries = jnp.einsum("sd,hdk->hsk", picked_rows, w_query, preferred_element_type=jnp.float32)
    queries = rotate(queries, (length + token_flat)[None, :]).astype(jnp.bfloat16)
    attend_heads = jax.vmap(attend, in_axes=(0, None, 1, 1, 1, 1, None))
    head_outs = attend_heads(
        queries,
        token_flat,
        split_old[:, :, 0],
        split_old[:, :, 1],
        split_fresh[:, :, 0],
        split_fresh[:, :, 1],
        length,
    )
    projected = jnp.einsum("hsk,hkd->sd", head_outs, w_out, preferred_element_type=jnp.float32)
    projected = (projected * share_flat[:, None]).reshape(block_count, slot_count, model_width)
    attn_ids = attn_tokens[:, 0, :]
    attn_own = lax.psum_scatter(
        spread_rows(projected, attn_ids, rows_block * lax.axis_size("exp")).astype(jnp.bfloat16),
        "exp",
        scatter_dimension=0,
        tiled=True,
    ).astype(jnp.float32)
    middle = lax.optimization_barrier(
        (own_rows.astype(jnp.float32) + attn_own).astype(jnp.bfloat16)
    )
    normed_mlp = rms_norm(middle, norm_mlp)
    experts_mlp = mlp_router.shape[1]
    split_count = device_count // experts_mlp
    my_expert = jnp.reshape(position // split_count, (1,))
    all_normed, all_routes = (
        lax.all_gather(normed_mlp, "exp", axis=0, tiled=True),
        lax.all_gather(mlp_routes[0], "exp", axis=0, tiled=True),
    )
    all_gates = pick_gates(all_normed, mlp_router, all_routes)
    mlp_tokens, mlp_shares = slot_tables(all_routes, all_gates, my_expert, rows_block, slot_count)
    inputs = all_normed[mlp_tokens.reshape(-1)]
    gate_part = jnp.dot(inputs, w_gate[0], preferred_element_type=jnp.float32)
    up_part = jnp.dot(inputs, w_up[0], preferred_element_type=jnp.float32)
    hidden = (jax.nn.silu(gate_part) * up_part).astype(jnp.bfloat16)
    slice_out = lax.optimization_barrier(
        jnp.dot(hidden, w_down[0], preferred_element_type=jnp.float32).astype(jnp.bfloat16)
    )
    weighted = (slice_out.astype(jnp.float32) * mlp_shares.reshape(-1)[:, None]).reshape(
        block_count, slot_count, model_width
    )
    mlp_ids = mlp_tokens[:, 0, :]
    mlp_own = lax.psum_scatter(
        spread_rows(weighted, mlp_ids, rows_block * lax.axis_size("exp")).astype(jnp.bfloat16),
        "exp",
        scatter_dimension=0,
        tiled=True,
    ).astype(jnp.float32)
    layer_out = (middle.astype(jnp.float32) + mlp_own).astype(jnp.bfloat16)
    return (layer_out[None], cache_next[None])


def solution(mesh):
    placed = (
        P("req", "exp", None),
        P("req", None, "exp"),
        P("req"),
        P("req", "exp", None),
        P("req", "exp", None),
        P(),
        P(),
        P("exp", None, None),
        P(None, "exp"),
        P("exp", None, None),
        P(),
        P(),
        P("exp", None, None),
        P("exp", None, None),
        P("exp", None, None),
    )
    return jax.shard_map(
        body,
        mesh=mesh,
        in_specs=placed,
        out_specs=(P("req", "exp", None), P("req", None, "exp")),
        check_vma=False,
    )
```

```python
import functools
import math

import jax
import jax.numpy as jnp
from jax import lax
from jax.experimental import pallas as pl
from jax.experimental.pallas import tpu as pltpu
from jax.sharding import PartitionSpec as P

MOST = 24


epsilon = 1e-05
rope_base = 10000.0
masked_score = -1e30


def from_partner(value, axis, stride):
    mask = 2**stride
    pairs = [(source, source ^ mask) for source in range(lax.axis_size(axis))]
    return lax.ppermute(value, axis, pairs)


def rms_norm(values, gain_vec):
    widened = values.astype(jnp.float32)
    inv_rms = lax.rsqrt(jnp.mean(widened * widened, axis=-1, keepdims=True) + epsilon)
    return (widened * inv_rms * gain_vec).astype(jnp.bfloat16)


def rotate(values, position):
    half_dim = values.shape[-1] // 2
    inv_freq = rope_base ** (-jnp.arange(half_dim).astype(jnp.float32) / half_dim)
    angles = position.astype(jnp.float32)[..., None] * inv_freq
    cosine = jnp.cos(angles)
    sines = jnp.sin(angles)
    first_half = values[..., :half_dim]
    second_half = values[..., half_dim:]
    return jnp.concatenate(
        [first_half * cosine - second_half * sines, second_half * cosine + first_half * sines],
        axis=-1,
    )


def pick_gates(normed, router, routes):
    logits = jnp.dot(normed, router, preferred_element_type=jnp.float32)
    labels = jnp.arange(router.shape[1], dtype=jnp.int32)
    onehot = (routes[:, :, None] == labels[None, None, :]).astype(jnp.float32)
    chosen = jnp.sum(onehot * logits[:, None, :], axis=-1)
    return jax.nn.softmax(chosen, axis=-1)


def slot_tables(routes, gates, labels, rows_block, slot_count):
    row_total = routes.shape[0]
    block_count = row_total // rows_block
    matches = routes[:, :, None] == labels[None, None, :]
    member = jnp.any(matches, axis=1).astype(jnp.int32).reshape(block_count, rows_block, -1)
    weight = jnp.sum(jnp.where(matches, gates[:, :, None], 0.0), axis=1).reshape(
        block_count, rows_block, -1
    )
    ranking = jnp.cumsum(member, axis=1) - 1
    slot_ids = jnp.arange(slot_count, dtype=jnp.int32)
    onehot = ((member[..., None] > 0) & (ranking[..., None] == slot_ids)).astype(jnp.int32)
    local_row = jnp.arange(rows_block, dtype=jnp.int32)[None, :, None, None]
    token_ids = (
        jnp.sum(onehot * local_row, axis=1)
        + (jnp.arange(block_count, dtype=jnp.int32) * rows_block)[:, None, None]
    )
    shares = jnp.sum(onehot.astype(jnp.float32) * weight[..., None], axis=1)
    return (token_ids, shares)


def spread_rows(terms, token_ids, extent):
    term_part = terms.reshape(-1, terms.shape[-1])
    id_part = token_ids.reshape(-1)
    return jnp.zeros((extent, terms.shape[-1]), jnp.float32).at[id_part].add(term_part, mode="drop")


def attend(queries, query_pos, key_cache, value_cache, key_fresh, value_fresh, length):
    query_count = queries.shape[0]
    head_dim = queries.shape[1]
    factor = head_dim ** (-0.5)

    def absorb(state, key_block, value_block, visible):
        running_top, running_total, running_acc = state
        scores = jnp.dot(queries, key_block.T, preferred_element_type=jnp.float32) * factor
        scores = jnp.where(visible, scores, masked_score)
        new_top = jnp.maximum(running_top, jnp.max(scores, axis=1))
        fading = jnp.exp(running_top - new_top)
        weights = jnp.exp(scores - new_top[:, None])
        running_total = running_total * fading + jnp.sum(weights, axis=1)
        running_acc = running_acc * fading[:, None] + jnp.dot(
            weights.astype(jnp.bfloat16), value_block, preferred_element_type=jnp.float32
        )
        return (new_top, running_total, running_acc)

    state = (
        jnp.full((query_count,), masked_score, jnp.float32),
        jnp.zeros((query_count,), jnp.float32),
        jnp.zeros((query_count, head_dim), jnp.float32),
    )
    cache_span = math.gcd(512, key_cache.shape[0])

    def cache_step(step_idx, state):
        offset = step_idx * cache_span
        key_block = lax.dynamic_slice_in_dim(key_cache, offset, cache_span, 0)
        value_block = lax.dynamic_slice_in_dim(value_cache, offset, cache_span, 0)
        visible = (offset + jnp.arange(cache_span, dtype=jnp.int32))[None, :] < length
        return absorb(state, key_block, value_block, visible)

    state = lax.fori_loop(0, (length + cache_span - 1) // cache_span, cache_step, state)
    fresh_span = math.gcd(512, key_fresh.shape[0])
    for offset in range(0, key_fresh.shape[0], fresh_span):
        visible = (offset + jnp.arange(fresh_span, dtype=jnp.int32))[None, :] <= query_pos[:, None]
        state = absorb(
            state,
            key_fresh[offset : offset + fresh_span],
            value_fresh[offset : offset + fresh_span],
            visible,
        )
    running_top, running_total, running_acc = state
    return (running_acc / running_total[:, None]).astype(jnp.bfloat16)


def running_count(member):
    rows = member.shape[0]
    lower = (
        jnp.arange(rows, dtype=jnp.int32)[None, :] <= jnp.arange(rows, dtype=jnp.int32)[:, None]
    ).astype(jnp.bfloat16)
    counts = jnp.dot(lower, member.astype(jnp.bfloat16), preferred_element_type=jnp.float32)
    return counts.astype(jnp.int32)


def local_slots(routes, labels, slot_count):
    matches = routes[:, :, None] == labels[None, None, :]
    member = jnp.any(matches, axis=1).astype(jnp.int32)
    ranking = running_count(member) - 1
    slot_ids = jnp.arange(slot_count, dtype=jnp.int32)
    onehot = ((member[..., None] > 0) & (ranking[..., None] == slot_ids)).astype(jnp.int32)
    rows = jnp.arange(routes.shape[0], dtype=jnp.int32)[:, None, None]
    return jnp.sum(onehot * rows, axis=0)


def route_slots(routes, label_count):
    labels = jnp.arange(label_count, dtype=jnp.int32)
    member = jnp.any(routes[:, :, None] == labels[None, None, :], axis=1).astype(jnp.int32)
    ranking = running_count(member) - 1
    return jnp.take_along_axis(ranking, routes, axis=1)


def combine(received, routes, gates, slots, split_count):
    slot_count = received.shape[1]
    flat = received.reshape(-1, received.shape[-1])
    total = jnp.zeros((routes.shape[0], received.shape[-1]), jnp.float32)
    for route in range(routes.shape[1]):
        expert = routes[:, route]
        part = jnp.zeros_like(total)
        for piece in range(split_count):
            index = (expert * split_count + piece) * slot_count + slots[:, route]
            part = part + flat[index].astype(jnp.float32)
        total = total + part * gates[:, route][:, None]
    return total


def mlp_kernel(x_ref, gate_ref, up_ref, down_ref, out_ref, acc_ref):
    step = pl.program_id(0)

    @pl.when(step == 0)
    def _():
        acc_ref[...] = jnp.zeros_like(acc_ref)

    rows = x_ref[...]
    gate_part = jnp.dot(rows, gate_ref[...], preferred_element_type=jnp.float32)
    up_part = jnp.dot(rows, up_ref[...], preferred_element_type=jnp.float32)
    hidden = (gate_part / (1.0 + jnp.exp(-gate_part)) * up_part).astype(jnp.bfloat16)
    acc_ref[...] += jnp.dot(hidden, down_ref[...], preferred_element_type=jnp.float32)

    @pl.when(step == pl.num_programs(0) - 1)
    def _():
        out_ref[...] = acc_ref[...].astype(out_ref.dtype)


def expert_mlp(rows, w_gate, w_up, w_down):
    row_count, width = rows.shape
    hidden_units = w_gate.shape[-1]
    tile = next(t for t in (512, 256, 128) if hidden_units % t == 0)
    return pl.pallas_call(
        mlp_kernel,
        grid=(hidden_units // tile,),
        in_specs=[
            pl.BlockSpec((row_count, width), lambda k: (0, 0)),
            pl.BlockSpec((None, width, tile), lambda k: (0, 0, k)),
            pl.BlockSpec((None, width, tile), lambda k: (0, 0, k)),
            pl.BlockSpec((None, tile, width), lambda k: (0, k, 0)),
        ],
        out_specs=pl.BlockSpec((row_count, width), lambda k: (0, 0)),
        out_shape=jax.ShapeDtypeStruct((row_count, width), jnp.bfloat16),
        scratch_shapes=[pltpu.VMEM((row_count, width), jnp.float32)],
        compiler_params=pltpu.CompilerParams(dimension_semantics=("arbitrary",)),
    )(rows, w_gate, w_up, w_down)


def attention_kernel(
    length_ref, query_ref, pos_ref, cache_key_ref, cache_value_ref, fresh_key_ref,
    fresh_value_ref, out_ref,
):
    length = length_ref[0]
    queries = query_ref[...]
    factor = queries.shape[-1] ** (-0.5)
    contract = (((1,), (1,)), ((), ()))
    cache_scores = (
        lax.dot_general(queries, cache_key_ref[...], contract, preferred_element_type=jnp.float32)
        * factor
    )
    fresh_scores = (
        lax.dot_general(queries, fresh_key_ref[...], contract, preferred_element_type=jnp.float32)
        * factor
    )
    cache_column = lax.broadcasted_iota(jnp.int32, cache_scores.shape, 1)
    fresh_column = lax.broadcasted_iota(jnp.int32, fresh_scores.shape, 1)
    cache_scores = jnp.where(cache_column < length, cache_scores, masked_score)
    fresh_scores = jnp.where(fresh_column <= pos_ref[...], fresh_scores, masked_score)
    top = jnp.maximum(
        jnp.max(cache_scores, axis=1, keepdims=True), jnp.max(fresh_scores, axis=1, keepdims=True)
    )
    cache_weights = jnp.exp(cache_scores - top)
    fresh_weights = jnp.exp(fresh_scores - top)
    total = jnp.sum(cache_weights, axis=1, keepdims=True) + jnp.sum(
        fresh_weights, axis=1, keepdims=True
    )
    summed = jnp.dot(
        cache_weights.astype(jnp.bfloat16), cache_value_ref[...], preferred_element_type=jnp.float32
    ) + jnp.dot(
        fresh_weights.astype(jnp.bfloat16), fresh_value_ref[...], preferred_element_type=jnp.float32
    )
    out_ref[...] = (summed / total).astype(out_ref.dtype)


def kernel_attention(queries, query_pos, cache, fresh, length):
    expert_count, head_count, slot_count, head_dim = queries.shape
    cache_rows = cache.shape[0]
    fresh_rows = fresh.shape[0]
    grid_spec = pltpu.PrefetchScalarGridSpec(
        num_scalar_prefetch=1,
        grid=(head_count, expert_count),
        in_specs=[
            pl.BlockSpec((None, None, slot_count, head_dim), lambda h, a, n: (a, h, 0, 0)),
            pl.BlockSpec((None, slot_count, 1), lambda h, a, n: (a, 0, 0)),
            pl.BlockSpec((cache_rows, head_dim), lambda h, a, n: (0, 2 * h)),
            pl.BlockSpec((cache_rows, head_dim), lambda h, a, n: (0, 2 * h + 1)),
            pl.BlockSpec((fresh_rows, head_dim), lambda h, a, n: (0, 2 * h)),
            pl.BlockSpec((fresh_rows, head_dim), lambda h, a, n: (0, 2 * h + 1)),
        ],
        out_specs=pl.BlockSpec((None, None, slot_count, head_dim), lambda h, a, n: (a, h, 0, 0)),
    )
    return pl.pallas_call(
        attention_kernel,
        grid_spec=grid_spec,
        out_shape=jax.ShapeDtypeStruct(queries.shape, jnp.bfloat16),
        compiler_params=pltpu.CompilerParams(dimension_semantics=("arbitrary", "arbitrary")),
    )(
        jnp.reshape(length, (1,)).astype(jnp.int32),
        queries,
        query_pos.reshape(expert_count, slot_count, 1),
        cache,
        cache,
        fresh,
        fresh,
    )


def head_attention(queries, query_pos, keys, values, length, cache_limit):
    factor = queries.shape[-1] ** (-0.5)
    scores = jnp.einsum("hqk,hsk->hqs", queries, keys, preferred_element_type=jnp.float32) * factor
    slot_ids = jnp.arange(keys.shape[1], dtype=jnp.int32)[None, :]
    visible = jnp.where(
        slot_ids < cache_limit, slot_ids < length, slot_ids - cache_limit <= query_pos[:, None]
    )
    scores = jnp.where(visible[None], scores, masked_score)
    top = jnp.max(scores, axis=-1, keepdims=True)
    weights = jnp.exp(scores - top)
    total = jnp.sum(weights, axis=-1, keepdims=True)
    summed = jnp.einsum(
        "hqs,hsk->hqk", weights.astype(jnp.bfloat16), values, preferred_element_type=jnp.float32
    )
    return (summed / total).astype(jnp.bfloat16)


def body(
    tokens,
    cache,
    cache_len,
    attn_routes,
    mlp_routes,
    norm_attn,
    attn_router,
    w_query,
    w_keyval,
    w_out,
    norm_mlp,
    mlp_router,
    w_gate,
    w_up,
    w_down,
):
    device_count = lax.axis_size("exp")
    position = lax.axis_index("exp")
    own_rows = tokens[0]
    rows_block = own_rows.shape[0]
    model_width = own_rows.shape[1]
    length = cache_len[0]
    slot_count = MOST
    heads_here = w_query.shape[0]
    head_dim = w_query.shape[2]
    columns = w_keyval.shape[1]
    experts_attn = attn_router.shape[1]
    kv_heads = columns * device_count // (2 * head_dim)
    fast_attn = (
        device_count == experts_attn and heads_here == kv_heads and columns % (2 * head_dim) == 0
    )
    if not fast_attn:
        return base_body(
            tokens, cache, cache_len, attn_routes, mlp_routes, norm_attn, attn_router, w_query,
            w_keyval, w_out, norm_mlp, mlp_router, w_gate, w_up, w_down,
        )
    normed = rms_norm(own_rows, norm_attn)
    route_rows = jnp.zeros((16, model_width), jnp.bfloat16)
    route_rows = route_rows.at[0, : 2 * rows_block].set(
        attn_routes[0].reshape(-1).astype(jnp.bfloat16)
    )
    gathered = lax.all_gather(
        jnp.concatenate([normed, route_rows], axis=0), "exp", axis=0, tiled=False
    )
    stride = gathered.shape[1]
    gathered_flat = gathered.reshape(-1, model_width)
    group_routes = (
        gathered[:, rows_block, : 2 * rows_block].astype(jnp.int32).reshape(-1, 2)
    )
    block_count = gathered.shape[0]
    row_total = block_count * rows_block
    new_pos = length + jnp.arange(row_total, dtype=jnp.int32)
    fresh_kv = jnp.dot(gathered_flat, w_keyval, preferred_element_type=jnp.float32)
    fresh_kv = fresh_kv.reshape(block_count, stride, columns)[:, :rows_block].reshape(row_total, columns)
    split_new = fresh_kv.reshape(row_total, columns // (2 * head_dim), 2, head_dim)
    rotated = rotate(split_new[:, :, 0], new_pos[:, None])
    fresh_kv = (
        jnp.stack([rotated, split_new[:, :, 1]], axis=2)
        .astype(jnp.bfloat16)
        .reshape(row_total, columns)
    )
    cache_limit = cache.shape[1]
    padded = jnp.concatenate([cache[0], jnp.zeros((row_total, columns), jnp.bfloat16)], axis=0)
    placed = lax.dynamic_update_slice(jnp.zeros_like(padded), fresh_kv, (length, jnp.int32(0)))
    slot_ids = jnp.arange(cache_limit + row_total, dtype=jnp.int32)
    cache_next = jnp.where((slot_ids < length)[:, None], padded, placed)

    all_labels = jnp.arange(experts_attn, dtype=jnp.int32)
    blocks_routes = group_routes.reshape(block_count, rows_block, -1)
    slot_tokens = jax.vmap(lambda r: local_slots(r, all_labels, slot_count))(blocks_routes)
    slot_tokens = slot_tokens + (jnp.arange(block_count, dtype=jnp.int32) * rows_block)[:, None, None]
    expert_tokens = jnp.swapaxes(slot_tokens, 0, 1).reshape(experts_attn, -1)
    my_tokens = expert_tokens[position]
    picked_rows = gathered_flat[my_tokens // rows_block * stride + my_tokens % rows_block]
    queries = jnp.einsum("sd,hdk->hsk", picked_rows, w_query, preferred_element_type=jnp.float32)
    queries = rotate(queries, (length + my_tokens)[None, :]).astype(jnp.bfloat16)
    heads_local = columns // (2 * head_dim)
    query_slots = queries.shape[1]
    send_q = queries.reshape(device_count, heads_local, query_slots, head_dim)
    recv_q = lax.all_to_all(send_q, "exp", 0, 0, tiled=True)
    send_o = kernel_attention(recv_q, expert_tokens, cache[0], fresh_kv, length)
    recv_o = lax.all_to_all(send_o, "exp", 0, 0, tiled=True)
    recv_o = recv_o.reshape(heads_here, query_slots, head_dim)
    projected = jnp.einsum("hsk,hkd->sd", recv_o, w_out, preferred_element_type=jnp.float32)
    send_p = projected.astype(jnp.bfloat16).reshape(block_count, slot_count, model_width)
    recv_p = lax.all_to_all(send_p, "exp", 0, 0, tiled=True)
    own_attn_routes = attn_routes[0]
    attn_gates = pick_gates(normed, attn_router, own_attn_routes)
    attn_own = combine(
        recv_p, own_attn_routes, attn_gates, route_slots(own_attn_routes, experts_attn), 1
    )
    middle = (own_rows.astype(jnp.float32) + attn_own).astype(jnp.bfloat16)
    normed_mlp = rms_norm(middle, norm_mlp)
    experts_mlp = mlp_router.shape[1]
    split_count = device_count // experts_mlp
    own_mlp_routes = mlp_routes[0]
    mlp_gates = pick_gates(normed_mlp, mlp_router, own_mlp_routes)
    mlp_tokens = local_slots(own_mlp_routes, jnp.arange(experts_mlp, dtype=jnp.int32), slot_count)
    dest_tokens = jnp.repeat(mlp_tokens, split_count, axis=0)
    send_m = normed_mlp[dest_tokens.reshape(-1)].reshape(device_count, slot_count, model_width)
    inputs = lax.all_to_all(send_m, "exp", 0, 0, tiled=True).reshape(-1, model_width)
    slice_out = expert_mlp(inputs, w_gate, w_up, w_down)
    recv_m = lax.all_to_all(
        slice_out.reshape(device_count, slot_count, model_width), "exp", 0, 0, tiled=True
    )
    mlp_own = combine(
        recv_m, own_mlp_routes, mlp_gates, route_slots(own_mlp_routes, experts_mlp), split_count
    )
    layer_out = (middle.astype(jnp.float32) + mlp_own).astype(jnp.bfloat16)
    return (layer_out[None], cache_next[None])


def base_body(
    tokens,
    cache,
    cache_len,
    attn_routes,
    mlp_routes,
    norm_attn,
    attn_router,
    w_query,
    w_keyval,
    w_out,
    norm_mlp,
    mlp_router,
    w_gate,
    w_up,
    w_down,
):
    device_count = lax.axis_size("exp")
    position = lax.axis_index("exp")
    own_rows = tokens[0]
    rows_block = own_rows.shape[0]
    model_width = own_rows.shape[1]
    length = cache_len[0]
    slot_count = MOST
    normed = rms_norm(own_rows, norm_attn)
    group_normed, group_routes = (
        lax.all_gather(normed, "exp", axis=0, tiled=True),
        lax.all_gather(attn_routes[0], "exp", axis=0, tiled=True),
    )
    row_total = group_normed.shape[0]
    block_count = row_total // rows_block
    heads_here = w_query.shape[0]
    head_dim = w_query.shape[2]
    columns = w_keyval.shape[1]
    experts_attn = attn_router.shape[1]
    my_attn = jnp.reshape(position % experts_attn, (1,))
    new_pos = length + jnp.arange(row_total, dtype=jnp.int32)
    fresh_kv = jnp.dot(group_normed, w_keyval, preferred_element_type=jnp.float32)
    if columns < 2 * head_dim:
        is_key = position % 2 == 0
        fresh_kv = jnp.where(is_key, rotate(fresh_kv, new_pos), fresh_kv).astype(jnp.bfloat16)
    else:
        split_new = fresh_kv.reshape(row_total, columns // (2 * head_dim), 2, head_dim)
        rotated = rotate(split_new[:, :, 0], new_pos[:, None])
        fresh_kv = (
            jnp.stack([rotated, split_new[:, :, 1]], axis=2)
            .astype(jnp.bfloat16)
            .reshape(row_total, columns)
        )
    cache_limit = cache.shape[1]
    padded = jnp.concatenate([cache[0], jnp.zeros((row_total, columns), jnp.bfloat16)], axis=0)
    placed = lax.dynamic_update_slice(jnp.zeros_like(padded), fresh_kv, (length, jnp.int32(0)))
    slot_ids = jnp.arange(cache_limit + row_total, dtype=jnp.int32)
    cache_next = jnp.where((slot_ids < length)[:, None], padded, placed)
    group_cache = cache[0]
    group_fresh = fresh_kv
    for bit in range(experts_attn.bit_length() - 1):
        other_cache, other_fresh = from_partner((group_cache, group_fresh), "exp", bit)
        lower = position // (1 << bit) % 2 == 0
        group_cache = jnp.where(
            lower,
            jnp.concatenate([group_cache, other_cache], axis=1),
            jnp.concatenate([other_cache, group_cache], axis=1),
        )
        group_fresh = jnp.where(
            lower,
            jnp.concatenate([group_fresh, other_fresh], axis=1),
            jnp.concatenate([other_fresh, group_fresh], axis=1),
        )
    split_old = group_cache.reshape(cache_limit, heads_here, 2, head_dim)
    split_fresh = group_fresh.reshape(row_total, heads_here, 2, head_dim)
    attn_gates = pick_gates(group_normed, attn_router, group_routes)
    attn_tokens, attn_shares = slot_tables(
        group_routes, attn_gates, my_attn, rows_block, slot_count
    )
    token_flat = attn_tokens[:, 0, :].reshape(-1)
    share_flat = attn_shares[:, 0, :].reshape(-1)
    picked_rows = group_normed[token_flat]
    queries = jnp.einsum("sd,hdk->hsk", picked_rows, w_query, preferred_element_type=jnp.float32)
    queries = rotate(queries, (length + token_flat)[None, :]).astype(jnp.bfloat16)
    attend_heads = jax.vmap(attend, in_axes=(0, None, 1, 1, 1, 1, None))
    head_outs = attend_heads(
        queries,
        token_flat,
        split_old[:, :, 0],
        split_old[:, :, 1],
        split_fresh[:, :, 0],
        split_fresh[:, :, 1],
        length,
    )
    projected = jnp.einsum("hsk,hkd->sd", head_outs, w_out, preferred_element_type=jnp.float32)
    projected = (projected * share_flat[:, None]).reshape(block_count, slot_count, model_width)
    attn_ids = attn_tokens[:, 0, :]
    attn_own = lax.psum_scatter(
        spread_rows(projected, attn_ids, rows_block * lax.axis_size("exp")).astype(jnp.bfloat16),
        "exp",
        scatter_dimension=0,
        tiled=True,
    ).astype(jnp.float32)
    middle = lax.optimization_barrier(
        (own_rows.astype(jnp.float32) + attn_own).astype(jnp.bfloat16)
    )
    normed_mlp = rms_norm(middle, norm_mlp)
    experts_mlp = mlp_router.shape[1]
    split_count = device_count // experts_mlp
    my_expert = jnp.reshape(position // split_count, (1,))
    all_normed, all_routes = (
        lax.all_gather(normed_mlp, "exp", axis=0, tiled=True),
        lax.all_gather(mlp_routes[0], "exp", axis=0, tiled=True),
    )
    all_gates = pick_gates(all_normed, mlp_router, all_routes)
    mlp_tokens, mlp_shares = slot_tables(all_routes, all_gates, my_expert, rows_block, slot_count)
    inputs = all_normed[mlp_tokens.reshape(-1)]
    gate_part = jnp.dot(inputs, w_gate[0], preferred_element_type=jnp.float32)
    up_part = jnp.dot(inputs, w_up[0], preferred_element_type=jnp.float32)
    hidden = (jax.nn.silu(gate_part) * up_part).astype(jnp.bfloat16)
    slice_out = lax.optimization_barrier(
        jnp.dot(hidden, w_down[0], preferred_element_type=jnp.float32).astype(jnp.bfloat16)
    )
    weighted = (slice_out.astype(jnp.float32) * mlp_shares.reshape(-1)[:, None]).reshape(
        block_count, slot_count, model_width
    )
    mlp_ids = mlp_tokens[:, 0, :]
    mlp_own = lax.psum_scatter(
        spread_rows(weighted, mlp_ids, rows_block * lax.axis_size("exp")).astype(jnp.bfloat16),
        "exp",
        scatter_dimension=0,
        tiled=True,
    ).astype(jnp.float32)
    layer_out = (middle.astype(jnp.float32) + mlp_own).astype(jnp.bfloat16)
    return (layer_out[None], cache_next[None])


def solution(mesh):
    placed = (
        P("req", "exp", None),
        P("req", None, "exp"),
        P("req"),
        P("req", "exp", None),
        P("req", "exp", None),
        P(),
        P(),
        P("exp", None, None),
        P(None, "exp"),
        P("exp", None, None),
        P(),
        P(),
        P("exp", None, None),
        P("exp", None, None),
        P("exp", None, None),
    )
    return jax.shard_map(
        body,
        mesh=mesh,
        in_specs=placed,
        out_specs=(P("req", "exp", None), P("req", None, "exp")),
        check_vma=False,
    )
```

```python
import functools
import math

import jax
import jax.numpy as jnp
from jax import lax
from jax.experimental import pallas as pl
from jax.experimental.pallas import tpu as pltpu
from jax.sharding import PartitionSpec as P

MOST = 24


epsilon = 1e-05
rope_base = 10000.0
masked_score = -1e30


def from_partner(value, axis, stride):
    mask = 2**stride
    pairs = [(source, source ^ mask) for source in range(lax.axis_size(axis))]
    return lax.ppermute(value, axis, pairs)


def rms_norm(values, gain_vec):
    widened = values.astype(jnp.float32)
    inv_rms = lax.rsqrt(jnp.mean(widened * widened, axis=-1, keepdims=True) + epsilon)
    return (widened * inv_rms * gain_vec).astype(jnp.bfloat16)


def rotate(values, position):
    half_dim = values.shape[-1] // 2
    inv_freq = rope_base ** (-jnp.arange(half_dim).astype(jnp.float32) / half_dim)
    angles = position.astype(jnp.float32)[..., None] * inv_freq
    cosine = jnp.cos(angles)
    sines = jnp.sin(angles)
    first_half = values[..., :half_dim]
    second_half = values[..., half_dim:]
    return jnp.concatenate(
        [first_half * cosine - second_half * sines, second_half * cosine + first_half * sines],
        axis=-1,
    )


def pick_gates(normed, router, routes):
    logits = jnp.dot(normed, router, preferred_element_type=jnp.float32)
    labels = jnp.arange(router.shape[1], dtype=jnp.int32)
    onehot = (routes[:, :, None] == labels[None, None, :]).astype(jnp.float32)
    chosen = jnp.sum(onehot * logits[:, None, :], axis=-1)
    return jax.nn.softmax(chosen, axis=-1)


def slot_tables(routes, gates, labels, rows_block, slot_count):
    row_total = routes.shape[0]
    block_count = row_total // rows_block
    matches = routes[:, :, None] == labels[None, None, :]
    member = jnp.any(matches, axis=1).astype(jnp.int32).reshape(block_count, rows_block, -1)
    weight = jnp.sum(jnp.where(matches, gates[:, :, None], 0.0), axis=1).reshape(
        block_count, rows_block, -1
    )
    ranking = jnp.cumsum(member, axis=1) - 1
    slot_ids = jnp.arange(slot_count, dtype=jnp.int32)
    onehot = ((member[..., None] > 0) & (ranking[..., None] == slot_ids)).astype(jnp.int32)
    local_row = jnp.arange(rows_block, dtype=jnp.int32)[None, :, None, None]
    token_ids = (
        jnp.sum(onehot * local_row, axis=1)
        + (jnp.arange(block_count, dtype=jnp.int32) * rows_block)[:, None, None]
    )
    shares = jnp.sum(onehot.astype(jnp.float32) * weight[..., None], axis=1)
    return (token_ids, shares)


def spread_rows(terms, token_ids, extent):
    term_part = terms.reshape(-1, terms.shape[-1])
    id_part = token_ids.reshape(-1)
    return jnp.zeros((extent, terms.shape[-1]), jnp.float32).at[id_part].add(term_part, mode="drop")


def attend(queries, query_pos, key_cache, value_cache, key_fresh, value_fresh, length):
    query_count = queries.shape[0]
    head_dim = queries.shape[1]
    factor = head_dim ** (-0.5)

    def absorb(state, key_block, value_block, visible):
        running_top, running_total, running_acc = state
        scores = jnp.dot(queries, key_block.T, preferred_element_type=jnp.float32) * factor
        scores = jnp.where(visible, scores, masked_score)
        new_top = jnp.maximum(running_top, jnp.max(scores, axis=1))
        fading = jnp.exp(running_top - new_top)
        weights = jnp.exp(scores - new_top[:, None])
        running_total = running_total * fading + jnp.sum(weights, axis=1)
        running_acc = running_acc * fading[:, None] + jnp.dot(
            weights.astype(jnp.bfloat16), value_block, preferred_element_type=jnp.float32
        )
        return (new_top, running_total, running_acc)

    state = (
        jnp.full((query_count,), masked_score, jnp.float32),
        jnp.zeros((query_count,), jnp.float32),
        jnp.zeros((query_count, head_dim), jnp.float32),
    )
    cache_span = math.gcd(512, key_cache.shape[0])

    def cache_step(step_idx, state):
        offset = step_idx * cache_span
        key_block = lax.dynamic_slice_in_dim(key_cache, offset, cache_span, 0)
        value_block = lax.dynamic_slice_in_dim(value_cache, offset, cache_span, 0)
        visible = (offset + jnp.arange(cache_span, dtype=jnp.int32))[None, :] < length
        return absorb(state, key_block, value_block, visible)

    state = lax.fori_loop(0, (length + cache_span - 1) // cache_span, cache_step, state)
    fresh_span = math.gcd(512, key_fresh.shape[0])
    for offset in range(0, key_fresh.shape[0], fresh_span):
        visible = (offset + jnp.arange(fresh_span, dtype=jnp.int32))[None, :] <= query_pos[:, None]
        state = absorb(
            state,
            key_fresh[offset : offset + fresh_span],
            value_fresh[offset : offset + fresh_span],
            visible,
        )
    running_top, running_total, running_acc = state
    return (running_acc / running_total[:, None]).astype(jnp.bfloat16)


def running_count(member):
    rows = member.shape[0]
    lower = (
        jnp.arange(rows, dtype=jnp.int32)[None, :] <= jnp.arange(rows, dtype=jnp.int32)[:, None]
    ).astype(jnp.bfloat16)
    counts = jnp.dot(lower, member.astype(jnp.bfloat16), preferred_element_type=jnp.float32)
    return counts.astype(jnp.int32)


def local_slots(routes, labels, slot_count):
    matches = routes[:, :, None] == labels[None, None, :]
    member = jnp.any(matches, axis=1).astype(jnp.int32)
    ranking = running_count(member) - 1
    slot_ids = jnp.arange(slot_count, dtype=jnp.int32)
    onehot = ((member[..., None] > 0) & (ranking[..., None] == slot_ids)).astype(jnp.int32)
    rows = jnp.arange(routes.shape[0], dtype=jnp.int32)[:, None, None]
    return jnp.sum(onehot * rows, axis=0)


def route_slots(routes, label_count):
    labels = jnp.arange(label_count, dtype=jnp.int32)
    member = jnp.any(routes[:, :, None] == labels[None, None, :], axis=1).astype(jnp.int32)
    ranking = running_count(member) - 1
    return jnp.take_along_axis(ranking, routes, axis=1)


def select_rows(index, source):
    onehot = (index[:, None] == jnp.arange(source.shape[0], dtype=jnp.int32)[None, :]).astype(
        source.dtype
    )
    return jnp.dot(onehot, source, preferred_element_type=jnp.float32)


def combine(received, routes, gates, slots, split_count):
    slot_count = received.shape[1]
    flat = received.reshape(-1, received.shape[-1])
    total = jnp.zeros((routes.shape[0], received.shape[-1]), jnp.float32)
    for route in range(routes.shape[1]):
        expert = routes[:, route]
        part = jnp.zeros_like(total)
        for piece in range(split_count):
            index = (expert * split_count + piece) * slot_count + slots[:, route]
            part = part + lax.optimization_barrier(select_rows(index, flat))
        total = total + part * gates[:, route][:, None]
    return total


def mlp_kernel(x_ref, gate_ref, up_ref, down_ref, out_ref, acc_ref):
    step = pl.program_id(0)

    @pl.when(step == 0)
    def _():
        acc_ref[...] = jnp.zeros_like(acc_ref)

    rows = x_ref[...]
    gate_part = jnp.dot(rows, gate_ref[...], preferred_element_type=jnp.float32)
    up_part = jnp.dot(rows, up_ref[...], preferred_element_type=jnp.float32)
    hidden = (gate_part / (1.0 + jnp.exp(-gate_part)) * up_part).astype(jnp.bfloat16)
    acc_ref[...] += jnp.dot(hidden, down_ref[...], preferred_element_type=jnp.float32)

    @pl.when(step == pl.num_programs(0) - 1)
    def _():
        out_ref[...] = acc_ref[...].astype(out_ref.dtype)


def expert_mlp(rows, w_gate, w_up, w_down):
    row_count, width = rows.shape
    hidden_units = w_gate.shape[-1]
    tile = next(t for t in (1408, 512, 256, 128) if hidden_units % t == 0)
    return pl.pallas_call(
        mlp_kernel,
        grid=(hidden_units // tile,),
        in_specs=[
            pl.BlockSpec((row_count, width), lambda k: (0, 0)),
            pl.BlockSpec((None, width, tile), lambda k: (0, 0, k)),
            pl.BlockSpec((None, width, tile), lambda k: (0, 0, k)),
            pl.BlockSpec((None, tile, width), lambda k: (0, k, 0)),
        ],
        out_specs=pl.BlockSpec((row_count, width), lambda k: (0, 0)),
        out_shape=jax.ShapeDtypeStruct((row_count, width), jnp.bfloat16),
        scratch_shapes=[pltpu.VMEM((row_count, width), jnp.float32)],
        compiler_params=pltpu.CompilerParams(dimension_semantics=("arbitrary",)),
    )(rows, w_gate, w_up, w_down)


def attention_kernel(length_ref, query_ref, pos_ref, key_ref, value_ref, out_ref, *, cache_limit):
    length = length_ref[0]
    queries = query_ref[...]
    factor = queries.shape[-1] ** (-0.5)
    scores = (
        lax.dot_general(
            queries, key_ref[...], (((1,), (1,)), ((), ())), preferred_element_type=jnp.float32
        )
        * factor
    )
    column = lax.broadcasted_iota(jnp.int32, scores.shape, 1)
    in_cache = column < cache_limit
    visible = (in_cache & (column < length)) | (
        jnp.logical_not(in_cache) & (column - cache_limit <= pos_ref[...])
    )
    scores = jnp.where(visible, scores, masked_score)
    top = jnp.max(scores, axis=1, keepdims=True)
    weights = jnp.exp(scores - top)
    total = jnp.sum(weights, axis=1, keepdims=True)
    summed = jnp.dot(weights.astype(jnp.bfloat16), value_ref[...], preferred_element_type=jnp.float32)
    out_ref[...] = (summed / total).astype(out_ref.dtype)


def kernel_attention(queries, query_pos, keys, values, length, cache_limit):
    expert_count, head_count, slot_count, head_dim = queries.shape
    key_count = keys.shape[1]
    grid_spec = pltpu.PrefetchScalarGridSpec(
        num_scalar_prefetch=1,
        grid=(head_count, expert_count),
        in_specs=[
            pl.BlockSpec((None, None, slot_count, head_dim), lambda h, a, n: (a, h, 0, 0)),
            pl.BlockSpec((None, slot_count, 1), lambda h, a, n: (a, 0, 0)),
            pl.BlockSpec((None, key_count, head_dim), lambda h, a, n: (h, 0, 0)),
            pl.BlockSpec((None, key_count, head_dim), lambda h, a, n: (h, 0, 0)),
        ],
        out_specs=pl.BlockSpec((None, None, slot_count, head_dim), lambda h, a, n: (a, h, 0, 0)),
    )
    return pl.pallas_call(
        functools.partial(attention_kernel, cache_limit=cache_limit),
        grid_spec=grid_spec,
        out_shape=jax.ShapeDtypeStruct(queries.shape, jnp.bfloat16),
        compiler_params=pltpu.CompilerParams(dimension_semantics=("arbitrary", "arbitrary")),
    )(
        jnp.reshape(length, (1,)).astype(jnp.int32),
        queries,
        query_pos.reshape(expert_count, slot_count, 1),
        keys,
        values,
    )


def head_attention(queries, query_pos, keys, values, length, cache_limit):
    factor = queries.shape[-1] ** (-0.5)
    scores = jnp.einsum("hqk,hsk->hqs", queries, keys, preferred_element_type=jnp.float32) * factor
    slot_ids = jnp.arange(keys.shape[1], dtype=jnp.int32)[None, :]
    visible = jnp.where(
        slot_ids < cache_limit, slot_ids < length, slot_ids - cache_limit <= query_pos[:, None]
    )
    scores = jnp.where(visible[None], scores, masked_score)
    top = jnp.max(scores, axis=-1, keepdims=True)
    weights = jnp.exp(scores - top)
    total = jnp.sum(weights, axis=-1, keepdims=True)
    summed = jnp.einsum(
        "hqs,hsk->hqk", weights.astype(jnp.bfloat16), values, preferred_element_type=jnp.float32
    )
    return (summed / total).astype(jnp.bfloat16)


def body(
    tokens,
    cache,
    cache_len,
    attn_routes,
    mlp_routes,
    norm_attn,
    attn_router,
    w_query,
    w_keyval,
    w_out,
    norm_mlp,
    mlp_router,
    w_gate,
    w_up,
    w_down,
):
    device_count = lax.axis_size("exp")
    position = lax.axis_index("exp")
    own_rows = tokens[0]
    rows_block = own_rows.shape[0]
    model_width = own_rows.shape[1]
    length = cache_len[0]
    slot_count = MOST
    heads_here = w_query.shape[0]
    head_dim = w_query.shape[2]
    columns = w_keyval.shape[1]
    experts_attn = attn_router.shape[1]
    kv_heads = columns * device_count // (2 * head_dim)
    fast_attn = (
        device_count == experts_attn and heads_here == kv_heads and columns % (2 * head_dim) == 0
    )
    if not fast_attn:
        return base_body(
            tokens, cache, cache_len, attn_routes, mlp_routes, norm_attn, attn_router, w_query,
            w_keyval, w_out, norm_mlp, mlp_router, w_gate, w_up, w_down,
        )
    normed = rms_norm(own_rows, norm_attn)
    route_rows = jnp.zeros((16, 2 * rows_block), jnp.bfloat16)
    route_rows = route_rows.at[0].set(attn_routes[0].reshape(-1).astype(jnp.bfloat16))
    group_normed = lax.all_gather(normed, "exp", axis=0, tiled=True)
    gathered_routes = lax.all_gather(route_rows, "exp", axis=0, tiled=False)
    group_routes = gathered_routes[:, 0].astype(jnp.int32).reshape(-1, 2)
    row_total = group_normed.shape[0]
    block_count = row_total // rows_block
    new_pos = length + jnp.arange(row_total, dtype=jnp.int32)
    fresh_kv = jnp.dot(group_normed, w_keyval, preferred_element_type=jnp.float32)
    split_new = fresh_kv.reshape(row_total, columns // (2 * head_dim), 2, head_dim)
    rotated = rotate(split_new[:, :, 0], new_pos[:, None])
    fresh_kv = (
        jnp.stack([rotated, split_new[:, :, 1]], axis=2)
        .astype(jnp.bfloat16)
        .reshape(row_total, columns)
    )
    cache_limit = cache.shape[1]
    padded = jnp.concatenate([cache[0], jnp.zeros((row_total, columns), jnp.bfloat16)], axis=0)
    placed = lax.dynamic_update_slice(jnp.zeros_like(padded), fresh_kv, (length, jnp.int32(0)))
    slot_ids = jnp.arange(cache_limit + row_total, dtype=jnp.int32)
    cache_next = jnp.where((slot_ids < length)[:, None], padded, placed)

    all_labels = jnp.arange(experts_attn, dtype=jnp.int32)
    blocks_routes = group_routes.reshape(block_count, rows_block, -1)
    slot_tokens = jax.vmap(lambda r: local_slots(r, all_labels, slot_count))(blocks_routes)
    slot_tokens = slot_tokens + (jnp.arange(block_count, dtype=jnp.int32) * rows_block)[:, None, None]
    expert_tokens = jnp.swapaxes(slot_tokens, 0, 1).reshape(experts_attn, -1)
    my_tokens = expert_tokens[position]
    picked_rows = select_rows(my_tokens, group_normed).astype(jnp.bfloat16)
    queries = jnp.einsum("sd,hdk->hsk", picked_rows, w_query, preferred_element_type=jnp.float32)
    queries = rotate(queries, (length + my_tokens)[None, :]).astype(jnp.bfloat16)
    heads_local = columns // (2 * head_dim)
    query_slots = queries.shape[1]
    send_q = queries.reshape(device_count, heads_local, query_slots, head_dim)
    recv_q = lax.all_to_all(send_q, "exp", 0, 0, tiled=True)
    split_old = cache[0].reshape(cache_limit, heads_local, 2, head_dim)
    split_fresh = fresh_kv.reshape(row_total, heads_local, 2, head_dim)
    keys = jnp.swapaxes(jnp.concatenate([split_old[:, :, 0], split_fresh[:, :, 0]], axis=0), 0, 1)
    values = jnp.swapaxes(jnp.concatenate([split_old[:, :, 1], split_fresh[:, :, 1]], axis=0), 0, 1)
    send_o = kernel_attention(recv_q, expert_tokens, keys, values, length, cache_limit)
    recv_o = lax.all_to_all(send_o, "exp", 0, 0, tiled=True)
    recv_o = recv_o.reshape(heads_here, query_slots, head_dim)
    projected = jnp.einsum("hsk,hkd->sd", recv_o, w_out, preferred_element_type=jnp.float32)
    send_p = projected.astype(jnp.bfloat16).reshape(block_count, slot_count, model_width)
    recv_p = lax.all_to_all(send_p, "exp", 0, 0, tiled=True)
    own_attn_routes = attn_routes[0]
    attn_gates = pick_gates(normed, attn_router, own_attn_routes)
    attn_own = combine(
        recv_p, own_attn_routes, attn_gates, route_slots(own_attn_routes, experts_attn), 1
    )
    middle = (own_rows.astype(jnp.float32) + attn_own).astype(jnp.bfloat16)
    normed_mlp = rms_norm(middle, norm_mlp)
    experts_mlp = mlp_router.shape[1]
    split_count = device_count // experts_mlp
    own_mlp_routes = mlp_routes[0]
    mlp_gates = pick_gates(normed_mlp, mlp_router, own_mlp_routes)
    mlp_tokens = local_slots(own_mlp_routes, jnp.arange(experts_mlp, dtype=jnp.int32), slot_count)
    dest_tokens = jnp.repeat(mlp_tokens, split_count, axis=0)
    send_m = (
        select_rows(dest_tokens.reshape(-1), normed_mlp)
        .astype(jnp.bfloat16)
        .reshape(device_count, slot_count, model_width)
    )
    inputs = lax.all_to_all(send_m, "exp", 0, 0, tiled=True).reshape(-1, model_width)
    slice_out = expert_mlp(inputs, w_gate, w_up, w_down)
    recv_m = lax.all_to_all(
        slice_out.reshape(device_count, slot_count, model_width), "exp", 0, 0, tiled=True
    )
    mlp_own = combine(
        recv_m, own_mlp_routes, mlp_gates, route_slots(own_mlp_routes, experts_mlp), split_count
    )
    layer_out = (middle.astype(jnp.float32) + mlp_own).astype(jnp.bfloat16)
    return (layer_out[None], cache_next[None])


def base_body(
    tokens,
    cache,
    cache_len,
    attn_routes,
    mlp_routes,
    norm_attn,
    attn_router,
    w_query,
    w_keyval,
    w_out,
    norm_mlp,
    mlp_router,
    w_gate,
    w_up,
    w_down,
):
    device_count = lax.axis_size("exp")
    position = lax.axis_index("exp")
    own_rows = tokens[0]
    rows_block = own_rows.shape[0]
    model_width = own_rows.shape[1]
    length = cache_len[0]
    slot_count = MOST
    normed = rms_norm(own_rows, norm_attn)
    group_normed, group_routes = (
        lax.all_gather(normed, "exp", axis=0, tiled=True),
        lax.all_gather(attn_routes[0], "exp", axis=0, tiled=True),
    )
    row_total = group_normed.shape[0]
    block_count = row_total // rows_block
    heads_here = w_query.shape[0]
    head_dim = w_query.shape[2]
    columns = w_keyval.shape[1]
    experts_attn = attn_router.shape[1]
    my_attn = jnp.reshape(position % experts_attn, (1,))
    new_pos = length + jnp.arange(row_total, dtype=jnp.int32)
    fresh_kv = jnp.dot(group_normed, w_keyval, preferred_element_type=jnp.float32)
    if columns < 2 * head_dim:
        is_key = position % 2 == 0
        fresh_kv = jnp.where(is_key, rotate(fresh_kv, new_pos), fresh_kv).astype(jnp.bfloat16)
    else:
        split_new = fresh_kv.reshape(row_total, columns // (2 * head_dim), 2, head_dim)
        rotated = rotate(split_new[:, :, 0], new_pos[:, None])
        fresh_kv = (
            jnp.stack([rotated, split_new[:, :, 1]], axis=2)
            .astype(jnp.bfloat16)
            .reshape(row_total, columns)
        )
    cache_limit = cache.shape[1]
    padded = jnp.concatenate([cache[0], jnp.zeros((row_total, columns), jnp.bfloat16)], axis=0)
    placed = lax.dynamic_update_slice(jnp.zeros_like(padded), fresh_kv, (length, jnp.int32(0)))
    slot_ids = jnp.arange(cache_limit + row_total, dtype=jnp.int32)
    cache_next = jnp.where((slot_ids < length)[:, None], padded, placed)
    group_cache = cache[0]
    group_fresh = fresh_kv
    for bit in range(experts_attn.bit_length() - 1):
        other_cache, other_fresh = from_partner((group_cache, group_fresh), "exp", bit)
        lower = position // (1 << bit) % 2 == 0
        group_cache = jnp.where(
            lower,
            jnp.concatenate([group_cache, other_cache], axis=1),
            jnp.concatenate([other_cache, group_cache], axis=1),
        )
        group_fresh = jnp.where(
            lower,
            jnp.concatenate([group_fresh, other_fresh], axis=1),
            jnp.concatenate([other_fresh, group_fresh], axis=1),
        )
    split_old = group_cache.reshape(cache_limit, heads_here, 2, head_dim)
    split_fresh = group_fresh.reshape(row_total, heads_here, 2, head_dim)
    attn_gates = pick_gates(group_normed, attn_router, group_routes)
    attn_tokens, attn_shares = slot_tables(
        group_routes, attn_gates, my_attn, rows_block, slot_count
    )
    token_flat = attn_tokens[:, 0, :].reshape(-1)
    share_flat = attn_shares[:, 0, :].reshape(-1)
    picked_rows = group_normed[token_flat]
    queries = jnp.einsum("sd,hdk->hsk", picked_rows, w_query, preferred_element_type=jnp.float32)
    queries = rotate(queries, (length + token_flat)[None, :]).astype(jnp.bfloat16)
    attend_heads = jax.vmap(attend, in_axes=(0, None, 1, 1, 1, 1, None))
    head_outs = attend_heads(
        queries,
        token_flat,
        split_old[:, :, 0],
        split_old[:, :, 1],
        split_fresh[:, :, 0],
        split_fresh[:, :, 1],
        length,
    )
    projected = jnp.einsum("hsk,hkd->sd", head_outs, w_out, preferred_element_type=jnp.float32)
    projected = (projected * share_flat[:, None]).reshape(block_count, slot_count, model_width)
    attn_ids = attn_tokens[:, 0, :]
    attn_own = lax.psum_scatter(
        spread_rows(projected, attn_ids, rows_block * lax.axis_size("exp")).astype(jnp.bfloat16),
        "exp",
        scatter_dimension=0,
        tiled=True,
    ).astype(jnp.float32)
    middle = lax.optimization_barrier(
        (own_rows.astype(jnp.float32) + attn_own).astype(jnp.bfloat16)
    )
    normed_mlp = rms_norm(middle, norm_mlp)
    experts_mlp = mlp_router.shape[1]
    split_count = device_count // experts_mlp
    my_expert = jnp.reshape(position // split_count, (1,))
    all_normed, all_routes = (
        lax.all_gather(normed_mlp, "exp", axis=0, tiled=True),
        lax.all_gather(mlp_routes[0], "exp", axis=0, tiled=True),
    )
    all_gates = pick_gates(all_normed, mlp_router, all_routes)
    mlp_tokens, mlp_shares = slot_tables(all_routes, all_gates, my_expert, rows_block, slot_count)
    inputs = all_normed[mlp_tokens.reshape(-1)]
    gate_part = jnp.dot(inputs, w_gate[0], preferred_element_type=jnp.float32)
    up_part = jnp.dot(inputs, w_up[0], preferred_element_type=jnp.float32)
    hidden = (jax.nn.silu(gate_part) * up_part).astype(jnp.bfloat16)
    slice_out = lax.optimization_barrier(
        jnp.dot(hidden, w_down[0], preferred_element_type=jnp.float32).astype(jnp.bfloat16)
    )
    weighted = (slice_out.astype(jnp.float32) * mlp_shares.reshape(-1)[:, None]).reshape(
        block_count, slot_count, model_width
    )
    mlp_ids = mlp_tokens[:, 0, :]
    mlp_own = lax.psum_scatter(
        spread_rows(weighted, mlp_ids, rows_block * lax.axis_size("exp")).astype(jnp.bfloat16),
        "exp",
        scatter_dimension=0,
        tiled=True,
    ).astype(jnp.float32)
    layer_out = (middle.astype(jnp.float32) + mlp_own).astype(jnp.bfloat16)
    return (layer_out[None], cache_next[None])


def solution(mesh):
    placed = (
        P("req", "exp", None),
        P("req", None, "exp"),
        P("req"),
        P("req", "exp", None),
        P("req", "exp", None),
        P(),
        P(),
        P("exp", None, None),
        P(None, "exp"),
        P("exp", None, None),
        P(),
        P(),
        P("exp", None, None),
        P("exp", None, None),
        P("exp", None, None),
    )
    return jax.shard_map(
        body,
        mesh=mesh,
        in_specs=placed,
        out_specs=(P("req", "exp", None), P("req", None, "exp")),
        check_vma=False,
    )
```

```python
import functools
import math

import jax
import jax.numpy as jnp
from jax import lax
from jax.experimental import pallas as pl
from jax.experimental.pallas import tpu as pltpu
from jax.sharding import PartitionSpec as P

MOST = 24


epsilon = 1e-05
rope_base = 10000.0
masked_score = -1e30


def from_partner(value, axis, stride):
    mask = 2**stride
    pairs = [(source, source ^ mask) for source in range(lax.axis_size(axis))]
    return lax.ppermute(value, axis, pairs)


def rms_norm(values, gain_vec):
    widened = values.astype(jnp.float32)
    inv_rms = lax.rsqrt(jnp.mean(widened * widened, axis=-1, keepdims=True) + epsilon)
    return (widened * inv_rms * gain_vec).astype(jnp.bfloat16)


def rotate(values, position):
    half_dim = values.shape[-1] // 2
    inv_freq = rope_base ** (-jnp.arange(half_dim).astype(jnp.float32) / half_dim)
    angles = position.astype(jnp.float32)[..., None] * inv_freq
    cosine = jnp.cos(angles)
    sines = jnp.sin(angles)
    first_half = values[..., :half_dim]
    second_half = values[..., half_dim:]
    return jnp.concatenate(
        [first_half * cosine - second_half * sines, second_half * cosine + first_half * sines],
        axis=-1,
    )


def pick_gates(normed, router, routes):
    logits = jnp.dot(normed, router, preferred_element_type=jnp.float32)
    labels = jnp.arange(router.shape[1], dtype=jnp.int32)
    onehot = (routes[:, :, None] == labels[None, None, :]).astype(jnp.float32)
    chosen = jnp.sum(onehot * logits[:, None, :], axis=-1)
    return jax.nn.softmax(chosen, axis=-1)


def slot_tables(routes, gates, labels, rows_block, slot_count):
    row_total = routes.shape[0]
    block_count = row_total // rows_block
    matches = routes[:, :, None] == labels[None, None, :]
    member = jnp.any(matches, axis=1).astype(jnp.int32).reshape(block_count, rows_block, -1)
    weight = jnp.sum(jnp.where(matches, gates[:, :, None], 0.0), axis=1).reshape(
        block_count, rows_block, -1
    )
    ranking = jnp.cumsum(member, axis=1) - 1
    slot_ids = jnp.arange(slot_count, dtype=jnp.int32)
    onehot = ((member[..., None] > 0) & (ranking[..., None] == slot_ids)).astype(jnp.int32)
    local_row = jnp.arange(rows_block, dtype=jnp.int32)[None, :, None, None]
    token_ids = (
        jnp.sum(onehot * local_row, axis=1)
        + (jnp.arange(block_count, dtype=jnp.int32) * rows_block)[:, None, None]
    )
    shares = jnp.sum(onehot.astype(jnp.float32) * weight[..., None], axis=1)
    return (token_ids, shares)


def spread_rows(terms, token_ids, extent):
    term_part = terms.reshape(-1, terms.shape[-1])
    id_part = token_ids.reshape(-1)
    return jnp.zeros((extent, terms.shape[-1]), jnp.float32).at[id_part].add(term_part, mode="drop")


def attend(queries, query_pos, key_cache, value_cache, key_fresh, value_fresh, length):
    query_count = queries.shape[0]
    head_dim = queries.shape[1]
    factor = head_dim ** (-0.5)

    def absorb(state, key_block, value_block, visible):
        running_top, running_total, running_acc = state
        scores = jnp.dot(queries, key_block.T, preferred_element_type=jnp.float32) * factor
        scores = jnp.where(visible, scores, masked_score)
        new_top = jnp.maximum(running_top, jnp.max(scores, axis=1))
        fading = jnp.exp(running_top - new_top)
        weights = jnp.exp(scores - new_top[:, None])
        running_total = running_total * fading + jnp.sum(weights, axis=1)
        running_acc = running_acc * fading[:, None] + jnp.dot(
            weights.astype(jnp.bfloat16), value_block, preferred_element_type=jnp.float32
        )
        return (new_top, running_total, running_acc)

    state = (
        jnp.full((query_count,), masked_score, jnp.float32),
        jnp.zeros((query_count,), jnp.float32),
        jnp.zeros((query_count, head_dim), jnp.float32),
    )
    cache_span = math.gcd(512, key_cache.shape[0])

    def cache_step(step_idx, state):
        offset = step_idx * cache_span
        key_block = lax.dynamic_slice_in_dim(key_cache, offset, cache_span, 0)
        value_block = lax.dynamic_slice_in_dim(value_cache, offset, cache_span, 0)
        visible = (offset + jnp.arange(cache_span, dtype=jnp.int32))[None, :] < length
        return absorb(state, key_block, value_block, visible)

    state = lax.fori_loop(0, (length + cache_span - 1) // cache_span, cache_step, state)
    fresh_span = math.gcd(512, key_fresh.shape[0])
    for offset in range(0, key_fresh.shape[0], fresh_span):
        visible = (offset + jnp.arange(fresh_span, dtype=jnp.int32))[None, :] <= query_pos[:, None]
        state = absorb(
            state,
            key_fresh[offset : offset + fresh_span],
            value_fresh[offset : offset + fresh_span],
            visible,
        )
    running_top, running_total, running_acc = state
    return (running_acc / running_total[:, None]).astype(jnp.bfloat16)


def running_count(member):
    rows = member.shape[0]
    lower = (
        jnp.arange(rows, dtype=jnp.int32)[None, :] <= jnp.arange(rows, dtype=jnp.int32)[:, None]
    ).astype(jnp.bfloat16)
    counts = jnp.dot(lower, member.astype(jnp.bfloat16), preferred_element_type=jnp.float32)
    return counts.astype(jnp.int32)


def local_slots(routes, labels, slot_count):
    matches = routes[:, :, None] == labels[None, None, :]
    member = jnp.any(matches, axis=1).astype(jnp.int32)
    ranking = running_count(member) - 1
    slot_ids = jnp.arange(slot_count, dtype=jnp.int32)
    onehot = ((member[..., None] > 0) & (ranking[..., None] == slot_ids)).astype(jnp.int32)
    rows = jnp.arange(routes.shape[0], dtype=jnp.int32)[:, None, None]
    return jnp.sum(onehot * rows, axis=0)


def route_slots(routes, label_count):
    labels = jnp.arange(label_count, dtype=jnp.int32)
    member = jnp.any(routes[:, :, None] == labels[None, None, :], axis=1).astype(jnp.int32)
    ranking = running_count(member) - 1
    return jnp.take_along_axis(ranking, routes, axis=1)


def select_rows(index, source):
    onehot = (index[:, None] == jnp.arange(source.shape[0], dtype=jnp.int32)[None, :]).astype(
        source.dtype
    )
    return jnp.dot(onehot, source, preferred_element_type=jnp.float32)


def combine(received, routes, gates, slots, split_count):
    slot_count = received.shape[1]
    flat = received.reshape(-1, received.shape[-1])
    total = jnp.zeros((routes.shape[0], received.shape[-1]), jnp.float32)
    for route in range(routes.shape[1]):
        expert = routes[:, route]
        part = jnp.zeros_like(total)
        for piece in range(split_count):
            index = (expert * split_count + piece) * slot_count + slots[:, route]
            part = part + lax.optimization_barrier(select_rows(index, flat))
        total = total + part * gates[:, route][:, None]
    return total


def mlp_kernel(x_ref, gate_ref, up_ref, down_ref, out_ref, acc_ref):
    step = pl.program_id(0)

    @pl.when(step == 0)
    def _():
        acc_ref[...] = jnp.zeros_like(acc_ref)

    rows = x_ref[...]
    gate_part = jnp.dot(rows, gate_ref[...], preferred_element_type=jnp.float32)
    up_part = jnp.dot(rows, up_ref[...], preferred_element_type=jnp.float32)
    hidden = (gate_part / (1.0 + jnp.exp(-gate_part)) * up_part).astype(jnp.bfloat16)
    acc_ref[...] += jnp.dot(hidden, down_ref[...], preferred_element_type=jnp.float32)

    @pl.when(step == pl.num_programs(0) - 1)
    def _():
        out_ref[...] = acc_ref[...].astype(out_ref.dtype)


def expert_mlp(rows, w_gate, w_up, w_down):
    row_count, width = rows.shape
    hidden_units = w_gate.shape[-1]
    tile = next(t for t in (1408, 512, 256, 128) if hidden_units % t == 0)
    return pl.pallas_call(
        mlp_kernel,
        grid=(hidden_units // tile,),
        in_specs=[
            pl.BlockSpec((row_count, width), lambda k: (0, 0)),
            pl.BlockSpec((None, width, tile), lambda k: (0, 0, k)),
            pl.BlockSpec((None, width, tile), lambda k: (0, 0, k)),
            pl.BlockSpec((None, tile, width), lambda k: (0, k, 0)),
        ],
        out_specs=pl.BlockSpec((row_count, width), lambda k: (0, 0)),
        out_shape=jax.ShapeDtypeStruct((row_count, width), jnp.bfloat16),
        scratch_shapes=[pltpu.VMEM((row_count, width), jnp.float32)],
        compiler_params=pltpu.CompilerParams(dimension_semantics=("arbitrary",)),
    )(rows, w_gate, w_up, w_down)


def attention_kernel(length_ref, query_ref, pos_ref, key_ref, value_ref, out_ref, *, cache_limit):
    length = length_ref[0]
    block_shape = query_ref.shape
    queries = query_ref[...].reshape(-1, block_shape[-1])
    query_pos = pos_ref[...].reshape(-1, 1)
    factor = queries.shape[-1] ** (-0.5)
    scores = (
        lax.dot_general(
            queries, key_ref[...], (((1,), (1,)), ((), ())), preferred_element_type=jnp.float32
        )
        * factor
    )
    column = lax.broadcasted_iota(jnp.int32, scores.shape, 1)
    in_cache = column < cache_limit
    visible = (in_cache & (column < length)) | (
        jnp.logical_not(in_cache) & (column - cache_limit <= query_pos)
    )
    scores = jnp.where(visible, scores, masked_score)
    top = jnp.max(scores, axis=1, keepdims=True)
    weights = jnp.exp(scores - top)
    total = jnp.sum(weights, axis=1, keepdims=True)
    summed = jnp.dot(weights.astype(jnp.bfloat16), value_ref[...], preferred_element_type=jnp.float32)
    out_ref[...] = (summed / total).astype(out_ref.dtype).reshape(block_shape)


def kernel_attention(queries, query_pos, keys, values, length, cache_limit):
    expert_count, head_count, slot_count, head_dim = queries.shape
    key_count = keys.shape[1]
    group = 2 if expert_count % 2 == 0 else 1
    grid_spec = pltpu.PrefetchScalarGridSpec(
        num_scalar_prefetch=1,
        grid=(head_count, expert_count // group),
        in_specs=[
            pl.BlockSpec((group, None, slot_count, head_dim), lambda h, a, n: (a, h, 0, 0)),
            pl.BlockSpec((group, slot_count, 1), lambda h, a, n: (a, 0, 0)),
            pl.BlockSpec((None, key_count, head_dim), lambda h, a, n: (h, 0, 0)),
            pl.BlockSpec((None, key_count, head_dim), lambda h, a, n: (h, 0, 0)),
        ],
        out_specs=pl.BlockSpec((group, None, slot_count, head_dim), lambda h, a, n: (a, h, 0, 0)),
    )
    return pl.pallas_call(
        functools.partial(attention_kernel, cache_limit=cache_limit),
        grid_spec=grid_spec,
        out_shape=jax.ShapeDtypeStruct(queries.shape, jnp.bfloat16),
        compiler_params=pltpu.CompilerParams(dimension_semantics=("arbitrary", "arbitrary")),
    )(
        jnp.reshape(length, (1,)).astype(jnp.int32),
        queries,
        query_pos.reshape(expert_count, slot_count, 1),
        keys,
        values,
    )


def head_attention(queries, query_pos, keys, values, length, cache_limit):
    factor = queries.shape[-1] ** (-0.5)
    scores = jnp.einsum("hqk,hsk->hqs", queries, keys, preferred_element_type=jnp.float32) * factor
    slot_ids = jnp.arange(keys.shape[1], dtype=jnp.int32)[None, :]
    visible = jnp.where(
        slot_ids < cache_limit, slot_ids < length, slot_ids - cache_limit <= query_pos[:, None]
    )
    scores = jnp.where(visible[None], scores, masked_score)
    top = jnp.max(scores, axis=-1, keepdims=True)
    weights = jnp.exp(scores - top)
    total = jnp.sum(weights, axis=-1, keepdims=True)
    summed = jnp.einsum(
        "hqs,hsk->hqk", weights.astype(jnp.bfloat16), values, preferred_element_type=jnp.float32
    )
    return (summed / total).astype(jnp.bfloat16)


def body(
    tokens,
    cache,
    cache_len,
    attn_routes,
    mlp_routes,
    norm_attn,
    attn_router,
    w_query,
    w_keyval,
    w_out,
    norm_mlp,
    mlp_router,
    w_gate,
    w_up,
    w_down,
):
    device_count = lax.axis_size("exp")
    position = lax.axis_index("exp")
    own_rows = tokens[0]
    rows_block = own_rows.shape[0]
    model_width = own_rows.shape[1]
    length = cache_len[0]
    slot_count = MOST
    heads_here = w_query.shape[0]
    head_dim = w_query.shape[2]
    columns = w_keyval.shape[1]
    experts_attn = attn_router.shape[1]
    kv_heads = columns * device_count // (2 * head_dim)
    fast_attn = (
        device_count == experts_attn and heads_here == kv_heads and columns % (2 * head_dim) == 0
    )
    if not fast_attn:
        return base_body(
            tokens, cache, cache_len, attn_routes, mlp_routes, norm_attn, attn_router, w_query,
            w_keyval, w_out, norm_mlp, mlp_router, w_gate, w_up, w_down,
        )
    normed = rms_norm(own_rows, norm_attn)
    route_rows = jnp.zeros((16, 2 * rows_block), jnp.bfloat16)
    route_rows = route_rows.at[0].set(attn_routes[0].reshape(-1).astype(jnp.bfloat16))
    group_normed = lax.all_gather(normed, "exp", axis=0, tiled=True)
    gathered_routes = lax.all_gather(route_rows, "exp", axis=0, tiled=False)
    group_routes = gathered_routes[:, 0].astype(jnp.int32).reshape(-1, 2)
    row_total = group_normed.shape[0]
    block_count = row_total // rows_block
    new_pos = length + jnp.arange(row_total, dtype=jnp.int32)
    fresh_kv = jnp.dot(group_normed, w_keyval, preferred_element_type=jnp.float32)
    split_new = fresh_kv.reshape(row_total, columns // (2 * head_dim), 2, head_dim)
    rotated = rotate(split_new[:, :, 0], new_pos[:, None])
    fresh_kv = (
        jnp.stack([rotated, split_new[:, :, 1]], axis=2)
        .astype(jnp.bfloat16)
        .reshape(row_total, columns)
    )
    cache_limit = cache.shape[1]
    padded = jnp.concatenate([cache[0], jnp.zeros((row_total, columns), jnp.bfloat16)], axis=0)
    placed = lax.dynamic_update_slice(jnp.zeros_like(padded), fresh_kv, (length, jnp.int32(0)))
    slot_ids = jnp.arange(cache_limit + row_total, dtype=jnp.int32)
    cache_next = jnp.where((slot_ids < length)[:, None], padded, placed)

    all_labels = jnp.arange(experts_attn, dtype=jnp.int32)
    blocks_routes = group_routes.reshape(block_count, rows_block, -1)
    slot_tokens = jax.vmap(lambda r: local_slots(r, all_labels, slot_count))(blocks_routes)
    slot_tokens = slot_tokens + (jnp.arange(block_count, dtype=jnp.int32) * rows_block)[:, None, None]
    expert_tokens = jnp.swapaxes(slot_tokens, 0, 1).reshape(experts_attn, -1)
    my_tokens = expert_tokens[position]
    picked_rows = select_rows(my_tokens, group_normed).astype(jnp.bfloat16)
    queries = jnp.einsum("sd,hdk->hsk", picked_rows, w_query, preferred_element_type=jnp.float32)
    queries = rotate(queries, (length + my_tokens)[None, :]).astype(jnp.bfloat16)
    heads_local = columns // (2 * head_dim)
    query_slots = queries.shape[1]
    send_q = queries.reshape(device_count, heads_local, query_slots, head_dim)
    recv_q = lax.all_to_all(send_q, "exp", 0, 0, tiled=True)
    split_old = cache[0].reshape(cache_limit, heads_local, 2, head_dim)
    split_fresh = fresh_kv.reshape(row_total, heads_local, 2, head_dim)
    keys = jnp.swapaxes(jnp.concatenate([split_old[:, :, 0], split_fresh[:, :, 0]], axis=0), 0, 1)
    values = jnp.swapaxes(jnp.concatenate([split_old[:, :, 1], split_fresh[:, :, 1]], axis=0), 0, 1)
    send_o = kernel_attention(recv_q, expert_tokens, keys, values, length, cache_limit)
    recv_o = lax.all_to_all(send_o, "exp", 0, 0, tiled=True)
    recv_o = recv_o.reshape(heads_here, query_slots, head_dim)
    projected = jnp.einsum("hsk,hkd->sd", recv_o, w_out, preferred_element_type=jnp.float32)
    send_p = projected.astype(jnp.bfloat16).reshape(block_count, slot_count, model_width)
    recv_p = lax.all_to_all(send_p, "exp", 0, 0, tiled=True)
    own_attn_routes = attn_routes[0]
    attn_gates = pick_gates(normed, attn_router, own_attn_routes)
    attn_own = combine(
        recv_p, own_attn_routes, attn_gates, route_slots(own_attn_routes, experts_attn), 1
    )
    middle = (own_rows.astype(jnp.float32) + attn_own).astype(jnp.bfloat16)
    normed_mlp = rms_norm(middle, norm_mlp)
    experts_mlp = mlp_router.shape[1]
    split_count = device_count // experts_mlp
    own_mlp_routes = mlp_routes[0]
    mlp_gates = pick_gates(normed_mlp, mlp_router, own_mlp_routes)
    mlp_tokens = local_slots(own_mlp_routes, jnp.arange(experts_mlp, dtype=jnp.int32), slot_count)
    dest_tokens = jnp.repeat(mlp_tokens, split_count, axis=0)
    send_m = (
        select_rows(dest_tokens.reshape(-1), normed_mlp)
        .astype(jnp.bfloat16)
        .reshape(device_count, slot_count, model_width)
    )
    inputs = lax.all_to_all(send_m, "exp", 0, 0, tiled=True).reshape(-1, model_width)
    slice_out = expert_mlp(inputs, w_gate, w_up, w_down)
    recv_m = lax.all_to_all(
        slice_out.reshape(device_count, slot_count, model_width), "exp", 0, 0, tiled=True
    )
    mlp_own = combine(
        recv_m, own_mlp_routes, mlp_gates, route_slots(own_mlp_routes, experts_mlp), split_count
    )
    layer_out = (middle.astype(jnp.float32) + mlp_own).astype(jnp.bfloat16)
    return (layer_out[None], cache_next[None])


def base_body(
    tokens,
    cache,
    cache_len,
    attn_routes,
    mlp_routes,
    norm_attn,
    attn_router,
    w_query,
    w_keyval,
    w_out,
    norm_mlp,
    mlp_router,
    w_gate,
    w_up,
    w_down,
):
    device_count = lax.axis_size("exp")
    position = lax.axis_index("exp")
    own_rows = tokens[0]
    rows_block = own_rows.shape[0]
    model_width = own_rows.shape[1]
    length = cache_len[0]
    slot_count = MOST
    normed = rms_norm(own_rows, norm_attn)
    group_normed, group_routes = (
        lax.all_gather(normed, "exp", axis=0, tiled=True),
        lax.all_gather(attn_routes[0], "exp", axis=0, tiled=True),
    )
    row_total = group_normed.shape[0]
    block_count = row_total // rows_block
    heads_here = w_query.shape[0]
    head_dim = w_query.shape[2]
    columns = w_keyval.shape[1]
    experts_attn = attn_router.shape[1]
    my_attn = jnp.reshape(position % experts_attn, (1,))
    new_pos = length + jnp.arange(row_total, dtype=jnp.int32)
    fresh_kv = jnp.dot(group_normed, w_keyval, preferred_element_type=jnp.float32)
    if columns < 2 * head_dim:
        is_key = position % 2 == 0
        fresh_kv = jnp.where(is_key, rotate(fresh_kv, new_pos), fresh_kv).astype(jnp.bfloat16)
    else:
        split_new = fresh_kv.reshape(row_total, columns // (2 * head_dim), 2, head_dim)
        rotated = rotate(split_new[:, :, 0], new_pos[:, None])
        fresh_kv = (
            jnp.stack([rotated, split_new[:, :, 1]], axis=2)
            .astype(jnp.bfloat16)
            .reshape(row_total, columns)
        )
    cache_limit = cache.shape[1]
    padded = jnp.concatenate([cache[0], jnp.zeros((row_total, columns), jnp.bfloat16)], axis=0)
    placed = lax.dynamic_update_slice(jnp.zeros_like(padded), fresh_kv, (length, jnp.int32(0)))
    slot_ids = jnp.arange(cache_limit + row_total, dtype=jnp.int32)
    cache_next = jnp.where((slot_ids < length)[:, None], padded, placed)
    group_cache = cache[0]
    group_fresh = fresh_kv
    for bit in range(experts_attn.bit_length() - 1):
        other_cache, other_fresh = from_partner((group_cache, group_fresh), "exp", bit)
        lower = position // (1 << bit) % 2 == 0
        group_cache = jnp.where(
            lower,
            jnp.concatenate([group_cache, other_cache], axis=1),
            jnp.concatenate([other_cache, group_cache], axis=1),
        )
        group_fresh = jnp.where(
            lower,
            jnp.concatenate([group_fresh, other_fresh], axis=1),
            jnp.concatenate([other_fresh, group_fresh], axis=1),
        )
    split_old = group_cache.reshape(cache_limit, heads_here, 2, head_dim)
    split_fresh = group_fresh.reshape(row_total, heads_here, 2, head_dim)
    attn_gates = pick_gates(group_normed, attn_router, group_routes)
    attn_tokens, attn_shares = slot_tables(
        group_routes, attn_gates, my_attn, rows_block, slot_count
    )
    token_flat = attn_tokens[:, 0, :].reshape(-1)
    share_flat = attn_shares[:, 0, :].reshape(-1)
    picked_rows = group_normed[token_flat]
    queries = jnp.einsum("sd,hdk->hsk", picked_rows, w_query, preferred_element_type=jnp.float32)
    queries = rotate(queries, (length + token_flat)[None, :]).astype(jnp.bfloat16)
    attend_heads = jax.vmap(attend, in_axes=(0, None, 1, 1, 1, 1, None))
    head_outs = attend_heads(
        queries,
        token_flat,
        split_old[:, :, 0],
        split_old[:, :, 1],
        split_fresh[:, :, 0],
        split_fresh[:, :, 1],
        length,
    )
    projected = jnp.einsum("hsk,hkd->sd", head_outs, w_out, preferred_element_type=jnp.float32)
    projected = (projected * share_flat[:, None]).reshape(block_count, slot_count, model_width)
    attn_ids = attn_tokens[:, 0, :]
    attn_own = lax.psum_scatter(
        spread_rows(projected, attn_ids, rows_block * lax.axis_size("exp")).astype(jnp.bfloat16),
        "exp",
        scatter_dimension=0,
        tiled=True,
    ).astype(jnp.float32)
    middle = lax.optimization_barrier(
        (own_rows.astype(jnp.float32) + attn_own).astype(jnp.bfloat16)
    )
    normed_mlp = rms_norm(middle, norm_mlp)
    experts_mlp = mlp_router.shape[1]
    split_count = device_count // experts_mlp
    my_expert = jnp.reshape(position // split_count, (1,))
    all_normed, all_routes = (
        lax.all_gather(normed_mlp, "exp", axis=0, tiled=True),
        lax.all_gather(mlp_routes[0], "exp", axis=0, tiled=True),
    )
    all_gates = pick_gates(all_normed, mlp_router, all_routes)
    mlp_tokens, mlp_shares = slot_tables(all_routes, all_gates, my_expert, rows_block, slot_count)
    inputs = all_normed[mlp_tokens.reshape(-1)]
    gate_part = jnp.dot(inputs, w_gate[0], preferred_element_type=jnp.float32)
    up_part = jnp.dot(inputs, w_up[0], preferred_element_type=jnp.float32)
    hidden = (jax.nn.silu(gate_part) * up_part).astype(jnp.bfloat16)
    slice_out = lax.optimization_barrier(
        jnp.dot(hidden, w_down[0], preferred_element_type=jnp.float32).astype(jnp.bfloat16)
    )
    weighted = (slice_out.astype(jnp.float32) * mlp_shares.reshape(-1)[:, None]).reshape(
        block_count, slot_count, model_width
    )
    mlp_ids = mlp_tokens[:, 0, :]
    mlp_own = lax.psum_scatter(
        spread_rows(weighted, mlp_ids, rows_block * lax.axis_size("exp")).astype(jnp.bfloat16),
        "exp",
        scatter_dimension=0,
        tiled=True,
    ).astype(jnp.float32)
    layer_out = (middle.astype(jnp.float32) + mlp_own).astype(jnp.bfloat16)
    return (layer_out[None], cache_next[None])


def solution(mesh):
    placed = (
        P("req", "exp", None),
        P("req", None, "exp"),
        P("req"),
        P("req", "exp", None),
        P("req", "exp", None),
        P(),
        P(),
        P("exp", None, None),
        P(None, "exp"),
        P("exp", None, None),
        P(),
        P(),
        P("exp", None, None),
        P("exp", None, None),
        P("exp", None, None),
    )
    return jax.shard_map(
        body,
        mesh=mesh,
        in_specs=placed,
        out_specs=(P("req", "exp", None), P("req", None, "exp")),
        check_vma=False,
    )
```

```python
import functools
import math

import jax
import jax.numpy as jnp
from jax import lax
from jax.experimental import pallas as pl
from jax.experimental.pallas import tpu as pltpu
from jax.sharding import PartitionSpec as P

MOST = 24


epsilon = 1e-05
rope_base = 10000.0
masked_score = -1e30


def from_partner(value, axis, stride):
    mask = 2**stride
    pairs = [(source, source ^ mask) for source in range(lax.axis_size(axis))]
    return lax.ppermute(value, axis, pairs)


def rms_norm(values, gain_vec):
    widened = values.astype(jnp.float32)
    inv_rms = lax.rsqrt(jnp.mean(widened * widened, axis=-1, keepdims=True) + epsilon)
    return (widened * inv_rms * gain_vec).astype(jnp.bfloat16)


def rotate(values, position):
    half_dim = values.shape[-1] // 2
    inv_freq = rope_base ** (-jnp.arange(half_dim).astype(jnp.float32) / half_dim)
    angles = position.astype(jnp.float32)[..., None] * inv_freq
    cosine = jnp.cos(angles)
    sines = jnp.sin(angles)
    first_half = values[..., :half_dim]
    second_half = values[..., half_dim:]
    return jnp.concatenate(
        [first_half * cosine - second_half * sines, second_half * cosine + first_half * sines],
        axis=-1,
    )


def rotate_whole(values, position):
    half_dim = values.shape[-1] // 2
    inv_freq = rope_base ** (-jnp.arange(half_dim).astype(jnp.float32) / half_dim)
    angles = position.astype(jnp.float32)[..., None] * inv_freq
    cosine = jnp.cos(angles)
    sines = jnp.sin(angles)
    swapped = jnp.concatenate([values[..., half_dim:], values[..., :half_dim]], axis=-1)
    return values * jnp.concatenate([cosine, cosine], axis=-1) + swapped * jnp.concatenate(
        [-sines, sines], axis=-1
    )


def pick_gates(normed, router, routes):
    logits = jnp.dot(normed, router, preferred_element_type=jnp.float32)
    labels = jnp.arange(router.shape[1], dtype=jnp.int32)
    onehot = (routes[:, :, None] == labels[None, None, :]).astype(jnp.float32)
    chosen = jnp.sum(onehot * logits[:, None, :], axis=-1)
    return jax.nn.softmax(chosen, axis=-1)


def slot_tables(routes, gates, labels, rows_block, slot_count):
    row_total = routes.shape[0]
    block_count = row_total // rows_block
    matches = routes[:, :, None] == labels[None, None, :]
    member = jnp.any(matches, axis=1).astype(jnp.int32).reshape(block_count, rows_block, -1)
    weight = jnp.sum(jnp.where(matches, gates[:, :, None], 0.0), axis=1).reshape(
        block_count, rows_block, -1
    )
    ranking = jnp.cumsum(member, axis=1) - 1
    slot_ids = jnp.arange(slot_count, dtype=jnp.int32)
    onehot = ((member[..., None] > 0) & (ranking[..., None] == slot_ids)).astype(jnp.int32)
    local_row = jnp.arange(rows_block, dtype=jnp.int32)[None, :, None, None]
    token_ids = (
        jnp.sum(onehot * local_row, axis=1)
        + (jnp.arange(block_count, dtype=jnp.int32) * rows_block)[:, None, None]
    )
    shares = jnp.sum(onehot.astype(jnp.float32) * weight[..., None], axis=1)
    return (token_ids, shares)


def spread_rows(terms, token_ids, extent):
    term_part = terms.reshape(-1, terms.shape[-1])
    id_part = token_ids.reshape(-1)
    return jnp.zeros((extent, terms.shape[-1]), jnp.float32).at[id_part].add(term_part, mode="drop")


def attend(queries, query_pos, key_cache, value_cache, key_fresh, value_fresh, length):
    query_count = queries.shape[0]
    head_dim = queries.shape[1]
    factor = head_dim ** (-0.5)

    def absorb(state, key_block, value_block, visible):
        running_top, running_total, running_acc = state
        scores = jnp.dot(queries, key_block.T, preferred_element_type=jnp.float32) * factor
        scores = jnp.where(visible, scores, masked_score)
        new_top = jnp.maximum(running_top, jnp.max(scores, axis=1))
        fading = jnp.exp(running_top - new_top)
        weights = jnp.exp(scores - new_top[:, None])
        running_total = running_total * fading + jnp.sum(weights, axis=1)
        running_acc = running_acc * fading[:, None] + jnp.dot(
            weights.astype(jnp.bfloat16), value_block, preferred_element_type=jnp.float32
        )
        return (new_top, running_total, running_acc)

    state = (
        jnp.full((query_count,), masked_score, jnp.float32),
        jnp.zeros((query_count,), jnp.float32),
        jnp.zeros((query_count, head_dim), jnp.float32),
    )
    cache_span = math.gcd(512, key_cache.shape[0])

    def cache_step(step_idx, state):
        offset = step_idx * cache_span
        key_block = lax.dynamic_slice_in_dim(key_cache, offset, cache_span, 0)
        value_block = lax.dynamic_slice_in_dim(value_cache, offset, cache_span, 0)
        visible = (offset + jnp.arange(cache_span, dtype=jnp.int32))[None, :] < length
        return absorb(state, key_block, value_block, visible)

    state = lax.fori_loop(0, (length + cache_span - 1) // cache_span, cache_step, state)
    fresh_span = math.gcd(512, key_fresh.shape[0])
    for offset in range(0, key_fresh.shape[0], fresh_span):
        visible = (offset + jnp.arange(fresh_span, dtype=jnp.int32))[None, :] <= query_pos[:, None]
        state = absorb(
            state,
            key_fresh[offset : offset + fresh_span],
            value_fresh[offset : offset + fresh_span],
            visible,
        )
    running_top, running_total, running_acc = state
    return (running_acc / running_total[:, None]).astype(jnp.bfloat16)


def running_count(member):
    rows = member.shape[0]
    lower = (
        jnp.arange(rows, dtype=jnp.int32)[None, :] <= jnp.arange(rows, dtype=jnp.int32)[:, None]
    ).astype(jnp.bfloat16)
    counts = jnp.dot(lower, member.astype(jnp.bfloat16), preferred_element_type=jnp.float32)
    return counts.astype(jnp.int32)


def local_slots(routes, labels, slot_count):
    matches = routes[:, :, None] == labels[None, None, :]
    member = jnp.any(matches, axis=1).astype(jnp.int32)
    ranking = running_count(member) - 1
    slot_ids = jnp.arange(slot_count, dtype=jnp.int32)
    onehot = ((member[..., None] > 0) & (ranking[..., None] == slot_ids)).astype(jnp.int32)
    rows = jnp.arange(routes.shape[0], dtype=jnp.int32)[:, None, None]
    return jnp.sum(onehot * rows, axis=0)


def route_slots(routes, label_count):
    labels = jnp.arange(label_count, dtype=jnp.int32)
    member = jnp.any(routes[:, :, None] == labels[None, None, :], axis=1).astype(jnp.int32)
    ranking = running_count(member) - 1
    return jnp.take_along_axis(ranking, routes, axis=1)


def select_rows(index, source):
    onehot = (index[:, None] == jnp.arange(source.shape[0], dtype=jnp.int32)[None, :]).astype(
        source.dtype
    )
    return jnp.dot(onehot, source, preferred_element_type=jnp.float32)


def combine(received, routes, gates, slots, split_count):
    slot_count = received.shape[1]
    flat = received.reshape(-1, received.shape[-1])
    total = jnp.zeros((routes.shape[0], received.shape[-1]), jnp.float32)
    for route in range(routes.shape[1]):
        expert = routes[:, route]
        part = jnp.zeros_like(total)
        for piece in range(split_count):
            index = (expert * split_count + piece) * slot_count + slots[:, route]
            part = part + lax.optimization_barrier(select_rows(index, flat))
        total = total + part * gates[:, route][:, None]
    return total


def mlp_kernel(x_ref, gate_ref, up_ref, down_ref, out_ref, acc_ref):
    step = pl.program_id(0)

    @pl.when(step == 0)
    def _():
        acc_ref[...] = jnp.zeros_like(acc_ref)

    rows = x_ref[...]
    gate_part = jnp.dot(rows, gate_ref[...], preferred_element_type=jnp.float32)
    up_part = jnp.dot(rows, up_ref[...], preferred_element_type=jnp.float32)
    hidden = (gate_part / (1.0 + jnp.exp(-gate_part)) * up_part).astype(jnp.bfloat16)
    acc_ref[...] += jnp.dot(hidden, down_ref[...], preferred_element_type=jnp.float32)

    @pl.when(step == pl.num_programs(0) - 1)
    def _():
        out_ref[...] = acc_ref[...].astype(out_ref.dtype)


def expert_mlp(rows, w_gate, w_up, w_down):
    row_count, width = rows.shape
    hidden_units = w_gate.shape[-1]
    tile = next(t for t in (1408, 512, 256, 128) if hidden_units % t == 0)
    return pl.pallas_call(
        mlp_kernel,
        grid=(hidden_units // tile,),
        in_specs=[
            pl.BlockSpec((row_count, width), lambda k: (0, 0)),
            pl.BlockSpec((None, width, tile), lambda k: (0, 0, k)),
            pl.BlockSpec((None, width, tile), lambda k: (0, 0, k)),
            pl.BlockSpec((None, tile, width), lambda k: (0, k, 0)),
        ],
        out_specs=pl.BlockSpec((row_count, width), lambda k: (0, 0)),
        out_shape=jax.ShapeDtypeStruct((row_count, width), jnp.bfloat16),
        scratch_shapes=[pltpu.VMEM((row_count, width), jnp.float32)],
        compiler_params=pltpu.CompilerParams(dimension_semantics=("arbitrary",)),
    )(rows, w_gate, w_up, w_down)


def attention_kernel(length_ref, query_ref, pos_ref, key_ref, value_ref, out_ref, *, cache_limit):
    length = length_ref[0]
    queries = query_ref[...]
    factor = queries.shape[-1] ** (-0.5)
    scores = (
        lax.dot_general(
            queries, key_ref[...], (((1,), (1,)), ((), ())), preferred_element_type=jnp.float32
        )
        * factor
    )
    column = lax.broadcasted_iota(jnp.int32, scores.shape, 1)
    in_cache = column < cache_limit
    visible = (in_cache & (column < length)) | (
        jnp.logical_not(in_cache) & (column - cache_limit <= pos_ref[...])
    )
    scores = jnp.where(visible, scores, masked_score)
    top = jnp.max(scores, axis=1, keepdims=True)
    weights = jnp.exp(scores - top)
    total = jnp.sum(weights, axis=1, keepdims=True)
    summed = jnp.dot(weights.astype(jnp.bfloat16), value_ref[...], preferred_element_type=jnp.float32)
    out_ref[...] = (summed / total).astype(out_ref.dtype)


def kernel_attention(queries, query_pos, keys, values, length, cache_limit):
    head_count, query_count, head_dim = queries.shape
    key_count = keys.shape[1]
    tile = next(t for t in (256, 128, 64, 32, 16, 8) if query_count % t == 0)
    grid_spec = pltpu.PrefetchScalarGridSpec(
        num_scalar_prefetch=1,
        grid=(head_count, query_count // tile),
        in_specs=[
            pl.BlockSpec((None, tile, head_dim), lambda h, i, n: (h, i, 0)),
            pl.BlockSpec((tile, 1), lambda h, i, n: (i, 0)),
            pl.BlockSpec((None, key_count, head_dim), lambda h, i, n: (h, 0, 0)),
            pl.BlockSpec((None, key_count, head_dim), lambda h, i, n: (h, 0, 0)),
        ],
        out_specs=pl.BlockSpec((None, tile, head_dim), lambda h, i, n: (h, i, 0)),
    )
    return pl.pallas_call(
        functools.partial(attention_kernel, cache_limit=cache_limit),
        grid_spec=grid_spec,
        out_shape=jax.ShapeDtypeStruct(queries.shape, jnp.bfloat16),
        compiler_params=pltpu.CompilerParams(dimension_semantics=("arbitrary", "arbitrary")),
    )(jnp.reshape(length, (1,)).astype(jnp.int32), queries, query_pos.reshape(-1, 1), keys, values)


def head_attention(queries, query_pos, keys, values, length, cache_limit):
    factor = queries.shape[-1] ** (-0.5)
    scores = jnp.einsum("hqk,hsk->hqs", queries, keys, preferred_element_type=jnp.float32) * factor
    slot_ids = jnp.arange(keys.shape[1], dtype=jnp.int32)[None, :]
    visible = jnp.where(
        slot_ids < cache_limit, slot_ids < length, slot_ids - cache_limit <= query_pos[:, None]
    )
    scores = jnp.where(visible[None], scores, masked_score)
    top = jnp.max(scores, axis=-1, keepdims=True)
    weights = jnp.exp(scores - top)
    total = jnp.sum(weights, axis=-1, keepdims=True)
    summed = jnp.einsum(
        "hqs,hsk->hqk", weights.astype(jnp.bfloat16), values, preferred_element_type=jnp.float32
    )
    return (summed / total).astype(jnp.bfloat16)


def body(
    tokens,
    cache,
    cache_len,
    attn_routes,
    mlp_routes,
    norm_attn,
    attn_router,
    w_query,
    w_keyval,
    w_out,
    norm_mlp,
    mlp_router,
    w_gate,
    w_up,
    w_down,
):
    device_count = lax.axis_size("exp")
    position = lax.axis_index("exp")
    own_rows = tokens[0]
    rows_block = own_rows.shape[0]
    model_width = own_rows.shape[1]
    length = cache_len[0]
    slot_count = MOST
    heads_here = w_query.shape[0]
    head_dim = w_query.shape[2]
    columns = w_keyval.shape[1]
    experts_attn = attn_router.shape[1]
    kv_heads = columns * device_count // (2 * head_dim)
    fast_attn = (
        device_count == experts_attn and heads_here == kv_heads and columns % (2 * head_dim) == 0
    )
    if not fast_attn:
        return base_body(
            tokens, cache, cache_len, attn_routes, mlp_routes, norm_attn, attn_router, w_query,
            w_keyval, w_out, norm_mlp, mlp_router, w_gate, w_up, w_down,
        )
    normed = rms_norm(own_rows, norm_attn)
    route_rows = jnp.zeros((16, 2 * rows_block), jnp.bfloat16)
    route_rows = route_rows.at[0].set(attn_routes[0].reshape(-1).astype(jnp.bfloat16))
    group_normed = lax.all_gather(normed, "exp", axis=0, tiled=True)
    gathered_routes = lax.all_gather(route_rows, "exp", axis=0, tiled=False)
    group_routes = gathered_routes[:, 0].astype(jnp.int32).reshape(-1, 2)
    row_total = group_normed.shape[0]
    block_count = row_total // rows_block
    new_pos = length + jnp.arange(row_total, dtype=jnp.int32)
    fresh_kv = jnp.dot(group_normed, w_keyval, preferred_element_type=jnp.float32)
    split_new = fresh_kv.reshape(row_total, columns // (2 * head_dim), 2, head_dim)
    rotated = rotate(split_new[:, :, 0], new_pos[:, None])
    fresh_kv = (
        jnp.stack([rotated, split_new[:, :, 1]], axis=2)
        .astype(jnp.bfloat16)
        .reshape(row_total, columns)
    )
    cache_limit = cache.shape[1]
    padded = jnp.concatenate([cache[0], jnp.zeros((row_total, columns), jnp.bfloat16)], axis=0)
    placed = lax.dynamic_update_slice(jnp.zeros_like(padded), fresh_kv, (length, jnp.int32(0)))
    slot_ids = jnp.arange(cache_limit + row_total, dtype=jnp.int32)
    cache_next = jnp.where((slot_ids < length)[:, None], padded, placed)

    all_labels = jnp.arange(experts_attn, dtype=jnp.int32)
    blocks_routes = group_routes.reshape(block_count, rows_block, -1)
    slot_tokens = jax.vmap(lambda r: local_slots(r, all_labels, slot_count))(blocks_routes)
    slot_tokens = slot_tokens + (jnp.arange(block_count, dtype=jnp.int32) * rows_block)[:, None, None]
    expert_tokens = jnp.swapaxes(slot_tokens, 0, 1).reshape(experts_attn, -1)
    my_tokens = expert_tokens[position]
    picked_rows = select_rows(my_tokens, group_normed).astype(jnp.bfloat16)
    queries = jnp.einsum("sd,hdk->hsk", picked_rows, w_query, preferred_element_type=jnp.float32)
    queries = rotate_whole(queries, (length + my_tokens)[None, :]).astype(jnp.bfloat16)
    heads_local = columns // (2 * head_dim)
    query_slots = queries.shape[1]
    send_q = queries.reshape(device_count, heads_local, query_slots, head_dim)
    recv_q = lax.all_to_all(send_q, "exp", 0, 0, tiled=True)
    recv_q = jnp.swapaxes(recv_q, 0, 1).reshape(heads_local, device_count * query_slots, head_dim)
    query_pos = expert_tokens.reshape(-1)
    split_old = cache[0].reshape(cache_limit, heads_local, 2, head_dim)
    split_fresh = fresh_kv.reshape(row_total, heads_local, 2, head_dim)
    keys = jnp.swapaxes(jnp.concatenate([split_old[:, :, 0], split_fresh[:, :, 0]], axis=0), 0, 1)
    values = jnp.swapaxes(jnp.concatenate([split_old[:, :, 1], split_fresh[:, :, 1]], axis=0), 0, 1)
    head_outs = kernel_attention(recv_q, query_pos, keys, values, length, cache_limit)
    send_o = jnp.swapaxes(
        head_outs.reshape(heads_local, device_count, query_slots, head_dim), 0, 1
    )
    recv_o = lax.all_to_all(send_o, "exp", 0, 0, tiled=True)
    recv_o = recv_o.reshape(heads_here, query_slots, head_dim)
    projected = jnp.einsum("hsk,hkd->sd", recv_o, w_out, preferred_element_type=jnp.float32)
    send_p = projected.astype(jnp.bfloat16).reshape(block_count, slot_count, model_width)
    recv_p = lax.all_to_all(send_p, "exp", 0, 0, tiled=True)
    own_attn_routes = attn_routes[0]
    attn_gates = pick_gates(normed, attn_router, own_attn_routes)
    attn_own = combine(
        recv_p, own_attn_routes, attn_gates, route_slots(own_attn_routes, experts_attn), 1
    )
    middle = (own_rows.astype(jnp.float32) + attn_own).astype(jnp.bfloat16)
    normed_mlp = rms_norm(middle, norm_mlp)
    experts_mlp = mlp_router.shape[1]
    split_count = device_count // experts_mlp
    own_mlp_routes = mlp_routes[0]
    mlp_gates = pick_gates(normed_mlp, mlp_router, own_mlp_routes)
    mlp_tokens = local_slots(own_mlp_routes, jnp.arange(experts_mlp, dtype=jnp.int32), slot_count)
    dest_tokens = jnp.repeat(mlp_tokens, split_count, axis=0)
    send_m = (
        select_rows(dest_tokens.reshape(-1), normed_mlp)
        .astype(jnp.bfloat16)
        .reshape(device_count, slot_count, model_width)
    )
    inputs = lax.all_to_all(send_m, "exp", 0, 0, tiled=True).reshape(-1, model_width)
    slice_out = expert_mlp(inputs, w_gate, w_up, w_down)
    recv_m = lax.all_to_all(
        slice_out.reshape(device_count, slot_count, model_width), "exp", 0, 0, tiled=True
    )
    mlp_own = combine(
        recv_m, own_mlp_routes, mlp_gates, route_slots(own_mlp_routes, experts_mlp), split_count
    )
    layer_out = (middle.astype(jnp.float32) + mlp_own).astype(jnp.bfloat16)
    return (layer_out[None], cache_next[None])


def base_body(
    tokens,
    cache,
    cache_len,
    attn_routes,
    mlp_routes,
    norm_attn,
    attn_router,
    w_query,
    w_keyval,
    w_out,
    norm_mlp,
    mlp_router,
    w_gate,
    w_up,
    w_down,
):
    device_count = lax.axis_size("exp")
    position = lax.axis_index("exp")
    own_rows = tokens[0]
    rows_block = own_rows.shape[0]
    model_width = own_rows.shape[1]
    length = cache_len[0]
    slot_count = MOST
    normed = rms_norm(own_rows, norm_attn)
    group_normed, group_routes = (
        lax.all_gather(normed, "exp", axis=0, tiled=True),
        lax.all_gather(attn_routes[0], "exp", axis=0, tiled=True),
    )
    row_total = group_normed.shape[0]
    block_count = row_total // rows_block
    heads_here = w_query.shape[0]
    head_dim = w_query.shape[2]
    columns = w_keyval.shape[1]
    experts_attn = attn_router.shape[1]
    my_attn = jnp.reshape(position % experts_attn, (1,))
    new_pos = length + jnp.arange(row_total, dtype=jnp.int32)
    fresh_kv = jnp.dot(group_normed, w_keyval, preferred_element_type=jnp.float32)
    if columns < 2 * head_dim:
        is_key = position % 2 == 0
        fresh_kv = jnp.where(is_key, rotate(fresh_kv, new_pos), fresh_kv).astype(jnp.bfloat16)
    else:
        split_new = fresh_kv.reshape(row_total, columns // (2 * head_dim), 2, head_dim)
        rotated = rotate(split_new[:, :, 0], new_pos[:, None])
        fresh_kv = (
            jnp.stack([rotated, split_new[:, :, 1]], axis=2)
            .astype(jnp.bfloat16)
            .reshape(row_total, columns)
        )
    cache_limit = cache.shape[1]
    padded = jnp.concatenate([cache[0], jnp.zeros((row_total, columns), jnp.bfloat16)], axis=0)
    placed = lax.dynamic_update_slice(jnp.zeros_like(padded), fresh_kv, (length, jnp.int32(0)))
    slot_ids = jnp.arange(cache_limit + row_total, dtype=jnp.int32)
    cache_next = jnp.where((slot_ids < length)[:, None], padded, placed)
    group_cache = cache[0]
    group_fresh = fresh_kv
    for bit in range(experts_attn.bit_length() - 1):
        other_cache, other_fresh = from_partner((group_cache, group_fresh), "exp", bit)
        lower = position // (1 << bit) % 2 == 0
        group_cache = jnp.where(
            lower,
            jnp.concatenate([group_cache, other_cache], axis=1),
            jnp.concatenate([other_cache, group_cache], axis=1),
        )
        group_fresh = jnp.where(
            lower,
            jnp.concatenate([group_fresh, other_fresh], axis=1),
            jnp.concatenate([other_fresh, group_fresh], axis=1),
        )
    split_old = group_cache.reshape(cache_limit, heads_here, 2, head_dim)
    split_fresh = group_fresh.reshape(row_total, heads_here, 2, head_dim)
    attn_gates = pick_gates(group_normed, attn_router, group_routes)
    attn_tokens, attn_shares = slot_tables(
        group_routes, attn_gates, my_attn, rows_block, slot_count
    )
    token_flat = attn_tokens[:, 0, :].reshape(-1)
    share_flat = attn_shares[:, 0, :].reshape(-1)
    picked_rows = group_normed[token_flat]
    queries = jnp.einsum("sd,hdk->hsk", picked_rows, w_query, preferred_element_type=jnp.float32)
    queries = rotate(queries, (length + token_flat)[None, :]).astype(jnp.bfloat16)
    attend_heads = jax.vmap(attend, in_axes=(0, None, 1, 1, 1, 1, None))
    head_outs = attend_heads(
        queries,
        token_flat,
        split_old[:, :, 0],
        split_old[:, :, 1],
        split_fresh[:, :, 0],
        split_fresh[:, :, 1],
        length,
    )
    projected = jnp.einsum("hsk,hkd->sd", head_outs, w_out, preferred_element_type=jnp.float32)
    projected = (projected * share_flat[:, None]).reshape(block_count, slot_count, model_width)
    attn_ids = attn_tokens[:, 0, :]
    attn_own = lax.psum_scatter(
        spread_rows(projected, attn_ids, rows_block * lax.axis_size("exp")).astype(jnp.bfloat16),
        "exp",
        scatter_dimension=0,
        tiled=True,
    ).astype(jnp.float32)
    middle = lax.optimization_barrier(
        (own_rows.astype(jnp.float32) + attn_own).astype(jnp.bfloat16)
    )
    normed_mlp = rms_norm(middle, norm_mlp)
    experts_mlp = mlp_router.shape[1]
    split_count = device_count // experts_mlp
    my_expert = jnp.reshape(position // split_count, (1,))
    all_normed, all_routes = (
        lax.all_gather(normed_mlp, "exp", axis=0, tiled=True),
        lax.all_gather(mlp_routes[0], "exp", axis=0, tiled=True),
    )
    all_gates = pick_gates(all_normed, mlp_router, all_routes)
    mlp_tokens, mlp_shares = slot_tables(all_routes, all_gates, my_expert, rows_block, slot_count)
    inputs = all_normed[mlp_tokens.reshape(-1)]
    gate_part = jnp.dot(inputs, w_gate[0], preferred_element_type=jnp.float32)
    up_part = jnp.dot(inputs, w_up[0], preferred_element_type=jnp.float32)
    hidden = (jax.nn.silu(gate_part) * up_part).astype(jnp.bfloat16)
    slice_out = lax.optimization_barrier(
        jnp.dot(hidden, w_down[0], preferred_element_type=jnp.float32).astype(jnp.bfloat16)
    )
    weighted = (slice_out.astype(jnp.float32) * mlp_shares.reshape(-1)[:, None]).reshape(
        block_count, slot_count, model_width
    )
    mlp_ids = mlp_tokens[:, 0, :]
    mlp_own = lax.psum_scatter(
        spread_rows(weighted, mlp_ids, rows_block * lax.axis_size("exp")).astype(jnp.bfloat16),
        "exp",
        scatter_dimension=0,
        tiled=True,
    ).astype(jnp.float32)
    layer_out = (middle.astype(jnp.float32) + mlp_own).astype(jnp.bfloat16)
    return (layer_out[None], cache_next[None])


def solution(mesh):
    placed = (
        P("req", "exp", None),
        P("req", None, "exp"),
        P("req"),
        P("req", "exp", None),
        P("req", "exp", None),
        P(),
        P(),
        P("exp", None, None),
        P(None, "exp"),
        P("exp", None, None),
        P(),
        P(),
        P("exp", None, None),
        P("exp", None, None),
        P("exp", None, None),
    )
    return jax.shard_map(
        body,
        mesh=mesh,
        in_specs=placed,
        out_specs=(P("req", "exp", None), P("req", None, "exp")),
        check_vma=False,
    )
```

```python
import functools
import math

import jax
import jax.numpy as jnp
from jax import lax
from jax.experimental import pallas as pl
from jax.experimental.pallas import tpu as pltpu
from jax.sharding import PartitionSpec as P

MOST = 24


epsilon = 1e-05
rope_base = 10000.0
masked_score = -1e30


def from_partner(value, axis, stride):
    mask = 2**stride
    pairs = [(source, source ^ mask) for source in range(lax.axis_size(axis))]
    return lax.ppermute(value, axis, pairs)


def rms_norm(values, gain_vec):
    widened = values.astype(jnp.float32)
    inv_rms = lax.rsqrt(jnp.mean(widened * widened, axis=-1, keepdims=True) + epsilon)
    return (widened * inv_rms * gain_vec).astype(jnp.bfloat16)


def rotate(values, position):
    half_dim = values.shape[-1] // 2
    inv_freq = rope_base ** (-jnp.arange(half_dim).astype(jnp.float32) / half_dim)
    angles = position.astype(jnp.float32)[..., None] * inv_freq
    cosine = jnp.cos(angles)
    sines = jnp.sin(angles)
    first_half = values[..., :half_dim]
    second_half = values[..., half_dim:]
    return jnp.concatenate(
        [first_half * cosine - second_half * sines, second_half * cosine + first_half * sines],
        axis=-1,
    )


def rotate_whole(values, position):
    half_dim = values.shape[-1] // 2
    inv_freq = rope_base ** (-jnp.arange(half_dim).astype(jnp.float32) / half_dim)
    angles = position.astype(jnp.float32)[..., None] * inv_freq
    cosine = jnp.cos(angles)
    sines = jnp.sin(angles)
    swapped = jnp.concatenate([values[..., half_dim:], values[..., :half_dim]], axis=-1)
    return values * jnp.concatenate([cosine, cosine], axis=-1) + swapped * jnp.concatenate(
        [-sines, sines], axis=-1
    )


def pick_gates(normed, router, routes):
    logits = jnp.dot(normed, router, preferred_element_type=jnp.float32)
    labels = jnp.arange(router.shape[1], dtype=jnp.int32)
    onehot = (routes[:, :, None] == labels[None, None, :]).astype(jnp.float32)
    chosen = jnp.sum(onehot * logits[:, None, :], axis=-1)
    return jax.nn.softmax(chosen, axis=-1)


def slot_tables(routes, gates, labels, rows_block, slot_count):
    row_total = routes.shape[0]
    block_count = row_total // rows_block
    matches = routes[:, :, None] == labels[None, None, :]
    member = jnp.any(matches, axis=1).astype(jnp.int32).reshape(block_count, rows_block, -1)
    weight = jnp.sum(jnp.where(matches, gates[:, :, None], 0.0), axis=1).reshape(
        block_count, rows_block, -1
    )
    ranking = jnp.cumsum(member, axis=1) - 1
    slot_ids = jnp.arange(slot_count, dtype=jnp.int32)
    onehot = ((member[..., None] > 0) & (ranking[..., None] == slot_ids)).astype(jnp.int32)
    local_row = jnp.arange(rows_block, dtype=jnp.int32)[None, :, None, None]
    token_ids = (
        jnp.sum(onehot * local_row, axis=1)
        + (jnp.arange(block_count, dtype=jnp.int32) * rows_block)[:, None, None]
    )
    shares = jnp.sum(onehot.astype(jnp.float32) * weight[..., None], axis=1)
    return (token_ids, shares)


def spread_rows(terms, token_ids, extent):
    term_part = terms.reshape(-1, terms.shape[-1])
    id_part = token_ids.reshape(-1)
    return jnp.zeros((extent, terms.shape[-1]), jnp.float32).at[id_part].add(term_part, mode="drop")


def attend(queries, query_pos, key_cache, value_cache, key_fresh, value_fresh, length):
    query_count = queries.shape[0]
    head_dim = queries.shape[1]
    factor = head_dim ** (-0.5)

    def absorb(state, key_block, value_block, visible):
        running_top, running_total, running_acc = state
        scores = jnp.dot(queries, key_block.T, preferred_element_type=jnp.float32) * factor
        scores = jnp.where(visible, scores, masked_score)
        new_top = jnp.maximum(running_top, jnp.max(scores, axis=1))
        fading = jnp.exp(running_top - new_top)
        weights = jnp.exp(scores - new_top[:, None])
        running_total = running_total * fading + jnp.sum(weights, axis=1)
        running_acc = running_acc * fading[:, None] + jnp.dot(
            weights.astype(jnp.bfloat16), value_block, preferred_element_type=jnp.float32
        )
        return (new_top, running_total, running_acc)

    state = (
        jnp.full((query_count,), masked_score, jnp.float32),
        jnp.zeros((query_count,), jnp.float32),
        jnp.zeros((query_count, head_dim), jnp.float32),
    )
    cache_span = math.gcd(512, key_cache.shape[0])

    def cache_step(step_idx, state):
        offset = step_idx * cache_span
        key_block = lax.dynamic_slice_in_dim(key_cache, offset, cache_span, 0)
        value_block = lax.dynamic_slice_in_dim(value_cache, offset, cache_span, 0)
        visible = (offset + jnp.arange(cache_span, dtype=jnp.int32))[None, :] < length
        return absorb(state, key_block, value_block, visible)

    state = lax.fori_loop(0, (length + cache_span - 1) // cache_span, cache_step, state)
    fresh_span = math.gcd(512, key_fresh.shape[0])
    for offset in range(0, key_fresh.shape[0], fresh_span):
        visible = (offset + jnp.arange(fresh_span, dtype=jnp.int32))[None, :] <= query_pos[:, None]
        state = absorb(
            state,
            key_fresh[offset : offset + fresh_span],
            value_fresh[offset : offset + fresh_span],
            visible,
        )
    running_top, running_total, running_acc = state
    return (running_acc / running_total[:, None]).astype(jnp.bfloat16)


def running_count(member):
    rows = member.shape[0]
    lower = (
        jnp.arange(rows, dtype=jnp.int32)[None, :] <= jnp.arange(rows, dtype=jnp.int32)[:, None]
    ).astype(jnp.bfloat16)
    counts = jnp.dot(lower, member.astype(jnp.bfloat16), preferred_element_type=jnp.float32)
    return counts.astype(jnp.int32)


def local_slots(routes, labels, slot_count):
    matches = routes[:, :, None] == labels[None, None, :]
    member = jnp.any(matches, axis=1).astype(jnp.int32)
    ranking = running_count(member) - 1
    slot_ids = jnp.arange(slot_count, dtype=jnp.int32)
    onehot = ((member[..., None] > 0) & (ranking[..., None] == slot_ids)).astype(jnp.int32)
    rows = jnp.arange(routes.shape[0], dtype=jnp.int32)[:, None, None]
    return jnp.sum(onehot * rows, axis=0)


def route_slots(routes, label_count):
    labels = jnp.arange(label_count, dtype=jnp.int32)
    member = jnp.any(routes[:, :, None] == labels[None, None, :], axis=1).astype(jnp.int32)
    ranking = running_count(member) - 1
    return jnp.take_along_axis(ranking, routes, axis=1)


def select_rows(index, source):
    onehot = (index[:, None] == jnp.arange(source.shape[0], dtype=jnp.int32)[None, :]).astype(
        source.dtype
    )
    return jnp.dot(onehot, source, preferred_element_type=jnp.float32)


def combine(received, routes, gates, slots, split_count):
    slot_count = received.shape[1]
    flat = received.reshape(-1, received.shape[-1])
    total = jnp.zeros((routes.shape[0], received.shape[-1]), jnp.float32)
    for route in range(routes.shape[1]):
        expert = routes[:, route]
        part = jnp.zeros_like(total)
        for piece in range(split_count):
            index = (expert * split_count + piece) * slot_count + slots[:, route]
            part = part + lax.optimization_barrier(select_rows(index, flat))
        total = total + part * gates[:, route][:, None]
    return total


def mlp_kernel(x_ref, gate_ref, up_ref, down_ref, out_ref, acc_ref):
    step = pl.program_id(0)

    @pl.when(step == 0)
    def _():
        acc_ref[...] = jnp.zeros_like(acc_ref)

    rows = x_ref[...]
    gate_part = jnp.dot(rows, gate_ref[...], preferred_element_type=jnp.float32)
    up_part = jnp.dot(rows, up_ref[...], preferred_element_type=jnp.float32)
    hidden = (gate_part / (1.0 + jnp.exp(-gate_part)) * up_part).astype(jnp.bfloat16)
    acc_ref[...] += jnp.dot(hidden, down_ref[...], preferred_element_type=jnp.float32)

    @pl.when(step == pl.num_programs(0) - 1)
    def _():
        out_ref[...] = acc_ref[...].astype(out_ref.dtype)


def expert_mlp(rows, w_gate, w_up, w_down):
    row_count, width = rows.shape
    hidden_units = w_gate.shape[-1]
    tile = next(t for t in (1408, 512, 256, 128) if hidden_units % t == 0)
    return pl.pallas_call(
        mlp_kernel,
        grid=(hidden_units // tile,),
        in_specs=[
            pl.BlockSpec((row_count, width), lambda k: (0, 0)),
            pl.BlockSpec((None, width, tile), lambda k: (0, 0, k)),
            pl.BlockSpec((None, width, tile), lambda k: (0, 0, k)),
            pl.BlockSpec((None, tile, width), lambda k: (0, k, 0)),
        ],
        out_specs=pl.BlockSpec((row_count, width), lambda k: (0, 0)),
        out_shape=jax.ShapeDtypeStruct((row_count, width), jnp.bfloat16),
        scratch_shapes=[pltpu.VMEM((row_count, width), jnp.float32)],
        compiler_params=pltpu.CompilerParams(dimension_semantics=("arbitrary",)),
    )(rows, w_gate, w_up, w_down)


def attention_kernel(length_ref, query_ref, pos_ref, key_ref, value_ref, out_ref, *, cache_limit):
    length = length_ref[0]
    queries = query_ref[...]
    factor = queries.shape[-1] ** (-0.5)
    scores = (
        lax.dot_general(
            queries, key_ref[...], (((1,), (1,)), ((), ())), preferred_element_type=jnp.float32
        )
        * factor
    )
    column = lax.broadcasted_iota(jnp.int32, scores.shape, 1)
    in_cache = column < cache_limit
    visible = (in_cache & (column < length)) | (
        jnp.logical_not(in_cache) & (column - cache_limit <= pos_ref[...])
    )
    scores = jnp.where(visible, scores, masked_score)
    top = jnp.max(scores, axis=1, keepdims=True)
    weights = jnp.exp(scores - top)
    total = jnp.sum(weights, axis=1, keepdims=True)
    summed = jnp.dot(weights.astype(jnp.bfloat16), value_ref[...], preferred_element_type=jnp.float32)
    out_ref[...] = (summed / total).astype(out_ref.dtype)


def kernel_attention(queries, query_pos, keys, values, length, cache_limit):
    head_count, query_count, head_dim = queries.shape
    key_count = keys.shape[1]
    tile = next(t for t in (256, 128, 64, 32, 16, 8) if query_count % t == 0)
    grid_spec = pltpu.PrefetchScalarGridSpec(
        num_scalar_prefetch=1,
        grid=(head_count, query_count // tile),
        in_specs=[
            pl.BlockSpec((None, tile, head_dim), lambda h, i, n: (h, i, 0)),
            pl.BlockSpec((tile, 1), lambda h, i, n: (i, 0)),
            pl.BlockSpec((None, key_count, head_dim), lambda h, i, n: (h, 0, 0)),
            pl.BlockSpec((None, key_count, head_dim), lambda h, i, n: (h, 0, 0)),
        ],
        out_specs=pl.BlockSpec((None, tile, head_dim), lambda h, i, n: (h, i, 0)),
    )
    return pl.pallas_call(
        functools.partial(attention_kernel, cache_limit=cache_limit),
        grid_spec=grid_spec,
        out_shape=jax.ShapeDtypeStruct(queries.shape, jnp.bfloat16),
        compiler_params=pltpu.CompilerParams(dimension_semantics=("arbitrary", "arbitrary")),
    )(jnp.reshape(length, (1,)).astype(jnp.int32), queries, query_pos.reshape(-1, 1), keys, values)


def head_attention(queries, query_pos, keys, values, length, cache_limit):
    factor = queries.shape[-1] ** (-0.5)
    scores = jnp.einsum("hqk,hsk->hqs", queries, keys, preferred_element_type=jnp.float32) * factor
    slot_ids = jnp.arange(keys.shape[1], dtype=jnp.int32)[None, :]
    visible = jnp.where(
        slot_ids < cache_limit, slot_ids < length, slot_ids - cache_limit <= query_pos[:, None]
    )
    scores = jnp.where(visible[None], scores, masked_score)
    top = jnp.max(scores, axis=-1, keepdims=True)
    weights = jnp.exp(scores - top)
    total = jnp.sum(weights, axis=-1, keepdims=True)
    summed = jnp.einsum(
        "hqs,hsk->hqk", weights.astype(jnp.bfloat16), values, preferred_element_type=jnp.float32
    )
    return (summed / total).astype(jnp.bfloat16)


def body(
    tokens,
    cache,
    cache_len,
    attn_routes,
    mlp_routes,
    norm_attn,
    attn_router,
    w_query,
    w_keyval,
    w_out,
    norm_mlp,
    mlp_router,
    w_gate,
    w_up,
    w_down,
):
    device_count = lax.axis_size("exp")
    position = lax.axis_index("exp")
    own_rows = tokens[0]
    rows_block = own_rows.shape[0]
    model_width = own_rows.shape[1]
    length = cache_len[0]
    slot_count = MOST
    heads_here = w_query.shape[0]
    head_dim = w_query.shape[2]
    columns = w_keyval.shape[1]
    experts_attn = attn_router.shape[1]
    kv_heads = columns * device_count // (2 * head_dim)
    fast_attn = (
        device_count == experts_attn and heads_here == kv_heads and columns % (2 * head_dim) == 0
    )
    if not fast_attn:
        return base_body(
            tokens, cache, cache_len, attn_routes, mlp_routes, norm_attn, attn_router, w_query,
            w_keyval, w_out, norm_mlp, mlp_router, w_gate, w_up, w_down,
        )
    normed = rms_norm(own_rows, norm_attn)
    route_rows = jnp.zeros((16, 2 * rows_block), jnp.bfloat16)
    route_rows = route_rows.at[0].set(attn_routes[0].reshape(-1).astype(jnp.bfloat16))
    group_normed = lax.all_gather(normed, "exp", axis=0, tiled=True)
    gathered_routes = lax.all_gather(route_rows, "exp", axis=0, tiled=False)
    group_routes = gathered_routes[:, 0].astype(jnp.int32).reshape(-1, 2)
    row_total = group_normed.shape[0]
    block_count = row_total // rows_block
    new_pos = length + jnp.arange(row_total, dtype=jnp.int32)
    fresh_kv = jnp.dot(group_normed, w_keyval, preferred_element_type=jnp.float32)
    split_new = fresh_kv.reshape(row_total, columns // (2 * head_dim), 2, head_dim)
    rotated = rotate(split_new[:, :, 0], new_pos[:, None])
    fresh_kv = (
        jnp.stack([rotated, split_new[:, :, 1]], axis=2)
        .astype(jnp.bfloat16)
        .reshape(row_total, columns)
    )
    cache_limit = cache.shape[1]
    padded = jnp.concatenate([cache[0], jnp.zeros((row_total, columns), jnp.bfloat16)], axis=0)
    placed = lax.dynamic_update_slice(jnp.zeros_like(padded), fresh_kv, (length, jnp.int32(0)))
    slot_ids = jnp.arange(cache_limit + row_total, dtype=jnp.int32)
    cache_next = jnp.where((slot_ids < length)[:, None], padded, placed)

    all_labels = jnp.arange(experts_attn, dtype=jnp.int32)
    blocks_routes = group_routes.reshape(block_count, rows_block, -1)
    slot_tokens = jax.vmap(lambda r: local_slots(r, all_labels, slot_count))(blocks_routes)
    slot_tokens = slot_tokens + (jnp.arange(block_count, dtype=jnp.int32) * rows_block)[:, None, None]
    expert_tokens = jnp.swapaxes(slot_tokens, 0, 1).reshape(experts_attn, -1)
    my_tokens = expert_tokens[position]
    picked_rows = select_rows(my_tokens, group_normed).astype(jnp.bfloat16)
    queries = jnp.einsum("sd,hdk->hsk", picked_rows, w_query, preferred_element_type=jnp.float32)
    queries = rotate_whole(queries, (length + my_tokens)[None, :]).astype(jnp.bfloat16)
    heads_local = columns // (2 * head_dim)
    query_slots = queries.shape[1]
    send_q = queries.reshape(device_count, heads_local, query_slots, head_dim)
    query_pos = expert_tokens.reshape(-1)
    split_old = cache[0].reshape(cache_limit, heads_local, 2, head_dim)
    split_fresh = fresh_kv.reshape(row_total, heads_local, 2, head_dim)
    keys = jnp.swapaxes(jnp.concatenate([split_old[:, :, 0], split_fresh[:, :, 0]], axis=0), 0, 1)
    values = jnp.swapaxes(jnp.concatenate([split_old[:, :, 1], split_fresh[:, :, 1]], axis=0), 0, 1)
    out_by_head = w_out.reshape(device_count, heads_local, head_dim, model_width)
    projected = jnp.zeros((query_slots, model_width), jnp.float32)
    for head in range(heads_local):
        recv_q = lax.all_to_all(send_q[:, head], "exp", 0, 0, tiled=True)
        head_out = kernel_attention(
            recv_q.reshape(1, device_count * query_slots, head_dim), query_pos,
            keys[head : head + 1], values[head : head + 1], length, cache_limit,
        )
        recv_o = lax.all_to_all(
            head_out.reshape(device_count, query_slots, head_dim), "exp", 0, 0, tiled=True
        )
        projected = projected + jnp.einsum(
            "dsk,dkm->sm", recv_o, out_by_head[:, head], preferred_element_type=jnp.float32
        )
    send_p = projected.astype(jnp.bfloat16).reshape(block_count, slot_count, model_width)
    recv_p = lax.all_to_all(send_p, "exp", 0, 0, tiled=True)
    own_attn_routes = attn_routes[0]
    attn_gates = pick_gates(normed, attn_router, own_attn_routes)
    attn_own = combine(
        recv_p, own_attn_routes, attn_gates, route_slots(own_attn_routes, experts_attn), 1
    )
    middle = (own_rows.astype(jnp.float32) + attn_own).astype(jnp.bfloat16)
    normed_mlp = rms_norm(middle, norm_mlp)
    experts_mlp = mlp_router.shape[1]
    split_count = device_count // experts_mlp
    own_mlp_routes = mlp_routes[0]
    mlp_gates = pick_gates(normed_mlp, mlp_router, own_mlp_routes)
    mlp_tokens = local_slots(own_mlp_routes, jnp.arange(experts_mlp, dtype=jnp.int32), slot_count)
    dest_tokens = jnp.repeat(mlp_tokens, split_count, axis=0)
    send_m = (
        select_rows(dest_tokens.reshape(-1), normed_mlp)
        .astype(jnp.bfloat16)
        .reshape(device_count, slot_count, model_width)
    )
    inputs = lax.all_to_all(send_m, "exp", 0, 0, tiled=True).reshape(-1, model_width)
    slice_out = expert_mlp(inputs, w_gate, w_up, w_down)
    recv_m = lax.all_to_all(
        slice_out.reshape(device_count, slot_count, model_width), "exp", 0, 0, tiled=True
    )
    mlp_own = combine(
        recv_m, own_mlp_routes, mlp_gates, route_slots(own_mlp_routes, experts_mlp), split_count
    )
    layer_out = (middle.astype(jnp.float32) + mlp_own).astype(jnp.bfloat16)
    return (layer_out[None], cache_next[None])


def base_body(
    tokens,
    cache,
    cache_len,
    attn_routes,
    mlp_routes,
    norm_attn,
    attn_router,
    w_query,
    w_keyval,
    w_out,
    norm_mlp,
    mlp_router,
    w_gate,
    w_up,
    w_down,
):
    device_count = lax.axis_size("exp")
    position = lax.axis_index("exp")
    own_rows = tokens[0]
    rows_block = own_rows.shape[0]
    model_width = own_rows.shape[1]
    length = cache_len[0]
    slot_count = MOST
    normed = rms_norm(own_rows, norm_attn)
    group_normed, group_routes = (
        lax.all_gather(normed, "exp", axis=0, tiled=True),
        lax.all_gather(attn_routes[0], "exp", axis=0, tiled=True),
    )
    row_total = group_normed.shape[0]
    block_count = row_total // rows_block
    heads_here = w_query.shape[0]
    head_dim = w_query.shape[2]
    columns = w_keyval.shape[1]
    experts_attn = attn_router.shape[1]
    my_attn = jnp.reshape(position % experts_attn, (1,))
    new_pos = length + jnp.arange(row_total, dtype=jnp.int32)
    fresh_kv = jnp.dot(group_normed, w_keyval, preferred_element_type=jnp.float32)
    if columns < 2 * head_dim:
        is_key = position % 2 == 0
        fresh_kv = jnp.where(is_key, rotate(fresh_kv, new_pos), fresh_kv).astype(jnp.bfloat16)
    else:
        split_new = fresh_kv.reshape(row_total, columns // (2 * head_dim), 2, head_dim)
        rotated = rotate(split_new[:, :, 0], new_pos[:, None])
        fresh_kv = (
            jnp.stack([rotated, split_new[:, :, 1]], axis=2)
            .astype(jnp.bfloat16)
            .reshape(row_total, columns)
        )
    cache_limit = cache.shape[1]
    padded = jnp.concatenate([cache[0], jnp.zeros((row_total, columns), jnp.bfloat16)], axis=0)
    placed = lax.dynamic_update_slice(jnp.zeros_like(padded), fresh_kv, (length, jnp.int32(0)))
    slot_ids = jnp.arange(cache_limit + row_total, dtype=jnp.int32)
    cache_next = jnp.where((slot_ids < length)[:, None], padded, placed)
    group_cache = cache[0]
    group_fresh = fresh_kv
    for bit in range(experts_attn.bit_length() - 1):
        other_cache, other_fresh = from_partner((group_cache, group_fresh), "exp", bit)
        lower = position // (1 << bit) % 2 == 0
        group_cache = jnp.where(
            lower,
            jnp.concatenate([group_cache, other_cache], axis=1),
            jnp.concatenate([other_cache, group_cache], axis=1),
        )
        group_fresh = jnp.where(
            lower,
            jnp.concatenate([group_fresh, other_fresh], axis=1),
            jnp.concatenate([other_fresh, group_fresh], axis=1),
        )
    split_old = group_cache.reshape(cache_limit, heads_here, 2, head_dim)
    split_fresh = group_fresh.reshape(row_total, heads_here, 2, head_dim)
    attn_gates = pick_gates(group_normed, attn_router, group_routes)
    attn_tokens, attn_shares = slot_tables(
        group_routes, attn_gates, my_attn, rows_block, slot_count
    )
    token_flat = attn_tokens[:, 0, :].reshape(-1)
    share_flat = attn_shares[:, 0, :].reshape(-1)
    picked_rows = group_normed[token_flat]
    queries = jnp.einsum("sd,hdk->hsk", picked_rows, w_query, preferred_element_type=jnp.float32)
    queries = rotate(queries, (length + token_flat)[None, :]).astype(jnp.bfloat16)
    attend_heads = jax.vmap(attend, in_axes=(0, None, 1, 1, 1, 1, None))
    head_outs = attend_heads(
        queries,
        token_flat,
        split_old[:, :, 0],
        split_old[:, :, 1],
        split_fresh[:, :, 0],
        split_fresh[:, :, 1],
        length,
    )
    projected = jnp.einsum("hsk,hkd->sd", head_outs, w_out, preferred_element_type=jnp.float32)
    projected = (projected * share_flat[:, None]).reshape(block_count, slot_count, model_width)
    attn_ids = attn_tokens[:, 0, :]
    attn_own = lax.psum_scatter(
        spread_rows(projected, attn_ids, rows_block * lax.axis_size("exp")).astype(jnp.bfloat16),
        "exp",
        scatter_dimension=0,
        tiled=True,
    ).astype(jnp.float32)
    middle = lax.optimization_barrier(
        (own_rows.astype(jnp.float32) + attn_own).astype(jnp.bfloat16)
    )
    normed_mlp = rms_norm(middle, norm_mlp)
    experts_mlp = mlp_router.shape[1]
    split_count = device_count // experts_mlp
    my_expert = jnp.reshape(position // split_count, (1,))
    all_normed, all_routes = (
        lax.all_gather(normed_mlp, "exp", axis=0, tiled=True),
        lax.all_gather(mlp_routes[0], "exp", axis=0, tiled=True),
    )
    all_gates = pick_gates(all_normed, mlp_router, all_routes)
    mlp_tokens, mlp_shares = slot_tables(all_routes, all_gates, my_expert, rows_block, slot_count)
    inputs = all_normed[mlp_tokens.reshape(-1)]
    gate_part = jnp.dot(inputs, w_gate[0], preferred_element_type=jnp.float32)
    up_part = jnp.dot(inputs, w_up[0], preferred_element_type=jnp.float32)
    hidden = (jax.nn.silu(gate_part) * up_part).astype(jnp.bfloat16)
    slice_out = lax.optimization_barrier(
        jnp.dot(hidden, w_down[0], preferred_element_type=jnp.float32).astype(jnp.bfloat16)
    )
    weighted = (slice_out.astype(jnp.float32) * mlp_shares.reshape(-1)[:, None]).reshape(
        block_count, slot_count, model_width
    )
    mlp_ids = mlp_tokens[:, 0, :]
    mlp_own = lax.psum_scatter(
        spread_rows(weighted, mlp_ids, rows_block * lax.axis_size("exp")).astype(jnp.bfloat16),
        "exp",
        scatter_dimension=0,
        tiled=True,
    ).astype(jnp.float32)
    layer_out = (middle.astype(jnp.float32) + mlp_own).astype(jnp.bfloat16)
    return (layer_out[None], cache_next[None])


def solution(mesh):
    placed = (
        P("req", "exp", None),
        P("req", None, "exp"),
        P("req"),
        P("req", "exp", None),
        P("req", "exp", None),
        P(),
        P(),
        P("exp", None, None),
        P(None, "exp"),
        P("exp", None, None),
        P(),
        P(),
        P("exp", None, None),
        P("exp", None, None),
        P("exp", None, None),
    )
    return jax.shard_map(
        body,
        mesh=mesh,
        in_specs=placed,
        out_specs=(P("req", "exp", None), P("req", None, "exp")),
        check_vma=False,
    )
```

```python
import functools
import math

import jax
import jax.numpy as jnp
from jax import lax
from jax.experimental import pallas as pl
from jax.experimental.pallas import tpu as pltpu
from jax.sharding import PartitionSpec as P

MOST = 24


epsilon = 1e-05
rope_base = 10000.0
masked_score = -1e30


def from_partner(value, axis, stride):
    mask = 2**stride
    pairs = [(source, source ^ mask) for source in range(lax.axis_size(axis))]
    return lax.ppermute(value, axis, pairs)


def rms_norm(values, gain_vec):
    widened = values.astype(jnp.float32)
    inv_rms = lax.rsqrt(jnp.mean(widened * widened, axis=-1, keepdims=True) + epsilon)
    return (widened * inv_rms * gain_vec).astype(jnp.bfloat16)


def rotate(values, position):
    half_dim = values.shape[-1] // 2
    inv_freq = rope_base ** (-jnp.arange(half_dim).astype(jnp.float32) / half_dim)
    angles = position.astype(jnp.float32)[..., None] * inv_freq
    cosine = jnp.cos(angles)
    sines = jnp.sin(angles)
    first_half = values[..., :half_dim]
    second_half = values[..., half_dim:]
    return jnp.concatenate(
        [first_half * cosine - second_half * sines, second_half * cosine + first_half * sines],
        axis=-1,
    )


def rotate_whole(values, position):
    half_dim = values.shape[-1] // 2
    inv_freq = rope_base ** (-jnp.arange(half_dim).astype(jnp.float32) / half_dim)
    angles = position.astype(jnp.float32)[..., None] * inv_freq
    cosine = jnp.cos(angles)
    sines = jnp.sin(angles)
    swapped = jnp.concatenate([values[..., half_dim:], values[..., :half_dim]], axis=-1)
    return values * jnp.concatenate([cosine, cosine], axis=-1) + swapped * jnp.concatenate(
        [-sines, sines], axis=-1
    )


def pick_gates(normed, router, routes):
    logits = jnp.dot(normed, router, preferred_element_type=jnp.float32)
    labels = jnp.arange(router.shape[1], dtype=jnp.int32)
    onehot = (routes[:, :, None] == labels[None, None, :]).astype(jnp.float32)
    chosen = jnp.sum(onehot * logits[:, None, :], axis=-1)
    return jax.nn.softmax(chosen, axis=-1)


def slot_tables(routes, gates, labels, rows_block, slot_count):
    row_total = routes.shape[0]
    block_count = row_total // rows_block
    matches = routes[:, :, None] == labels[None, None, :]
    member = jnp.any(matches, axis=1).astype(jnp.int32).reshape(block_count, rows_block, -1)
    weight = jnp.sum(jnp.where(matches, gates[:, :, None], 0.0), axis=1).reshape(
        block_count, rows_block, -1
    )
    ranking = jnp.cumsum(member, axis=1) - 1
    slot_ids = jnp.arange(slot_count, dtype=jnp.int32)
    onehot = ((member[..., None] > 0) & (ranking[..., None] == slot_ids)).astype(jnp.int32)
    local_row = jnp.arange(rows_block, dtype=jnp.int32)[None, :, None, None]
    token_ids = (
        jnp.sum(onehot * local_row, axis=1)
        + (jnp.arange(block_count, dtype=jnp.int32) * rows_block)[:, None, None]
    )
    shares = jnp.sum(onehot.astype(jnp.float32) * weight[..., None], axis=1)
    return (token_ids, shares)


def spread_rows(terms, token_ids, extent):
    term_part = terms.reshape(-1, terms.shape[-1])
    id_part = token_ids.reshape(-1)
    return jnp.zeros((extent, terms.shape[-1]), jnp.float32).at[id_part].add(term_part, mode="drop")


def attend(queries, query_pos, key_cache, value_cache, key_fresh, value_fresh, length):
    query_count = queries.shape[0]
    head_dim = queries.shape[1]
    factor = head_dim ** (-0.5)

    def absorb(state, key_block, value_block, visible):
        running_top, running_total, running_acc = state
        scores = jnp.dot(queries, key_block.T, preferred_element_type=jnp.float32) * factor
        scores = jnp.where(visible, scores, masked_score)
        new_top = jnp.maximum(running_top, jnp.max(scores, axis=1))
        fading = jnp.exp(running_top - new_top)
        weights = jnp.exp(scores - new_top[:, None])
        running_total = running_total * fading + jnp.sum(weights, axis=1)
        running_acc = running_acc * fading[:, None] + jnp.dot(
            weights.astype(jnp.bfloat16), value_block, preferred_element_type=jnp.float32
        )
        return (new_top, running_total, running_acc)

    state = (
        jnp.full((query_count,), masked_score, jnp.float32),
        jnp.zeros((query_count,), jnp.float32),
        jnp.zeros((query_count, head_dim), jnp.float32),
    )
    cache_span = math.gcd(512, key_cache.shape[0])

    def cache_step(step_idx, state):
        offset = step_idx * cache_span
        key_block = lax.dynamic_slice_in_dim(key_cache, offset, cache_span, 0)
        value_block = lax.dynamic_slice_in_dim(value_cache, offset, cache_span, 0)
        visible = (offset + jnp.arange(cache_span, dtype=jnp.int32))[None, :] < length
        return absorb(state, key_block, value_block, visible)

    state = lax.fori_loop(0, (length + cache_span - 1) // cache_span, cache_step, state)
    fresh_span = math.gcd(512, key_fresh.shape[0])
    for offset in range(0, key_fresh.shape[0], fresh_span):
        visible = (offset + jnp.arange(fresh_span, dtype=jnp.int32))[None, :] <= query_pos[:, None]
        state = absorb(
            state,
            key_fresh[offset : offset + fresh_span],
            value_fresh[offset : offset + fresh_span],
            visible,
        )
    running_top, running_total, running_acc = state
    return (running_acc / running_total[:, None]).astype(jnp.bfloat16)


def running_count(member):
    rows = member.shape[0]
    lower = (
        jnp.arange(rows, dtype=jnp.int32)[None, :] <= jnp.arange(rows, dtype=jnp.int32)[:, None]
    ).astype(jnp.bfloat16)
    counts = jnp.dot(lower, member.astype(jnp.bfloat16), preferred_element_type=jnp.float32)
    return counts.astype(jnp.int32)


def local_slots(routes, labels, slot_count):
    matches = routes[:, :, None] == labels[None, None, :]
    member = jnp.any(matches, axis=1).astype(jnp.int32)
    ranking = running_count(member) - 1
    slot_ids = jnp.arange(slot_count, dtype=jnp.int32)
    onehot = ((member[..., None] > 0) & (ranking[..., None] == slot_ids)).astype(jnp.int32)
    rows = jnp.arange(routes.shape[0], dtype=jnp.int32)[:, None, None]
    return jnp.sum(onehot * rows, axis=0)


def route_slots(routes, label_count):
    labels = jnp.arange(label_count, dtype=jnp.int32)
    member = jnp.any(routes[:, :, None] == labels[None, None, :], axis=1).astype(jnp.int32)
    ranking = running_count(member) - 1
    return jnp.take_along_axis(ranking, routes, axis=1)


def select_rows(index, source):
    onehot = (index[:, None] == jnp.arange(source.shape[0], dtype=jnp.int32)[None, :]).astype(
        source.dtype
    )
    return jnp.dot(onehot, source, preferred_element_type=jnp.float32)


def combine(received, routes, gates, slots, split_count):
    slot_count = received.shape[1]
    flat = received.reshape(-1, received.shape[-1])
    total = jnp.zeros((routes.shape[0], received.shape[-1]), jnp.float32)
    for route in range(routes.shape[1]):
        expert = routes[:, route]
        part = jnp.zeros_like(total)
        for piece in range(split_count):
            index = (expert * split_count + piece) * slot_count + slots[:, route]
            part = part + lax.optimization_barrier(select_rows(index, flat))
        total = total + part * gates[:, route][:, None]
    return total


def mlp_kernel(x_ref, gate_ref, up_ref, down_ref, out_ref, acc_ref):
    step = pl.program_id(0)

    @pl.when(step == 0)
    def _():
        acc_ref[...] = jnp.zeros_like(acc_ref)

    rows = x_ref[...]
    gate_part = jnp.dot(rows, gate_ref[...], preferred_element_type=jnp.float32)
    up_part = jnp.dot(rows, up_ref[...], preferred_element_type=jnp.float32)
    hidden = (gate_part / (1.0 + jnp.exp(-gate_part)) * up_part).astype(jnp.bfloat16)
    acc_ref[...] += jnp.dot(hidden, down_ref[...], preferred_element_type=jnp.float32)

    @pl.when(step == pl.num_programs(0) - 1)
    def _():
        out_ref[...] = acc_ref[...].astype(out_ref.dtype)


def expert_mlp(rows, w_gate, w_up, w_down):
    row_count, width = rows.shape
    hidden_units = w_gate.shape[-1]
    tile = next(t for t in (1408, 512, 256, 128) if hidden_units % t == 0)
    return pl.pallas_call(
        mlp_kernel,
        grid=(hidden_units // tile,),
        in_specs=[
            pl.BlockSpec((row_count, width), lambda k: (0, 0)),
            pl.BlockSpec((None, width, tile), lambda k: (0, 0, k)),
            pl.BlockSpec((None, width, tile), lambda k: (0, 0, k)),
            pl.BlockSpec((None, tile, width), lambda k: (0, k, 0)),
        ],
        out_specs=pl.BlockSpec((row_count, width), lambda k: (0, 0)),
        out_shape=jax.ShapeDtypeStruct((row_count, width), jnp.bfloat16),
        scratch_shapes=[pltpu.VMEM((row_count, width), jnp.float32)],
        compiler_params=pltpu.CompilerParams(dimension_semantics=("arbitrary",)),
    )(rows, w_gate, w_up, w_down)


def attention_kernel(length_ref, query_ref, pos_ref, key_ref, value_ref, out_ref, *, cache_limit):
    length = length_ref[0]
    queries = query_ref[...]
    factor = queries.shape[-1] ** (-0.5)
    scores = (
        lax.dot_general(
            queries, key_ref[...], (((1,), (1,)), ((), ())), preferred_element_type=jnp.float32
        )
        * factor
    )
    column = lax.broadcasted_iota(jnp.int32, scores.shape, 1)
    in_cache = column < cache_limit
    visible = (in_cache & (column < length)) | (
        jnp.logical_not(in_cache) & (column - cache_limit <= pos_ref[...])
    )
    scores = jnp.where(visible, scores, masked_score)
    top = jnp.max(scores, axis=1, keepdims=True)
    weights = jnp.exp(scores - top)
    total = jnp.sum(weights, axis=1, keepdims=True)
    summed = jnp.dot(weights.astype(jnp.bfloat16), value_ref[...], preferred_element_type=jnp.float32)
    out_ref[...] = (summed / total).astype(out_ref.dtype)


def kernel_attention(queries, query_pos, keys, values, length, cache_limit):
    head_count, query_count, head_dim = queries.shape
    key_count = keys.shape[1]
    tile = next(t for t in (512, 256, 128, 64, 32, 16, 8) if query_count % t == 0)
    grid_spec = pltpu.PrefetchScalarGridSpec(
        num_scalar_prefetch=1,
        grid=(head_count, query_count // tile),
        in_specs=[
            pl.BlockSpec((None, tile, head_dim), lambda h, i, n: (h, i, 0)),
            pl.BlockSpec((tile, 1), lambda h, i, n: (i, 0)),
            pl.BlockSpec((None, key_count, head_dim), lambda h, i, n: (h, 0, 0)),
            pl.BlockSpec((None, key_count, head_dim), lambda h, i, n: (h, 0, 0)),
        ],
        out_specs=pl.BlockSpec((None, tile, head_dim), lambda h, i, n: (h, i, 0)),
    )
    return pl.pallas_call(
        functools.partial(attention_kernel, cache_limit=cache_limit),
        grid_spec=grid_spec,
        out_shape=jax.ShapeDtypeStruct(queries.shape, jnp.bfloat16),
        compiler_params=pltpu.CompilerParams(dimension_semantics=("arbitrary", "arbitrary")),
    )(jnp.reshape(length, (1,)).astype(jnp.int32), queries, query_pos.reshape(-1, 1), keys, values)


def head_attention(queries, query_pos, keys, values, length, cache_limit):
    factor = queries.shape[-1] ** (-0.5)
    scores = jnp.einsum("hqk,hsk->hqs", queries, keys, preferred_element_type=jnp.float32) * factor
    slot_ids = jnp.arange(keys.shape[1], dtype=jnp.int32)[None, :]
    visible = jnp.where(
        slot_ids < cache_limit, slot_ids < length, slot_ids - cache_limit <= query_pos[:, None]
    )
    scores = jnp.where(visible[None], scores, masked_score)
    top = jnp.max(scores, axis=-1, keepdims=True)
    weights = jnp.exp(scores - top)
    total = jnp.sum(weights, axis=-1, keepdims=True)
    summed = jnp.einsum(
        "hqs,hsk->hqk", weights.astype(jnp.bfloat16), values, preferred_element_type=jnp.float32
    )
    return (summed / total).astype(jnp.bfloat16)


def body(
    tokens,
    cache,
    cache_len,
    attn_routes,
    mlp_routes,
    norm_attn,
    attn_router,
    w_query,
    w_keyval,
    w_out,
    norm_mlp,
    mlp_router,
    w_gate,
    w_up,
    w_down,
):
    device_count = lax.axis_size("exp")
    position = lax.axis_index("exp")
    own_rows = tokens[0]
    rows_block = own_rows.shape[0]
    model_width = own_rows.shape[1]
    length = cache_len[0]
    slot_count = MOST
    heads_here = w_query.shape[0]
    head_dim = w_query.shape[2]
    columns = w_keyval.shape[1]
    experts_attn = attn_router.shape[1]
    kv_heads = columns * device_count // (2 * head_dim)
    fast_attn = (
        device_count == experts_attn and heads_here == kv_heads and columns % (2 * head_dim) == 0
    )
    if not fast_attn:
        return base_body(
            tokens, cache, cache_len, attn_routes, mlp_routes, norm_attn, attn_router, w_query,
            w_keyval, w_out, norm_mlp, mlp_router, w_gate, w_up, w_down,
        )
    normed = rms_norm(own_rows, norm_attn)
    route_rows = jnp.zeros((16, 2 * rows_block), jnp.bfloat16)
    route_rows = route_rows.at[0].set(attn_routes[0].reshape(-1).astype(jnp.bfloat16))
    group_normed = lax.all_gather(normed, "exp", axis=0, tiled=True)
    gathered_routes = lax.all_gather(route_rows, "exp", axis=0, tiled=False)
    group_routes = gathered_routes[:, 0].astype(jnp.int32).reshape(-1, 2)
    row_total = group_normed.shape[0]
    block_count = row_total // rows_block
    new_pos = length + jnp.arange(row_total, dtype=jnp.int32)
    fresh_kv = jnp.dot(group_normed, w_keyval, preferred_element_type=jnp.float32)
    split_new = fresh_kv.reshape(row_total, columns // (2 * head_dim), 2, head_dim)
    rotated = rotate(split_new[:, :, 0], new_pos[:, None])
    fresh_kv = (
        jnp.stack([rotated, split_new[:, :, 1]], axis=2)
        .astype(jnp.bfloat16)
        .reshape(row_total, columns)
    )
    cache_limit = cache.shape[1]
    padded = jnp.concatenate([cache[0], jnp.zeros((row_total, columns), jnp.bfloat16)], axis=0)
    placed = lax.dynamic_update_slice(jnp.zeros_like(padded), fresh_kv, (length, jnp.int32(0)))
    slot_ids = jnp.arange(cache_limit + row_total, dtype=jnp.int32)
    cache_next = jnp.where((slot_ids < length)[:, None], padded, placed)

    all_labels = jnp.arange(experts_attn, dtype=jnp.int32)
    blocks_routes = group_routes.reshape(block_count, rows_block, -1)
    slot_tokens = jax.vmap(lambda r: local_slots(r, all_labels, slot_count))(blocks_routes)
    slot_tokens = slot_tokens + (jnp.arange(block_count, dtype=jnp.int32) * rows_block)[:, None, None]
    expert_tokens = jnp.swapaxes(slot_tokens, 0, 1).reshape(experts_attn, -1)
    my_tokens = expert_tokens[position]
    picked_rows = select_rows(my_tokens, group_normed).astype(jnp.bfloat16)
    queries = jnp.einsum("sd,hdk->hsk", picked_rows, w_query, preferred_element_type=jnp.float32)
    queries = rotate_whole(queries, (length + my_tokens)[None, :]).astype(jnp.bfloat16)
    heads_local = columns // (2 * head_dim)
    query_slots = queries.shape[1]
    send_q = queries.reshape(device_count, heads_local, query_slots, head_dim)
    recv_q = lax.all_to_all(send_q, "exp", 0, 0, tiled=True)
    recv_q = jnp.swapaxes(recv_q, 0, 1).reshape(heads_local, device_count * query_slots, head_dim)
    query_pos = expert_tokens.reshape(-1)
    split_old = cache[0].reshape(cache_limit, heads_local, 2, head_dim)
    split_fresh = fresh_kv.reshape(row_total, heads_local, 2, head_dim)
    keys = jnp.swapaxes(jnp.concatenate([split_old[:, :, 0], split_fresh[:, :, 0]], axis=0), 0, 1)
    values = jnp.swapaxes(jnp.concatenate([split_old[:, :, 1], split_fresh[:, :, 1]], axis=0), 0, 1)
    out_by_head = w_out.reshape(device_count, heads_local, head_dim, model_width)
    projected = jnp.zeros((query_slots, model_width), jnp.float32)
    for head in range(heads_local):
        head_out = kernel_attention(
            recv_q[head : head + 1], query_pos, keys[head : head + 1], values[head : head + 1],
            length, cache_limit,
        )
        recv_o = lax.all_to_all(
            head_out.reshape(device_count, query_slots, head_dim), "exp", 0, 0, tiled=True
        )
        projected = projected + jnp.einsum(
            "dsk,dkm->sm", recv_o, out_by_head[:, head], preferred_element_type=jnp.float32
        )
    send_p = projected.astype(jnp.bfloat16).reshape(block_count, slot_count, model_width)
    recv_p = lax.all_to_all(send_p, "exp", 0, 0, tiled=True)
    own_attn_routes = attn_routes[0]
    attn_gates = pick_gates(normed, attn_router, own_attn_routes)
    attn_own = combine(
        recv_p, own_attn_routes, attn_gates, route_slots(own_attn_routes, experts_attn), 1
    )
    middle = (own_rows.astype(jnp.float32) + attn_own).astype(jnp.bfloat16)
    normed_mlp = rms_norm(middle, norm_mlp)
    experts_mlp = mlp_router.shape[1]
    split_count = device_count // experts_mlp
    own_mlp_routes = mlp_routes[0]
    mlp_gates = pick_gates(normed_mlp, mlp_router, own_mlp_routes)
    mlp_tokens = local_slots(own_mlp_routes, jnp.arange(experts_mlp, dtype=jnp.int32), slot_count)
    dest_tokens = jnp.repeat(mlp_tokens, split_count, axis=0)
    send_m = (
        select_rows(dest_tokens.reshape(-1), normed_mlp)
        .astype(jnp.bfloat16)
        .reshape(device_count, slot_count, model_width)
    )
    inputs = lax.all_to_all(send_m, "exp", 0, 0, tiled=True).reshape(-1, model_width)
    slice_out = expert_mlp(inputs, w_gate, w_up, w_down)
    recv_m = lax.all_to_all(
        slice_out.reshape(device_count, slot_count, model_width), "exp", 0, 0, tiled=True
    )
    mlp_own = combine(
        recv_m, own_mlp_routes, mlp_gates, route_slots(own_mlp_routes, experts_mlp), split_count
    )
    layer_out = (middle.astype(jnp.float32) + mlp_own).astype(jnp.bfloat16)
    return (layer_out[None], cache_next[None])


def base_body(
    tokens,
    cache,
    cache_len,
    attn_routes,
    mlp_routes,
    norm_attn,
    attn_router,
    w_query,
    w_keyval,
    w_out,
    norm_mlp,
    mlp_router,
    w_gate,
    w_up,
    w_down,
):
    device_count = lax.axis_size("exp")
    position = lax.axis_index("exp")
    own_rows = tokens[0]
    rows_block = own_rows.shape[0]
    model_width = own_rows.shape[1]
    length = cache_len[0]
    slot_count = MOST
    normed = rms_norm(own_rows, norm_attn)
    group_normed, group_routes = (
        lax.all_gather(normed, "exp", axis=0, tiled=True),
        lax.all_gather(attn_routes[0], "exp", axis=0, tiled=True),
    )
    row_total = group_normed.shape[0]
    block_count = row_total // rows_block
    heads_here = w_query.shape[0]
    head_dim = w_query.shape[2]
    columns = w_keyval.shape[1]
    experts_attn = attn_router.shape[1]
    my_attn = jnp.reshape(position % experts_attn, (1,))
    new_pos = length + jnp.arange(row_total, dtype=jnp.int32)
    fresh_kv = jnp.dot(group_normed, w_keyval, preferred_element_type=jnp.float32)
    if columns < 2 * head_dim:
        is_key = position % 2 == 0
        fresh_kv = jnp.where(is_key, rotate(fresh_kv, new_pos), fresh_kv).astype(jnp.bfloat16)
    else:
        split_new = fresh_kv.reshape(row_total, columns // (2 * head_dim), 2, head_dim)
        rotated = rotate(split_new[:, :, 0], new_pos[:, None])
        fresh_kv = (
            jnp.stack([rotated, split_new[:, :, 1]], axis=2)
            .astype(jnp.bfloat16)
            .reshape(row_total, columns)
        )
    cache_limit = cache.shape[1]
    padded = jnp.concatenate([cache[0], jnp.zeros((row_total, columns), jnp.bfloat16)], axis=0)
    placed = lax.dynamic_update_slice(jnp.zeros_like(padded), fresh_kv, (length, jnp.int32(0)))
    slot_ids = jnp.arange(cache_limit + row_total, dtype=jnp.int32)
    cache_next = jnp.where((slot_ids < length)[:, None], padded, placed)
    group_cache = cache[0]
    group_fresh = fresh_kv
    for bit in range(experts_attn.bit_length() - 1):
        other_cache, other_fresh = from_partner((group_cache, group_fresh), "exp", bit)
        lower = position // (1 << bit) % 2 == 0
        group_cache = jnp.where(
            lower,
            jnp.concatenate([group_cache, other_cache], axis=1),
            jnp.concatenate([other_cache, group_cache], axis=1),
        )
        group_fresh = jnp.where(
            lower,
            jnp.concatenate([group_fresh, other_fresh], axis=1),
            jnp.concatenate([other_fresh, group_fresh], axis=1),
        )
    split_old = group_cache.reshape(cache_limit, heads_here, 2, head_dim)
    split_fresh = group_fresh.reshape(row_total, heads_here, 2, head_dim)
    attn_gates = pick_gates(group_normed, attn_router, group_routes)
    attn_tokens, attn_shares = slot_tables(
        group_routes, attn_gates, my_attn, rows_block, slot_count
    )
    token_flat = attn_tokens[:, 0, :].reshape(-1)
    share_flat = attn_shares[:, 0, :].reshape(-1)
    picked_rows = group_normed[token_flat]
    queries = jnp.einsum("sd,hdk->hsk", picked_rows, w_query, preferred_element_type=jnp.float32)
    queries = rotate(queries, (length + token_flat)[None, :]).astype(jnp.bfloat16)
    attend_heads = jax.vmap(attend, in_axes=(0, None, 1, 1, 1, 1, None))
    head_outs = attend_heads(
        queries,
        token_flat,
        split_old[:, :, 0],
        split_old[:, :, 1],
        split_fresh[:, :, 0],
        split_fresh[:, :, 1],
        length,
    )
    projected = jnp.einsum("hsk,hkd->sd", head_outs, w_out, preferred_element_type=jnp.float32)
    projected = (projected * share_flat[:, None]).reshape(block_count, slot_count, model_width)
    attn_ids = attn_tokens[:, 0, :]
    attn_own = lax.psum_scatter(
        spread_rows(projected, attn_ids, rows_block * lax.axis_size("exp")).astype(jnp.bfloat16),
        "exp",
        scatter_dimension=0,
        tiled=True,
    ).astype(jnp.float32)
    middle = lax.optimization_barrier(
        (own_rows.astype(jnp.float32) + attn_own).astype(jnp.bfloat16)
    )
    normed_mlp = rms_norm(middle, norm_mlp)
    experts_mlp = mlp_router.shape[1]
    split_count = device_count // experts_mlp
    my_expert = jnp.reshape(position // split_count, (1,))
    all_normed, all_routes = (
        lax.all_gather(normed_mlp, "exp", axis=0, tiled=True),
        lax.all_gather(mlp_routes[0], "exp", axis=0, tiled=True),
    )
    all_gates = pick_gates(all_normed, mlp_router, all_routes)
    mlp_tokens, mlp_shares = slot_tables(all_routes, all_gates, my_expert, rows_block, slot_count)
    inputs = all_normed[mlp_tokens.reshape(-1)]
    gate_part = jnp.dot(inputs, w_gate[0], preferred_element_type=jnp.float32)
    up_part = jnp.dot(inputs, w_up[0], preferred_element_type=jnp.float32)
    hidden = (jax.nn.silu(gate_part) * up_part).astype(jnp.bfloat16)
    slice_out = lax.optimization_barrier(
        jnp.dot(hidden, w_down[0], preferred_element_type=jnp.float32).astype(jnp.bfloat16)
    )
    weighted = (slice_out.astype(jnp.float32) * mlp_shares.reshape(-1)[:, None]).reshape(
        block_count, slot_count, model_width
    )
    mlp_ids = mlp_tokens[:, 0, :]
    mlp_own = lax.psum_scatter(
        spread_rows(weighted, mlp_ids, rows_block * lax.axis_size("exp")).astype(jnp.bfloat16),
        "exp",
        scatter_dimension=0,
        tiled=True,
    ).astype(jnp.float32)
    layer_out = (middle.astype(jnp.float32) + mlp_own).astype(jnp.bfloat16)
    return (layer_out[None], cache_next[None])


def solution(mesh):
    placed = (
        P("req", "exp", None),
        P("req", None, "exp"),
        P("req"),
        P("req", "exp", None),
        P("req", "exp", None),
        P(),
        P(),
        P("exp", None, None),
        P(None, "exp"),
        P("exp", None, None),
        P(),
        P(),
        P("exp", None, None),
        P("exp", None, None),
        P("exp", None, None),
    )
    return jax.shard_map(
        body,
        mesh=mesh,
        in_specs=placed,
        out_specs=(P("req", "exp", None), P("req", None, "exp")),
        check_vma=False,
    )
```

```python
import functools
import math

import jax
import jax.numpy as jnp
from jax import lax
from jax.experimental import pallas as pl
from jax.experimental.pallas import tpu as pltpu
from jax.sharding import PartitionSpec as P

MOST = 24


epsilon = 1e-05
rope_base = 10000.0
masked_score = -1e30


def from_partner(value, axis, stride):
    mask = 2**stride
    pairs = [(source, source ^ mask) for source in range(lax.axis_size(axis))]
    return lax.ppermute(value, axis, pairs)


def rms_norm(values, gain_vec):
    widened = values.astype(jnp.float32)
    inv_rms = lax.rsqrt(jnp.mean(widened * widened, axis=-1, keepdims=True) + epsilon)
    return (widened * inv_rms * gain_vec).astype(jnp.bfloat16)


def rotate(values, position):
    half_dim = values.shape[-1] // 2
    inv_freq = rope_base ** (-jnp.arange(half_dim).astype(jnp.float32) / half_dim)
    angles = position.astype(jnp.float32)[..., None] * inv_freq
    cosine = jnp.cos(angles)
    sines = jnp.sin(angles)
    first_half = values[..., :half_dim]
    second_half = values[..., half_dim:]
    return jnp.concatenate(
        [first_half * cosine - second_half * sines, second_half * cosine + first_half * sines],
        axis=-1,
    )


def rotate_whole(values, position):
    half_dim = values.shape[-1] // 2
    inv_freq = rope_base ** (-jnp.arange(half_dim).astype(jnp.float32) / half_dim)
    angles = position.astype(jnp.float32)[..., None] * inv_freq
    cosine = jnp.cos(angles)
    sines = jnp.sin(angles)
    swapped = jnp.concatenate([values[..., half_dim:], values[..., :half_dim]], axis=-1)
    return values * jnp.concatenate([cosine, cosine], axis=-1) + swapped * jnp.concatenate(
        [-sines, sines], axis=-1
    )


def pick_gates(normed, router, routes):
    logits = jnp.dot(normed, router, preferred_element_type=jnp.float32)
    labels = jnp.arange(router.shape[1], dtype=jnp.int32)
    onehot = (routes[:, :, None] == labels[None, None, :]).astype(jnp.float32)
    chosen = jnp.sum(onehot * logits[:, None, :], axis=-1)
    return jax.nn.softmax(chosen, axis=-1)


def slot_tables(routes, gates, labels, rows_block, slot_count):
    row_total = routes.shape[0]
    block_count = row_total // rows_block
    matches = routes[:, :, None] == labels[None, None, :]
    member = jnp.any(matches, axis=1).astype(jnp.int32).reshape(block_count, rows_block, -1)
    weight = jnp.sum(jnp.where(matches, gates[:, :, None], 0.0), axis=1).reshape(
        block_count, rows_block, -1
    )
    ranking = jnp.cumsum(member, axis=1) - 1
    slot_ids = jnp.arange(slot_count, dtype=jnp.int32)
    onehot = ((member[..., None] > 0) & (ranking[..., None] == slot_ids)).astype(jnp.int32)
    local_row = jnp.arange(rows_block, dtype=jnp.int32)[None, :, None, None]
    token_ids = (
        jnp.sum(onehot * local_row, axis=1)
        + (jnp.arange(block_count, dtype=jnp.int32) * rows_block)[:, None, None]
    )
    shares = jnp.sum(onehot.astype(jnp.float32) * weight[..., None], axis=1)
    return (token_ids, shares)


def spread_rows(terms, token_ids, extent):
    term_part = terms.reshape(-1, terms.shape[-1])
    id_part = token_ids.reshape(-1)
    return jnp.zeros((extent, terms.shape[-1]), jnp.float32).at[id_part].add(term_part, mode="drop")


def attend(queries, query_pos, key_cache, value_cache, key_fresh, value_fresh, length):
    query_count = queries.shape[0]
    head_dim = queries.shape[1]
    factor = head_dim ** (-0.5)

    def absorb(state, key_block, value_block, visible):
        running_top, running_total, running_acc = state
        scores = jnp.dot(queries, key_block.T, preferred_element_type=jnp.float32) * factor
        scores = jnp.where(visible, scores, masked_score)
        new_top = jnp.maximum(running_top, jnp.max(scores, axis=1))
        fading = jnp.exp(running_top - new_top)
        weights = jnp.exp(scores - new_top[:, None])
        running_total = running_total * fading + jnp.sum(weights, axis=1)
        running_acc = running_acc * fading[:, None] + jnp.dot(
            weights.astype(jnp.bfloat16), value_block, preferred_element_type=jnp.float32
        )
        return (new_top, running_total, running_acc)

    state = (
        jnp.full((query_count,), masked_score, jnp.float32),
        jnp.zeros((query_count,), jnp.float32),
        jnp.zeros((query_count, head_dim), jnp.float32),
    )
    cache_span = math.gcd(512, key_cache.shape[0])

    def cache_step(step_idx, state):
        offset = step_idx * cache_span
        key_block = lax.dynamic_slice_in_dim(key_cache, offset, cache_span, 0)
        value_block = lax.dynamic_slice_in_dim(value_cache, offset, cache_span, 0)
        visible = (offset + jnp.arange(cache_span, dtype=jnp.int32))[None, :] < length
        return absorb(state, key_block, value_block, visible)

    state = lax.fori_loop(0, (length + cache_span - 1) // cache_span, cache_step, state)
    fresh_span = math.gcd(512, key_fresh.shape[0])
    for offset in range(0, key_fresh.shape[0], fresh_span):
        visible = (offset + jnp.arange(fresh_span, dtype=jnp.int32))[None, :] <= query_pos[:, None]
        state = absorb(
            state,
            key_fresh[offset : offset + fresh_span],
            value_fresh[offset : offset + fresh_span],
            visible,
        )
    running_top, running_total, running_acc = state
    return (running_acc / running_total[:, None]).astype(jnp.bfloat16)


def running_count(member):
    rows = member.shape[0]
    lower = (
        jnp.arange(rows, dtype=jnp.int32)[None, :] <= jnp.arange(rows, dtype=jnp.int32)[:, None]
    ).astype(jnp.bfloat16)
    counts = jnp.dot(lower, member.astype(jnp.bfloat16), preferred_element_type=jnp.float32)
    return counts.astype(jnp.int32)


def local_slots(routes, labels, slot_count):
    matches = routes[:, :, None] == labels[None, None, :]
    member = jnp.any(matches, axis=1).astype(jnp.int32)
    ranking = running_count(member) - 1
    slot_ids = jnp.arange(slot_count, dtype=jnp.int32)
    onehot = ((member[..., None] > 0) & (ranking[..., None] == slot_ids)).astype(jnp.int32)
    rows = jnp.arange(routes.shape[0], dtype=jnp.int32)[:, None, None]
    return jnp.sum(onehot * rows, axis=0)


def route_slots(routes, label_count):
    labels = jnp.arange(label_count, dtype=jnp.int32)
    member = jnp.any(routes[:, :, None] == labels[None, None, :], axis=1).astype(jnp.int32)
    ranking = running_count(member) - 1
    return jnp.take_along_axis(ranking, routes, axis=1)


def select_rows(index, source):
    onehot = (index[:, None] == jnp.arange(source.shape[0], dtype=jnp.int32)[None, :]).astype(
        source.dtype
    )
    return jnp.dot(onehot, source, preferred_element_type=jnp.float32)


def combine(received, routes, gates, slots, split_count):
    slot_count = received.shape[1]
    flat = received.reshape(-1, received.shape[-1])
    total = jnp.zeros((routes.shape[0], received.shape[-1]), jnp.float32)
    for route in range(routes.shape[1]):
        expert = routes[:, route]
        part = jnp.zeros_like(total)
        for piece in range(split_count):
            index = (expert * split_count + piece) * slot_count + slots[:, route]
            part = part + lax.optimization_barrier(select_rows(index, flat))
        total = total + part * gates[:, route][:, None]
    return total


def mlp_kernel(x_ref, gate_ref, up_ref, down_ref, out_ref, acc_ref):
    step = pl.program_id(0)

    @pl.when(step == 0)
    def _():
        acc_ref[...] = jnp.zeros_like(acc_ref)

    rows = x_ref[...]
    gate_part = jnp.dot(rows, gate_ref[...], preferred_element_type=jnp.float32)
    up_part = jnp.dot(rows, up_ref[...], preferred_element_type=jnp.float32)
    hidden = (gate_part / (1.0 + jnp.exp(-gate_part)) * up_part).astype(jnp.bfloat16)
    acc_ref[...] += jnp.dot(hidden, down_ref[...], preferred_element_type=jnp.float32)

    @pl.when(step == pl.num_programs(0) - 1)
    def _():
        out_ref[...] = acc_ref[...].astype(out_ref.dtype)


def expert_mlp(rows, w_gate, w_up, w_down):
    row_count, width = rows.shape
    hidden_units = w_gate.shape[-1]
    tile = next(t for t in (512, 256, 128) if hidden_units % t == 0)
    return pl.pallas_call(
        mlp_kernel,
        grid=(hidden_units // tile,),
        in_specs=[
            pl.BlockSpec((row_count, width), lambda k: (0, 0)),
            pl.BlockSpec((None, width, tile), lambda k: (0, 0, k)),
            pl.BlockSpec((None, width, tile), lambda k: (0, 0, k)),
            pl.BlockSpec((None, tile, width), lambda k: (0, k, 0)),
        ],
        out_specs=pl.BlockSpec((row_count, width), lambda k: (0, 0)),
        out_shape=jax.ShapeDtypeStruct((row_count, width), jnp.bfloat16),
        scratch_shapes=[pltpu.VMEM((row_count, width), jnp.float32)],
        compiler_params=pltpu.CompilerParams(dimension_semantics=("arbitrary",)),
    )(rows, w_gate, w_up, w_down)


def attention_kernel(length_ref, query_ref, pos_ref, key_ref, value_ref, out_ref, *, cache_limit):
    length = length_ref[0]
    queries = query_ref[...]
    factor = queries.shape[-1] ** (-0.5)
    scores = (
        lax.dot_general(
            queries, key_ref[...], (((1,), (1,)), ((), ())), preferred_element_type=jnp.float32
        )
        * factor
    )
    column = lax.broadcasted_iota(jnp.int32, scores.shape, 1)
    in_cache = column < cache_limit
    visible = (in_cache & (column < length)) | (
        jnp.logical_not(in_cache) & (column - cache_limit <= pos_ref[...])
    )
    scores = jnp.where(visible, scores, masked_score)
    top = jnp.max(scores, axis=1, keepdims=True)
    weights = jnp.exp(scores - top)
    total = jnp.sum(weights, axis=1, keepdims=True)
    summed = jnp.dot(weights.astype(jnp.bfloat16), value_ref[...], preferred_element_type=jnp.float32)
    out_ref[...] = (summed / total).astype(out_ref.dtype)


def kernel_attention(queries, query_pos, keys, values, length, cache_limit):
    head_count, query_count, head_dim = queries.shape
    key_count = keys.shape[1]
    tile = next(t for t in (256, 128, 64, 32, 16, 8) if query_count % t == 0)
    grid_spec = pltpu.PrefetchScalarGridSpec(
        num_scalar_prefetch=1,
        grid=(head_count, query_count // tile),
        in_specs=[
            pl.BlockSpec((None, tile, head_dim), lambda h, i, n: (h, i, 0)),
            pl.BlockSpec((tile, 1), lambda h, i, n: (i, 0)),
            pl.BlockSpec((None, key_count, head_dim), lambda h, i, n: (h, 0, 0)),
            pl.BlockSpec((None, key_count, head_dim), lambda h, i, n: (h, 0, 0)),
        ],
        out_specs=pl.BlockSpec((None, tile, head_dim), lambda h, i, n: (h, i, 0)),
    )
    return pl.pallas_call(
        functools.partial(attention_kernel, cache_limit=cache_limit),
        grid_spec=grid_spec,
        out_shape=jax.ShapeDtypeStruct(queries.shape, jnp.bfloat16),
        compiler_params=pltpu.CompilerParams(dimension_semantics=("arbitrary", "arbitrary")),
    )(jnp.reshape(length, (1,)).astype(jnp.int32), queries, query_pos.reshape(-1, 1), keys, values)


def head_attention(queries, query_pos, keys, values, length, cache_limit):
    factor = queries.shape[-1] ** (-0.5)
    scores = jnp.einsum("hqk,hsk->hqs", queries, keys, preferred_element_type=jnp.float32) * factor
    slot_ids = jnp.arange(keys.shape[1], dtype=jnp.int32)[None, :]
    visible = jnp.where(
        slot_ids < cache_limit, slot_ids < length, slot_ids - cache_limit <= query_pos[:, None]
    )
    scores = jnp.where(visible[None], scores, masked_score)
    top = jnp.max(scores, axis=-1, keepdims=True)
    weights = jnp.exp(scores - top)
    total = jnp.sum(weights, axis=-1, keepdims=True)
    summed = jnp.einsum(
        "hqs,hsk->hqk", weights.astype(jnp.bfloat16), values, preferred_element_type=jnp.float32
    )
    return (summed / total).astype(jnp.bfloat16)


def body(
    tokens,
    cache,
    cache_len,
    attn_routes,
    mlp_routes,
    norm_attn,
    attn_router,
    w_query,
    w_keyval,
    w_out,
    norm_mlp,
    mlp_router,
    w_gate,
    w_up,
    w_down,
):
    device_count = lax.axis_size("exp")
    position = lax.axis_index("exp")
    own_rows = tokens[0]
    rows_block = own_rows.shape[0]
    model_width = own_rows.shape[1]
    length = cache_len[0]
    slot_count = MOST
    heads_here = w_query.shape[0]
    head_dim = w_query.shape[2]
    columns = w_keyval.shape[1]
    experts_attn = attn_router.shape[1]
    kv_heads = columns * device_count // (2 * head_dim)
    fast_attn = (
        device_count == experts_attn and heads_here == kv_heads and columns % (2 * head_dim) == 0
    )
    if not fast_attn:
        return base_body(
            tokens, cache, cache_len, attn_routes, mlp_routes, norm_attn, attn_router, w_query,
            w_keyval, w_out, norm_mlp, mlp_router, w_gate, w_up, w_down,
        )
    normed = rms_norm(own_rows, norm_attn)
    route_rows = jnp.zeros((16, 2 * rows_block), jnp.bfloat16)
    route_rows = route_rows.at[0].set(attn_routes[0].reshape(-1).astype(jnp.bfloat16))
    group_normed = lax.all_gather(normed, "exp", axis=0, tiled=True)
    gathered_routes = lax.all_gather(route_rows, "exp", axis=0, tiled=False)
    group_routes = gathered_routes[:, 0].astype(jnp.int32).reshape(-1, 2)
    row_total = group_normed.shape[0]
    block_count = row_total // rows_block
    new_pos = length + jnp.arange(row_total, dtype=jnp.int32)
    fresh_kv = jnp.dot(group_normed, w_keyval, preferred_element_type=jnp.float32)
    split_new = fresh_kv.reshape(row_total, columns // (2 * head_dim), 2, head_dim)
    rotated = rotate(split_new[:, :, 0], new_pos[:, None])
    fresh_kv = (
        jnp.stack([rotated, split_new[:, :, 1]], axis=2)
        .astype(jnp.bfloat16)
        .reshape(row_total, columns)
    )
    cache_limit = cache.shape[1]
    padded = jnp.concatenate([cache[0], jnp.zeros((row_total, columns), jnp.bfloat16)], axis=0)
    placed = lax.dynamic_update_slice(jnp.zeros_like(padded), fresh_kv, (length, jnp.int32(0)))
    slot_ids = jnp.arange(cache_limit + row_total, dtype=jnp.int32)
    cache_next = jnp.where((slot_ids < length)[:, None], padded, placed)

    all_labels = jnp.arange(experts_attn, dtype=jnp.int32)
    blocks_routes = group_routes.reshape(block_count, rows_block, -1)
    slot_tokens = jax.vmap(lambda r: local_slots(r, all_labels, slot_count))(blocks_routes)
    slot_tokens = slot_tokens + (jnp.arange(block_count, dtype=jnp.int32) * rows_block)[:, None, None]
    expert_tokens = jnp.swapaxes(slot_tokens, 0, 1).reshape(experts_attn, -1)
    my_tokens = expert_tokens[position]
    picked_rows = select_rows(my_tokens, group_normed).astype(jnp.bfloat16)
    queries = jnp.einsum("sd,hdk->hsk", picked_rows, w_query, preferred_element_type=jnp.float32)
    queries = rotate_whole(queries, (length + my_tokens)[None, :]).astype(jnp.bfloat16)
    heads_local = columns // (2 * head_dim)
    query_slots = queries.shape[1]
    send_q = queries.reshape(device_count, heads_local, query_slots, head_dim)
    recv_q = lax.all_to_all(send_q, "exp", 0, 0, tiled=True)
    recv_q = jnp.swapaxes(recv_q, 0, 1).reshape(heads_local, device_count * query_slots, head_dim)
    query_pos = expert_tokens.reshape(-1)
    split_old = cache[0].reshape(cache_limit, heads_local, 2, head_dim)
    split_fresh = fresh_kv.reshape(row_total, heads_local, 2, head_dim)
    keys = jnp.swapaxes(jnp.concatenate([split_old[:, :, 0], split_fresh[:, :, 0]], axis=0), 0, 1)
    values = jnp.swapaxes(jnp.concatenate([split_old[:, :, 1], split_fresh[:, :, 1]], axis=0), 0, 1)
    out_by_head = w_out.reshape(device_count, heads_local, head_dim, model_width)
    projected = jnp.zeros((query_slots, model_width), jnp.float32)
    for head in range(heads_local):
        head_out = kernel_attention(
            recv_q[head : head + 1], query_pos, keys[head : head + 1], values[head : head + 1],
            length, cache_limit,
        )
        recv_o = lax.all_to_all(
            head_out.reshape(device_count, query_slots, head_dim), "exp", 0, 0, tiled=True
        )
        projected = projected + jnp.einsum(
            "dsk,dkm->sm", recv_o, out_by_head[:, head], preferred_element_type=jnp.float32
        )
    send_p = projected.astype(jnp.bfloat16).reshape(block_count, slot_count, model_width)
    recv_p = lax.all_to_all(send_p, "exp", 0, 0, tiled=True)
    own_attn_routes = attn_routes[0]
    attn_gates = pick_gates(normed, attn_router, own_attn_routes)
    attn_own = combine(
        recv_p, own_attn_routes, attn_gates, route_slots(own_attn_routes, experts_attn), 1
    )
    middle = (own_rows.astype(jnp.float32) + attn_own).astype(jnp.bfloat16)
    normed_mlp = rms_norm(middle, norm_mlp)
    experts_mlp = mlp_router.shape[1]
    split_count = device_count // experts_mlp
    own_mlp_routes = mlp_routes[0]
    mlp_gates = pick_gates(normed_mlp, mlp_router, own_mlp_routes)
    mlp_tokens = local_slots(own_mlp_routes, jnp.arange(experts_mlp, dtype=jnp.int32), slot_count)
    dest_tokens = jnp.repeat(mlp_tokens, split_count, axis=0)
    send_m = (
        select_rows(dest_tokens.reshape(-1), normed_mlp)
        .astype(jnp.bfloat16)
        .reshape(device_count, slot_count, model_width)
    )
    inputs = lax.all_to_all(send_m, "exp", 0, 0, tiled=True).reshape(-1, model_width)
    slice_out = expert_mlp(inputs, w_gate, w_up, w_down)
    recv_m = lax.all_to_all(
        slice_out.reshape(device_count, slot_count, model_width), "exp", 0, 0, tiled=True
    )
    mlp_own = combine(
        recv_m, own_mlp_routes, mlp_gates, route_slots(own_mlp_routes, experts_mlp), split_count
    )
    layer_out = (middle.astype(jnp.float32) + mlp_own).astype(jnp.bfloat16)
    return (layer_out[None], cache_next[None])


def base_body(
    tokens,
    cache,
    cache_len,
    attn_routes,
    mlp_routes,
    norm_attn,
    attn_router,
    w_query,
    w_keyval,
    w_out,
    norm_mlp,
    mlp_router,
    w_gate,
    w_up,
    w_down,
):
    device_count = lax.axis_size("exp")
    position = lax.axis_index("exp")
    own_rows = tokens[0]
    rows_block = own_rows.shape[0]
    model_width = own_rows.shape[1]
    length = cache_len[0]
    slot_count = MOST
    normed = rms_norm(own_rows, norm_attn)
    group_normed, group_routes = (
        lax.all_gather(normed, "exp", axis=0, tiled=True),
        lax.all_gather(attn_routes[0], "exp", axis=0, tiled=True),
    )
    row_total = group_normed.shape[0]
    block_count = row_total // rows_block
    heads_here = w_query.shape[0]
    head_dim = w_query.shape[2]
    columns = w_keyval.shape[1]
    experts_attn = attn_router.shape[1]
    my_attn = jnp.reshape(position % experts_attn, (1,))
    new_pos = length + jnp.arange(row_total, dtype=jnp.int32)
    fresh_kv = jnp.dot(group_normed, w_keyval, preferred_element_type=jnp.float32)
    if columns < 2 * head_dim:
        is_key = position % 2 == 0
        fresh_kv = jnp.where(is_key, rotate(fresh_kv, new_pos), fresh_kv).astype(jnp.bfloat16)
    else:
        split_new = fresh_kv.reshape(row_total, columns // (2 * head_dim), 2, head_dim)
        rotated = rotate(split_new[:, :, 0], new_pos[:, None])
        fresh_kv = (
            jnp.stack([rotated, split_new[:, :, 1]], axis=2)
            .astype(jnp.bfloat16)
            .reshape(row_total, columns)
        )
    cache_limit = cache.shape[1]
    padded = jnp.concatenate([cache[0], jnp.zeros((row_total, columns), jnp.bfloat16)], axis=0)
    placed = lax.dynamic_update_slice(jnp.zeros_like(padded), fresh_kv, (length, jnp.int32(0)))
    slot_ids = jnp.arange(cache_limit + row_total, dtype=jnp.int32)
    cache_next = jnp.where((slot_ids < length)[:, None], padded, placed)
    group_cache = cache[0]
    group_fresh = fresh_kv
    for bit in range(experts_attn.bit_length() - 1):
        other_cache, other_fresh = from_partner((group_cache, group_fresh), "exp", bit)
        lower = position // (1 << bit) % 2 == 0
        group_cache = jnp.where(
            lower,
            jnp.concatenate([group_cache, other_cache], axis=1),
            jnp.concatenate([other_cache, group_cache], axis=1),
        )
        group_fresh = jnp.where(
            lower,
            jnp.concatenate([group_fresh, other_fresh], axis=1),
            jnp.concatenate([other_fresh, group_fresh], axis=1),
        )
    split_old = group_cache.reshape(cache_limit, heads_here, 2, head_dim)
    split_fresh = group_fresh.reshape(row_total, heads_here, 2, head_dim)
    attn_gates = pick_gates(group_normed, attn_router, group_routes)
    attn_tokens, attn_shares = slot_tables(
        group_routes, attn_gates, my_attn, rows_block, slot_count
    )
    token_flat = attn_tokens[:, 0, :].reshape(-1)
    share_flat = attn_shares[:, 0, :].reshape(-1)
    picked_rows = group_normed[token_flat]
    queries = jnp.einsum("sd,hdk->hsk", picked_rows, w_query, preferred_element_type=jnp.float32)
    queries = rotate(queries, (length + token_flat)[None, :]).astype(jnp.bfloat16)
    attend_heads = jax.vmap(attend, in_axes=(0, None, 1, 1, 1, 1, None))
    head_outs = attend_heads(
        queries,
        token_flat,
        split_old[:, :, 0],
        split_old[:, :, 1],
        split_fresh[:, :, 0],
        split_fresh[:, :, 1],
        length,
    )
    projected = jnp.einsum("hsk,hkd->sd", head_outs, w_out, preferred_element_type=jnp.float32)
    projected = (projected * share_flat[:, None]).reshape(block_count, slot_count, model_width)
    attn_ids = attn_tokens[:, 0, :]
    attn_own = lax.psum_scatter(
        spread_rows(projected, attn_ids, rows_block * lax.axis_size("exp")).astype(jnp.bfloat16),
        "exp",
        scatter_dimension=0,
        tiled=True,
    ).astype(jnp.float32)
    middle = lax.optimization_barrier(
        (own_rows.astype(jnp.float32) + attn_own).astype(jnp.bfloat16)
    )
    normed_mlp = rms_norm(middle, norm_mlp)
    experts_mlp = mlp_router.shape[1]
    split_count = device_count // experts_mlp
    my_expert = jnp.reshape(position // split_count, (1,))
    all_normed, all_routes = (
        lax.all_gather(normed_mlp, "exp", axis=0, tiled=True),
        lax.all_gather(mlp_routes[0], "exp", axis=0, tiled=True),
    )
    all_gates = pick_gates(all_normed, mlp_router, all_routes)
    mlp_tokens, mlp_shares = slot_tables(all_routes, all_gates, my_expert, rows_block, slot_count)
    inputs = all_normed[mlp_tokens.reshape(-1)]
    gate_part = jnp.dot(inputs, w_gate[0], preferred_element_type=jnp.float32)
    up_part = jnp.dot(inputs, w_up[0], preferred_element_type=jnp.float32)
    hidden = (jax.nn.silu(gate_part) * up_part).astype(jnp.bfloat16)
    slice_out = lax.optimization_barrier(
        jnp.dot(hidden, w_down[0], preferred_element_type=jnp.float32).astype(jnp.bfloat16)
    )
    weighted = (slice_out.astype(jnp.float32) * mlp_shares.reshape(-1)[:, None]).reshape(
        block_count, slot_count, model_width
    )
    mlp_ids = mlp_tokens[:, 0, :]
    mlp_own = lax.psum_scatter(
        spread_rows(weighted, mlp_ids, rows_block * lax.axis_size("exp")).astype(jnp.bfloat16),
        "exp",
        scatter_dimension=0,
        tiled=True,
    ).astype(jnp.float32)
    layer_out = (middle.astype(jnp.float32) + mlp_own).astype(jnp.bfloat16)
    return (layer_out[None], cache_next[None])


def solution(mesh):
    placed = (
        P("req", "exp", None),
        P("req", None, "exp"),
        P("req"),
        P("req", "exp", None),
        P("req", "exp", None),
        P(),
        P(),
        P("exp", None, None),
        P(None, "exp"),
        P("exp", None, None),
        P(),
        P(),
        P("exp", None, None),
        P("exp", None, None),
        P("exp", None, None),
    )
    return jax.shard_map(
        body,
        mesh=mesh,
        in_specs=placed,
        out_specs=(P("req", "exp", None), P("req", None, "exp")),
        check_vma=False,
    )
```

```python
import functools
import math

import jax
import jax.numpy as jnp
from jax import lax
from jax.experimental import pallas as pl
from jax.experimental.pallas import tpu as pltpu
from jax.sharding import PartitionSpec as P

MOST = 24


epsilon = 1e-05
rope_base = 10000.0
masked_score = -1e30


def from_partner(value, axis, stride):
    mask = 2**stride
    pairs = [(source, source ^ mask) for source in range(lax.axis_size(axis))]
    return lax.ppermute(value, axis, pairs)


def rms_norm(values, gain_vec):
    widened = values.astype(jnp.float32)
    inv_rms = lax.rsqrt(jnp.mean(widened * widened, axis=-1, keepdims=True) + epsilon)
    return (widened * inv_rms * gain_vec).astype(jnp.bfloat16)


def rotate(values, position):
    half_dim = values.shape[-1] // 2
    inv_freq = rope_base ** (-jnp.arange(half_dim).astype(jnp.float32) / half_dim)
    angles = position.astype(jnp.float32)[..., None] * inv_freq
    cosine = jnp.cos(angles)
    sines = jnp.sin(angles)
    first_half = values[..., :half_dim]
    second_half = values[..., half_dim:]
    return jnp.concatenate(
        [first_half * cosine - second_half * sines, second_half * cosine + first_half * sines],
        axis=-1,
    )


def rotate_whole(values, position):
    half_dim = values.shape[-1] // 2
    inv_freq = rope_base ** (-jnp.arange(half_dim).astype(jnp.float32) / half_dim)
    angles = position.astype(jnp.float32)[..., None] * inv_freq
    cosine = jnp.cos(angles)
    sines = jnp.sin(angles)
    swapped = jnp.concatenate([values[..., half_dim:], values[..., :half_dim]], axis=-1)
    return values * jnp.concatenate([cosine, cosine], axis=-1) + swapped * jnp.concatenate(
        [-sines, sines], axis=-1
    )


def pick_gates(normed, router, routes):
    logits = jnp.dot(normed, router, preferred_element_type=jnp.float32)
    labels = jnp.arange(router.shape[1], dtype=jnp.int32)
    onehot = (routes[:, :, None] == labels[None, None, :]).astype(jnp.float32)
    chosen = jnp.sum(onehot * logits[:, None, :], axis=-1)
    return jax.nn.softmax(chosen, axis=-1)


def slot_tables(routes, gates, labels, rows_block, slot_count):
    row_total = routes.shape[0]
    block_count = row_total // rows_block
    matches = routes[:, :, None] == labels[None, None, :]
    member = jnp.any(matches, axis=1).astype(jnp.int32).reshape(block_count, rows_block, -1)
    weight = jnp.sum(jnp.where(matches, gates[:, :, None], 0.0), axis=1).reshape(
        block_count, rows_block, -1
    )
    ranking = jnp.cumsum(member, axis=1) - 1
    slot_ids = jnp.arange(slot_count, dtype=jnp.int32)
    onehot = ((member[..., None] > 0) & (ranking[..., None] == slot_ids)).astype(jnp.int32)
    local_row = jnp.arange(rows_block, dtype=jnp.int32)[None, :, None, None]
    token_ids = (
        jnp.sum(onehot * local_row, axis=1)
        + (jnp.arange(block_count, dtype=jnp.int32) * rows_block)[:, None, None]
    )
    shares = jnp.sum(onehot.astype(jnp.float32) * weight[..., None], axis=1)
    return (token_ids, shares)


def spread_rows(terms, token_ids, extent):
    term_part = terms.reshape(-1, terms.shape[-1])
    id_part = token_ids.reshape(-1)
    return jnp.zeros((extent, terms.shape[-1]), jnp.float32).at[id_part].add(term_part, mode="drop")


def attend(queries, query_pos, key_cache, value_cache, key_fresh, value_fresh, length):
    query_count = queries.shape[0]
    head_dim = queries.shape[1]
    factor = head_dim ** (-0.5)

    def absorb(state, key_block, value_block, visible):
        running_top, running_total, running_acc = state
        scores = jnp.dot(queries, key_block.T, preferred_element_type=jnp.float32) * factor
        scores = jnp.where(visible, scores, masked_score)
        new_top = jnp.maximum(running_top, jnp.max(scores, axis=1))
        fading = jnp.exp(running_top - new_top)
        weights = jnp.exp(scores - new_top[:, None])
        running_total = running_total * fading + jnp.sum(weights, axis=1)
        running_acc = running_acc * fading[:, None] + jnp.dot(
            weights.astype(jnp.bfloat16), value_block, preferred_element_type=jnp.float32
        )
        return (new_top, running_total, running_acc)

    state = (
        jnp.full((query_count,), masked_score, jnp.float32),
        jnp.zeros((query_count,), jnp.float32),
        jnp.zeros((query_count, head_dim), jnp.float32),
    )
    cache_span = math.gcd(512, key_cache.shape[0])

    def cache_step(step_idx, state):
        offset = step_idx * cache_span
        key_block = lax.dynamic_slice_in_dim(key_cache, offset, cache_span, 0)
        value_block = lax.dynamic_slice_in_dim(value_cache, offset, cache_span, 0)
        visible = (offset + jnp.arange(cache_span, dtype=jnp.int32))[None, :] < length
        return absorb(state, key_block, value_block, visible)

    state = lax.fori_loop(0, (length + cache_span - 1) // cache_span, cache_step, state)
    fresh_span = math.gcd(512, key_fresh.shape[0])
    for offset in range(0, key_fresh.shape[0], fresh_span):
        visible = (offset + jnp.arange(fresh_span, dtype=jnp.int32))[None, :] <= query_pos[:, None]
        state = absorb(
            state,
            key_fresh[offset : offset + fresh_span],
            value_fresh[offset : offset + fresh_span],
            visible,
        )
    running_top, running_total, running_acc = state
    return (running_acc / running_total[:, None]).astype(jnp.bfloat16)


def running_count(member):
    rows = member.shape[0]
    lower = (
        jnp.arange(rows, dtype=jnp.int32)[None, :] <= jnp.arange(rows, dtype=jnp.int32)[:, None]
    ).astype(jnp.bfloat16)
    counts = jnp.dot(lower, member.astype(jnp.bfloat16), preferred_element_type=jnp.float32)
    return counts.astype(jnp.int32)


def local_slots(routes, labels, slot_count):
    matches = routes[:, :, None] == labels[None, None, :]
    member = jnp.any(matches, axis=1).astype(jnp.int32)
    ranking = running_count(member) - 1
    slot_ids = jnp.arange(slot_count, dtype=jnp.int32)
    onehot = ((member[..., None] > 0) & (ranking[..., None] == slot_ids)).astype(jnp.int32)
    rows = jnp.arange(routes.shape[0], dtype=jnp.int32)[:, None, None]
    return jnp.sum(onehot * rows, axis=0)


def route_slots(routes, label_count):
    labels = jnp.arange(label_count, dtype=jnp.int32)
    member = jnp.any(routes[:, :, None] == labels[None, None, :], axis=1).astype(jnp.int32)
    ranking = running_count(member) - 1
    return jnp.take_along_axis(ranking, routes, axis=1)


def select_rows(index, source):
    onehot = (index[:, None] == jnp.arange(source.shape[0], dtype=jnp.int32)[None, :]).astype(
        source.dtype
    )
    return jnp.dot(onehot, source, preferred_element_type=jnp.float32)


def combine(received, routes, gates, slots, split_count):
    slot_count = received.shape[1]
    flat = received.reshape(-1, received.shape[-1])
    total = jnp.zeros((routes.shape[0], received.shape[-1]), jnp.float32)
    for route in range(routes.shape[1]):
        expert = routes[:, route]
        part = jnp.zeros_like(total)
        for piece in range(split_count):
            index = (expert * split_count + piece) * slot_count + slots[:, route]
            part = part + lax.optimization_barrier(select_rows(index, flat))
        total = total + part * gates[:, route][:, None]
    return total


def mlp_kernel(x_ref, gate_ref, up_ref, down_ref, out_ref, acc_ref):
    step = pl.program_id(0)

    @pl.when(step == 0)
    def _():
        acc_ref[...] = jnp.zeros_like(acc_ref)

    rows = x_ref[...]
    gate_part = jnp.dot(rows, gate_ref[...], preferred_element_type=jnp.float32)
    up_part = jnp.dot(rows, up_ref[...], preferred_element_type=jnp.float32)
    hidden = (gate_part / (1.0 + jnp.exp(-gate_part)) * up_part).astype(jnp.bfloat16)
    acc_ref[...] += jnp.dot(hidden, down_ref[...], preferred_element_type=jnp.float32)

    @pl.when(step == pl.num_programs(0) - 1)
    def _():
        out_ref[...] = acc_ref[...].astype(out_ref.dtype)


def expert_mlp(rows, w_gate, w_up, w_down):
    row_count, width = rows.shape
    hidden_units = w_gate.shape[-1]
    tile = next(t for t in (1408, 512, 256, 128) if hidden_units % t == 0)
    return pl.pallas_call(
        mlp_kernel,
        grid=(hidden_units // tile,),
        in_specs=[
            pl.BlockSpec((row_count, width), lambda k: (0, 0)),
            pl.BlockSpec((None, width, tile), lambda k: (0, 0, k)),
            pl.BlockSpec((None, width, tile), lambda k: (0, 0, k)),
            pl.BlockSpec((None, tile, width), lambda k: (0, k, 0)),
        ],
        out_specs=pl.BlockSpec((row_count, width), lambda k: (0, 0)),
        out_shape=jax.ShapeDtypeStruct((row_count, width), jnp.bfloat16),
        scratch_shapes=[pltpu.VMEM((row_count, width), jnp.float32)],
        compiler_params=pltpu.CompilerParams(dimension_semantics=("arbitrary",)),
    )(rows, w_gate, w_up, w_down)


def attention_kernel(length_ref, query_ref, pos_ref, key_ref, value_ref, out_ref, *, cache_limit):
    length = length_ref[0]
    queries = query_ref[...]
    factor = queries.shape[-1] ** (-0.5)
    scores = (
        lax.dot_general(
            queries, key_ref[...], (((1,), (1,)), ((), ())), preferred_element_type=jnp.float32
        )
        * factor
    )
    column = lax.broadcasted_iota(jnp.int32, scores.shape, 1)
    in_cache = column < cache_limit
    visible = (in_cache & (column < length)) | (
        jnp.logical_not(in_cache) & (column - cache_limit <= pos_ref[...])
    )
    scores = jnp.where(visible, scores, masked_score)
    top = jnp.max(scores, axis=1, keepdims=True)
    weights = jnp.exp(scores - top)
    total = jnp.sum(weights, axis=1, keepdims=True)
    summed = jnp.dot(weights.astype(jnp.bfloat16), value_ref[...], preferred_element_type=jnp.float32)
    out_ref[...] = (summed / total).astype(out_ref.dtype)


def kernel_attention(queries, query_pos, keys, values, length, cache_limit):
    head_count, query_count, head_dim = queries.shape
    key_count = keys.shape[1]
    tile = next(t for t in (384, 256, 128, 64, 32, 16, 8) if query_count % t == 0)
    grid_spec = pltpu.PrefetchScalarGridSpec(
        num_scalar_prefetch=1,
        grid=(head_count, query_count // tile),
        in_specs=[
            pl.BlockSpec((None, tile, head_dim), lambda h, i, n: (h, i, 0)),
            pl.BlockSpec((tile, 1), lambda h, i, n: (i, 0)),
            pl.BlockSpec((None, key_count, head_dim), lambda h, i, n: (h, 0, 0)),
            pl.BlockSpec((None, key_count, head_dim), lambda h, i, n: (h, 0, 0)),
        ],
        out_specs=pl.BlockSpec((None, tile, head_dim), lambda h, i, n: (h, i, 0)),
    )
    return pl.pallas_call(
        functools.partial(attention_kernel, cache_limit=cache_limit),
        grid_spec=grid_spec,
        out_shape=jax.ShapeDtypeStruct(queries.shape, jnp.bfloat16),
        compiler_params=pltpu.CompilerParams(dimension_semantics=("arbitrary", "arbitrary")),
    )(jnp.reshape(length, (1,)).astype(jnp.int32), queries, query_pos.reshape(-1, 1), keys, values)


def head_attention(queries, query_pos, keys, values, length, cache_limit):
    factor = queries.shape[-1] ** (-0.5)
    scores = jnp.einsum("hqk,hsk->hqs", queries, keys, preferred_element_type=jnp.float32) * factor
    slot_ids = jnp.arange(keys.shape[1], dtype=jnp.int32)[None, :]
    visible = jnp.where(
        slot_ids < cache_limit, slot_ids < length, slot_ids - cache_limit <= query_pos[:, None]
    )
    scores = jnp.where(visible[None], scores, masked_score)
    top = jnp.max(scores, axis=-1, keepdims=True)
    weights = jnp.exp(scores - top)
    total = jnp.sum(weights, axis=-1, keepdims=True)
    summed = jnp.einsum(
        "hqs,hsk->hqk", weights.astype(jnp.bfloat16), values, preferred_element_type=jnp.float32
    )
    return (summed / total).astype(jnp.bfloat16)


def body(
    tokens,
    cache,
    cache_len,
    attn_routes,
    mlp_routes,
    norm_attn,
    attn_router,
    w_query,
    w_keyval,
    w_out,
    norm_mlp,
    mlp_router,
    w_gate,
    w_up,
    w_down,
):
    device_count = lax.axis_size("exp")
    position = lax.axis_index("exp")
    own_rows = tokens[0]
    rows_block = own_rows.shape[0]
    model_width = own_rows.shape[1]
    length = cache_len[0]
    slot_count = MOST
    heads_here = w_query.shape[0]
    head_dim = w_query.shape[2]
    columns = w_keyval.shape[1]
    experts_attn = attn_router.shape[1]
    kv_heads = columns * device_count // (2 * head_dim)
    fast_attn = (
        device_count == experts_attn and heads_here == kv_heads and columns % (2 * head_dim) == 0
    )
    if not fast_attn:
        return base_body(
            tokens, cache, cache_len, attn_routes, mlp_routes, norm_attn, attn_router, w_query,
            w_keyval, w_out, norm_mlp, mlp_router, w_gate, w_up, w_down,
        )
    normed = rms_norm(own_rows, norm_attn)
    route_rows = jnp.zeros((16, 2 * rows_block), jnp.bfloat16)
    route_rows = route_rows.at[0].set(attn_routes[0].reshape(-1).astype(jnp.bfloat16))
    group_normed = lax.all_gather(normed, "exp", axis=0, tiled=True)
    gathered_routes = lax.all_gather(route_rows, "exp", axis=0, tiled=False)
    group_routes = gathered_routes[:, 0].astype(jnp.int32).reshape(-1, 2)
    row_total = group_normed.shape[0]
    block_count = row_total // rows_block
    new_pos = length + jnp.arange(row_total, dtype=jnp.int32)
    fresh_kv = jnp.dot(group_normed, w_keyval, preferred_element_type=jnp.float32)
    split_new = fresh_kv.reshape(row_total, columns // (2 * head_dim), 2, head_dim)
    rotated = rotate(split_new[:, :, 0], new_pos[:, None])
    fresh_kv = (
        jnp.stack([rotated, split_new[:, :, 1]], axis=2)
        .astype(jnp.bfloat16)
        .reshape(row_total, columns)
    )
    cache_limit = cache.shape[1]
    padded = jnp.concatenate([cache[0], jnp.zeros((row_total, columns), jnp.bfloat16)], axis=0)
    placed = lax.dynamic_update_slice(jnp.zeros_like(padded), fresh_kv, (length, jnp.int32(0)))
    slot_ids = jnp.arange(cache_limit + row_total, dtype=jnp.int32)
    cache_next = jnp.where((slot_ids < length)[:, None], padded, placed)

    all_labels = jnp.arange(experts_attn, dtype=jnp.int32)
    blocks_routes = group_routes.reshape(block_count, rows_block, -1)
    slot_tokens = jax.vmap(lambda r: local_slots(r, all_labels, slot_count))(blocks_routes)
    slot_tokens = slot_tokens + (jnp.arange(block_count, dtype=jnp.int32) * rows_block)[:, None, None]
    expert_tokens = jnp.swapaxes(slot_tokens, 0, 1).reshape(experts_attn, -1)
    my_tokens = expert_tokens[position]
    picked_rows = select_rows(my_tokens, group_normed).astype(jnp.bfloat16)
    queries = jnp.einsum("sd,hdk->hsk", picked_rows, w_query, preferred_element_type=jnp.float32)
    queries = rotate_whole(queries, (length + my_tokens)[None, :]).astype(jnp.bfloat16)
    heads_local = columns // (2 * head_dim)
    query_slots = queries.shape[1]
    send_q = queries.reshape(device_count, heads_local, query_slots, head_dim)
    recv_q = lax.all_to_all(send_q, "exp", 0, 0, tiled=True)
    recv_q = jnp.swapaxes(recv_q, 0, 1).reshape(heads_local, device_count * query_slots, head_dim)
    query_pos = expert_tokens.reshape(-1)
    split_old = cache[0].reshape(cache_limit, heads_local, 2, head_dim)
    split_fresh = fresh_kv.reshape(row_total, heads_local, 2, head_dim)
    keys = jnp.swapaxes(jnp.concatenate([split_old[:, :, 0], split_fresh[:, :, 0]], axis=0), 0, 1)
    values = jnp.swapaxes(jnp.concatenate([split_old[:, :, 1], split_fresh[:, :, 1]], axis=0), 0, 1)
    out_by_head = w_out.reshape(device_count, heads_local, head_dim, model_width)
    projected = jnp.zeros((query_slots, model_width), jnp.float32)
    for head in range(heads_local):
        head_out = kernel_attention(
            recv_q[head : head + 1], query_pos, keys[head : head + 1], values[head : head + 1],
            length, cache_limit,
        )
        recv_o = lax.all_to_all(
            head_out.reshape(device_count, query_slots, head_dim), "exp", 0, 0, tiled=True
        )
        projected = projected + jnp.einsum(
            "dsk,dkm->sm", recv_o, out_by_head[:, head], preferred_element_type=jnp.float32
        )
    send_p = projected.astype(jnp.bfloat16).reshape(block_count, slot_count, model_width)
    recv_p = lax.all_to_all(send_p, "exp", 0, 0, tiled=True)
    own_attn_routes = attn_routes[0]
    attn_gates = pick_gates(normed, attn_router, own_attn_routes)
    attn_own = combine(
        recv_p, own_attn_routes, attn_gates, route_slots(own_attn_routes, experts_attn), 1
    )
    middle = (own_rows.astype(jnp.float32) + attn_own).astype(jnp.bfloat16)
    normed_mlp = rms_norm(middle, norm_mlp)
    experts_mlp = mlp_router.shape[1]
    split_count = device_count // experts_mlp
    own_mlp_routes = mlp_routes[0]
    mlp_gates = pick_gates(normed_mlp, mlp_router, own_mlp_routes)
    mlp_tokens = local_slots(own_mlp_routes, jnp.arange(experts_mlp, dtype=jnp.int32), slot_count)
    dest_tokens = jnp.repeat(mlp_tokens, split_count, axis=0)
    send_m = (
        select_rows(dest_tokens.reshape(-1), normed_mlp)
        .astype(jnp.bfloat16)
        .reshape(device_count, slot_count, model_width)
    )
    inputs = lax.all_to_all(send_m, "exp", 0, 0, tiled=True).reshape(-1, model_width)
    slice_out = expert_mlp(inputs, w_gate, w_up, w_down)
    recv_m = lax.all_to_all(
        slice_out.reshape(device_count, slot_count, model_width), "exp", 0, 0, tiled=True
    )
    mlp_own = combine(
        recv_m, own_mlp_routes, mlp_gates, route_slots(own_mlp_routes, experts_mlp), split_count
    )
    layer_out = (middle.astype(jnp.float32) + mlp_own).astype(jnp.bfloat16)
    return (layer_out[None], cache_next[None])


def base_body(
    tokens,
    cache,
    cache_len,
    attn_routes,
    mlp_routes,
    norm_attn,
    attn_router,
    w_query,
    w_keyval,
    w_out,
    norm_mlp,
    mlp_router,
    w_gate,
    w_up,
    w_down,
):
    device_count = lax.axis_size("exp")
    position = lax.axis_index("exp")
    own_rows = tokens[0]
    rows_block = own_rows.shape[0]
    model_width = own_rows.shape[1]
    length = cache_len[0]
    slot_count = MOST
    normed = rms_norm(own_rows, norm_attn)
    group_normed, group_routes = (
        lax.all_gather(normed, "exp", axis=0, tiled=True),
        lax.all_gather(attn_routes[0], "exp", axis=0, tiled=True),
    )
    row_total = group_normed.shape[0]
    block_count = row_total // rows_block
    heads_here = w_query.shape[0]
    head_dim = w_query.shape[2]
    columns = w_keyval.shape[1]
    experts_attn = attn_router.shape[1]
    my_attn = jnp.reshape(position % experts_attn, (1,))
    new_pos = length + jnp.arange(row_total, dtype=jnp.int32)
    fresh_kv = jnp.dot(group_normed, w_keyval, preferred_element_type=jnp.float32)
    if columns < 2 * head_dim:
        is_key = position % 2 == 0
        fresh_kv = jnp.where(is_key, rotate(fresh_kv, new_pos), fresh_kv).astype(jnp.bfloat16)
    else:
        split_new = fresh_kv.reshape(row_total, columns // (2 * head_dim), 2, head_dim)
        rotated = rotate(split_new[:, :, 0], new_pos[:, None])
        fresh_kv = (
            jnp.stack([rotated, split_new[:, :, 1]], axis=2)
            .astype(jnp.bfloat16)
            .reshape(row_total, columns)
        )
    cache_limit = cache.shape[1]
    padded = jnp.concatenate([cache[0], jnp.zeros((row_total, columns), jnp.bfloat16)], axis=0)
    placed = lax.dynamic_update_slice(jnp.zeros_like(padded), fresh_kv, (length, jnp.int32(0)))
    slot_ids = jnp.arange(cache_limit + row_total, dtype=jnp.int32)
    cache_next = jnp.where((slot_ids < length)[:, None], padded, placed)
    group_cache = cache[0]
    group_fresh = fresh_kv
    for bit in range(experts_attn.bit_length() - 1):
        other_cache, other_fresh = from_partner((group_cache, group_fresh), "exp", bit)
        lower = position // (1 << bit) % 2 == 0
        group_cache = jnp.where(
            lower,
            jnp.concatenate([group_cache, other_cache], axis=1),
            jnp.concatenate([other_cache, group_cache], axis=1),
        )
        group_fresh = jnp.where(
            lower,
            jnp.concatenate([group_fresh, other_fresh], axis=1),
            jnp.concatenate([other_fresh, group_fresh], axis=1),
        )
    split_old = group_cache.reshape(cache_limit, heads_here, 2, head_dim)
    split_fresh = group_fresh.reshape(row_total, heads_here, 2, head_dim)
    attn_gates = pick_gates(group_normed, attn_router, group_routes)
    attn_tokens, attn_shares = slot_tables(
        group_routes, attn_gates, my_attn, rows_block, slot_count
    )
    token_flat = attn_tokens[:, 0, :].reshape(-1)
    share_flat = attn_shares[:, 0, :].reshape(-1)
    picked_rows = group_normed[token_flat]
    queries = jnp.einsum("sd,hdk->hsk", picked_rows, w_query, preferred_element_type=jnp.float32)
    queries = rotate(queries, (length + token_flat)[None, :]).astype(jnp.bfloat16)
    attend_heads = jax.vmap(attend, in_axes=(0, None, 1, 1, 1, 1, None))
    head_outs = attend_heads(
        queries,
        token_flat,
        split_old[:, :, 0],
        split_old[:, :, 1],
        split_fresh[:, :, 0],
        split_fresh[:, :, 1],
        length,
    )
    projected = jnp.einsum("hsk,hkd->sd", head_outs, w_out, preferred_element_type=jnp.float32)
    projected = (projected * share_flat[:, None]).reshape(block_count, slot_count, model_width)
    attn_ids = attn_tokens[:, 0, :]
    attn_own = lax.psum_scatter(
        spread_rows(projected, attn_ids, rows_block * lax.axis_size("exp")).astype(jnp.bfloat16),
        "exp",
        scatter_dimension=0,
        tiled=True,
    ).astype(jnp.float32)
    middle = lax.optimization_barrier(
        (own_rows.astype(jnp.float32) + attn_own).astype(jnp.bfloat16)
    )
    normed_mlp = rms_norm(middle, norm_mlp)
    experts_mlp = mlp_router.shape[1]
    split_count = device_count // experts_mlp
    my_expert = jnp.reshape(position // split_count, (1,))
    all_normed, all_routes = (
        lax.all_gather(normed_mlp, "exp", axis=0, tiled=True),
        lax.all_gather(mlp_routes[0], "exp", axis=0, tiled=True),
    )
    all_gates = pick_gates(all_normed, mlp_router, all_routes)
    mlp_tokens, mlp_shares = slot_tables(all_routes, all_gates, my_expert, rows_block, slot_count)
    inputs = all_normed[mlp_tokens.reshape(-1)]
    gate_part = jnp.dot(inputs, w_gate[0], preferred_element_type=jnp.float32)
    up_part = jnp.dot(inputs, w_up[0], preferred_element_type=jnp.float32)
    hidden = (jax.nn.silu(gate_part) * up_part).astype(jnp.bfloat16)
    slice_out = lax.optimization_barrier(
        jnp.dot(hidden, w_down[0], preferred_element_type=jnp.float32).astype(jnp.bfloat16)
    )
    weighted = (slice_out.astype(jnp.float32) * mlp_shares.reshape(-1)[:, None]).reshape(
        block_count, slot_count, model_width
    )
    mlp_ids = mlp_tokens[:, 0, :]
    mlp_own = lax.psum_scatter(
        spread_rows(weighted, mlp_ids, rows_block * lax.axis_size("exp")).astype(jnp.bfloat16),
        "exp",
        scatter_dimension=0,
        tiled=True,
    ).astype(jnp.float32)
    layer_out = (middle.astype(jnp.float32) + mlp_own).astype(jnp.bfloat16)
    return (layer_out[None], cache_next[None])


def solution(mesh):
    placed = (
        P("req", "exp", None),
        P("req", None, "exp"),
        P("req"),
        P("req", "exp", None),
        P("req", "exp", None),
        P(),
        P(),
        P("exp", None, None),
        P(None, "exp"),
        P("exp", None, None),
        P(),
        P(),
        P("exp", None, None),
        P("exp", None, None),
        P("exp", None, None),
    )
    return jax.shard_map(
        body,
        mesh=mesh,
        in_specs=placed,
        out_specs=(P("req", "exp", None), P("req", None, "exp")),
        check_vma=False,
    )
```
